32 devices in a mesh: dp: 8 (over y, x, core), mp: 4 (over z).
Axes of the slice: x: 2, y: 2, z: 4, core: 2. Of those that a mesh axis runs over, the one named last changes fastest.
Arguments:
- inputs: bfloat16 [120, 128, 768], P('dp'), may hold values from -6 to 6
- timesteps: int32 [120], P('dp'), may hold values from 0 to 999
- segments: int32 [120, 128], P('dp'), may hold values from 0 to 5, never falling along the last dimension, each value on 1 to 48 neighbouring positions
- valid_mask: int32 [120, 128], P('dp'), may hold values from 0 to 1, as said below
- step_table: bfloat16 [1000, 768], replicated, may hold values from -6 to 6
- ln1_gain: float32 [768], replicated, may hold values from 0.5 to 1.5
- ln1_shift: float32 [768], replicated, may hold values from -1 to 1
- w_query: bfloat16 [768, 768], P(None, 'mp'), may hold values from -0.21875 to 0.21875
- b_query: float32 [768], P('mp'), may hold values from -1 to 1
- w_key: bfloat16 [768, 768], P(None, 'mp'), may hold values from -0.21875 to 0.21875
- w_value: bfloat16 [768, 768], P(None, 'mp'), may hold values from -0.21875 to 0.21875
- b_value: float32 [768], P('mp'), may hold values from -1 to 1
- w_out: bfloat16 [768, 768], P('mp'), may hold values from -0.875 to 0.875
- b_out: float32 [768], replicated, may hold values from -1 to 1
- ln2_gain: float32 [768], replicated, may hold values from 0.5 to 1.5
- ln2_shift: float32 [768], replicated, may hold values from -1 to 1
- w_up: bfloat16 [768, 3072], P(None, 'mp'), may hold values from -0.21875 to 0.21875
- b_up: float32 [3072], P('mp'), may hold values from -1 to 1
- w_down: bfloat16 [3072, 768], P('mp'), may hold values from -0.109375 to 0.109375
- b_down: float32 [768], replicated, may hold values from -1 to 1
- cotangent: bfloat16 [120, 128, 768], P('dp'), may hold values from -6 to 6
Outputs:
- output: bfloat16 [120, 128, 768], P('dp')
- input_grad: bfloat16 [120, 128, 768], P('dp')
- grad_ln1_gain: float32 [768], replicated
- grad_ln1_shift: float32 [768], replicated
- grad_w_query: float32 [768, 768], P(None, 'mp')
- grad_b_query: float32 [768], P('mp')
- grad_w_key: float32 [768, 768], P(None, 'mp')
- grad_w_value: float32 [768, 768], P(None, 'mp')
- grad_b_value: float32 [768], P('mp')
- grad_w_out: float32 [768, 768], P('mp')
- grad_b_out: float32 [768], replicated
- grad_ln2_gain: float32 [768], replicated
- grad_ln2_shift: float32 [768], replicated
- grad_w_up: float32 [768, 3072], P(None, 'mp')
- grad_b_up: float32 [3072], P('mp')
- grad_w_down: float32 [3072, 768], P('mp')
- grad_b_down: float32 [768], replicated
- table_grad: float32 [1000, 768], P(None, 'mp')
The draws below stay inside these ranges and needn't reach their ends.
Inputs may be any that keep to these rules, and one draw needn't show every extreme that they name: `valid_mask`: in each row the zeros, if any, are its last positions.
All inputs are finite; a program needn't handle non-finite values.
Results may differ from the reference program's by a relative error of at most 0.014.
Values sent between devices are 32-bit elements; how exact they have to be, the bound alone decides.
No kernel may reach another device: no remote copies, remote signals or barrier semaphores. Data moves between devices by JAX's collectives and lax.ppermute only.
A program may use at most 192 MiB of HBM per device.

```python
import math
import jax
import jax.numpy as jnp
import numpy as np
from jax import lax

D = 768
HEADS = 12
HD = 64
FF = 3072
TSTEPS = 1000
SEQ = 128
SEGS = 6
SEGMOST = 48
ROWS_DEV = 15
ROWS = 120
N_DP = 8


def draw_valid_mask(key, part):
    padding = jax.random.randint(key, (ROWS, 1), 0, SEQ // 8, dtype=jnp.int32)
    places = jnp.arange(SEQ, dtype=jnp.int32)[None, :]
    return (places < SEQ - padding).astype(jnp.int32)


def plant(entries, key, smallest, high):
    index_at = [jax.random.randint(jax.random.fold_in(key, axis), (), 0, length) for axis, length in enumerate(entries.shape)]
    longest = entries.shape.index(max(entries.shape))
    beside = index_at[:longest] + [(index_at[longest] + 1) % entries.shape[longest]] + index_at[longest + 1:]
    return entries.at[tuple(index_at)].set(smallest).at[tuple(beside)].set(high)


def block_scale(own_key, dims, cuts, least, top_value):
    level, own = 1.0, jax.random.fold_in(own_key, 6)
    for position, shards_of in cuts:
        heights = jnp.exp(jax.random.uniform(jax.random.fold_in(own, position), (shards_of,), jnp.float32, least / len(cuts), top_value / len(cuts)))
        level = level * jnp.repeat(heights, dims[position] // shards_of).reshape([-1 if axis == position else 1 for axis in range(len(dims))])
    return level


def length_profile(count, total, reach, lean):
    portions = [(1 << 20) // math.isqrt(grade ** lean) + 1 for grade in range(2, count + 1)]
    spare, given = total - reach - (count - 1), [1] * (count - 1)
    while spare > 0:
        movable = [i for i in range(count - 1) if given[i] < reach]
        mass, remaining = sum([portions[i] for i in movable]), spare
        for i in movable:
            more = min(reach - given[i], max(1, remaining * portions[i] // mass), spare)
            given[i] = given[i] + more
            spare = spare - more
    return np.array([reach] + given)


def uneven(stream_key, count, total, reach, skew):
    if count == 2:
        one = jax.random.randint(stream_key, (), max(1, total - reach), min(reach, total - 1) + 1)
        return jnp.stack([one, total - one])
    tallies = jnp.asarray(length_profile(count, total, reach, skew), jnp.int32)
    twos = (count - 1) // 2
    donor, taker = tallies[1:1 + 2 * twos:2], tallies[2:2 + 2 * twos:2]
    room = jnp.minimum(donor - 1, reach - taker)
    moved = jax.random.randint(jax.random.fold_in(stream_key, 1), (twos,), 0, 1 << 20) % (room + 1)
    tallies = tallies.at[1:1 + 2 * twos:2].set(donor - moved).at[2:2 + 2 * twos:2].set(taker + moved)
    return tallies[jax.random.permutation(jax.random.fold_in(stream_key, 2), count)]


def gaussian(rng, extent, spread, limit, shards=(), held_as=jnp.bfloat16):
    loudness = block_scale(rng, extent, shards, -0.22, 0.18) if shards else 1.0
    drawn = jax.random.normal(rng, extent, jnp.float32) * spread * loudness
    return jnp.minimum(jnp.maximum(drawn, -limit), limit).astype(held_as)


def setup_inputs(seed: int = 0) -> dict:
    splits = jax.random.split(jax.random.key(seed), 22)
    inputs = gaussian(splits[0], (ROWS, SEQ, D), 1.0, 6.0, ((0, 8),))
    timesteps = plant(jax.random.randint(splits[1], (ROWS,), 0, TSTEPS), jax.random.fold_in(splits[1], 1), 0, TSTEPS - 1).astype(jnp.int32)
    segments = jax.vmap(lambda own: jnp.searchsorted(jnp.cumsum(uneven(own, SEGS, SEQ, SEGMOST, 0)), jnp.arange(SEQ), side="right"))(jax.random.split(splits[2], ROWS)).reshape((ROWS, SEQ)).astype(jnp.int32)
    valid_mask = draw_valid_mask(jax.random.fold_in(splits[21], 71), 0)
    step_table = gaussian(splits[4], (TSTEPS, D), 1.0, 6.0)
    ln1_gain = jnp.clip(1.0 + 0.1 * jax.random.normal(splits[5], (D,), jnp.float32), 0.5, 1.5)
    ln1_shift = gaussian(splits[6], (D,), 0.2, 1.0, (), jnp.float32)
    w_query = gaussian(splits[7], (D, HEADS * HD), D ** -0.5, 0.21875, ((1, 4),))
    b_query = gaussian(splits[8], (HEADS * HD,), 0.2, 1.0, ((0, 4),), jnp.float32)
    w_key = gaussian(splits[9], (D, HEADS * HD), D ** -0.5, 0.21875, ((1, 4),))
    w_value = gaussian(splits[10], (D, HEADS * HD), D ** -0.5, 0.21875, ((1, 4),))
    b_value = gaussian(splits[11], (HEADS * HD,), 0.2, 1.0, ((0, 4),), jnp.float32)
    w_out = gaussian(splits[12], (HEADS * HD, D), (HEADS * HD // 16) ** -0.5, 0.875, ((0, 4),))
    b_out = gaussian(splits[13], (D,), 0.2, 1.0, (), jnp.float32)
    ln2_gain = jnp.clip(1.0 + 0.1 * jax.random.normal(splits[14], (D,), jnp.float32), 0.5, 1.5)
    ln2_shift = gaussian(splits[15], (D,), 0.2, 1.0, (), jnp.float32)
    w_up = gaussian(splits[16], (D, FF), D ** -0.5, 0.21875, ((1, 4),))
    b_up = gaussian(splits[17], (FF,), 0.2, 1.0, ((0, 4),), jnp.float32)
    w_down = gaussian(splits[18], (FF, D), FF ** -0.5, 0.109375, ((0, 4),))
    b_down = gaussian(splits[19], (D,), 0.2, 1.0, (), jnp.float32)
    cotangent = gaussian(splits[20], (ROWS, SEQ, D), 1.0, 6.0, ((0, 8),))
    return dict(inputs=inputs, timesteps=timesteps, segments=segments, valid_mask=valid_mask, step_table=step_table, ln1_gain=ln1_gain, ln1_shift=ln1_shift, w_query=w_query, b_query=b_query, w_key=w_key, w_value=w_value, b_value=b_value, w_out=w_out, b_out=b_out, ln2_gain=ln2_gain, ln2_shift=ln2_shift, w_up=w_up, b_up=b_up, w_down=w_down, b_down=b_down, cotangent=cotangent)


EPSILON = 1e-05

@jax.custom_vjp
def low(v):
    return lax.optimization_barrier(v.astype(jnp.bfloat16)).astype(jnp.float32)

@jax.custom_vjp
def low_back(v):
    return v

def low_keep(v):
    return (low(v), None)

def low_pass(kept, grad):
    return (grad,)

def back_keep(v):
    return (v, None)

def back_low(kept, grad):
    return (low(grad),)
low.defvjp(low_keep, low_pass)
low_back.defvjp(back_keep, back_low)

def normalize(values, gain, shift):
    average = lax.optimization_barrier(jnp.mean(values, axis=-1, keepdims=True))
    centered = values - average
    variance = lax.optimization_barrier(jnp.mean(centered * centered, axis=-1, keepdims=True))
    return centered * lax.rsqrt(variance + EPSILON) * gain + shift

def matmul(left, right):
    return jnp.dot(left, right, precision=lax.Precision.HIGHEST)

def block_layer(params, inputs, table, timesteps, segments, valid_mask):
    ln1_gain, ln1_shift, w_query, b_query, w_key, w_value, b_value, w_out, b_out, ln2_gain, ln2_shift, w_up, b_up, w_down, b_down = params
    row_count, seq_len, model_width = inputs.shape
    start = (inputs + table[timesteps][:, None, :]).reshape(row_count * seq_len, model_width)
    normed = low(normalize(start, ln1_gain, ln1_shift))
    queries = low(low_back(matmul(normed, w_query) + b_query))
    key_rows = low(low_back(matmul(normed, w_key)))
    value_rows = low(low_back(matmul(normed, w_value) + b_value))
    head_shape = (row_count, seq_len, HEADS, HD)
    scaling = 1.0 / math.sqrt(HD)
    scores = jnp.einsum('rqhe,rkhe->rhqk', queries.reshape(head_shape), key_rows.reshape(head_shape), precision=lax.Precision.HIGHEST) * scaling
    scores = low_back(scores)
    places = jnp.arange(seq_len, dtype=jnp.int32)
    diagonal = places[:, None] == places[None, :]
    allowed = (segments[:, :, None] == segments[:, None, :]) & ((valid_mask[:, None, :] > 0) | diagonal[None])
    scores = jnp.where(allowed[:, None], scores, -1e+30)
    probabilities = low(jax.nn.softmax(scores, axis=-1))
    mixed = jnp.einsum('rhqk,rkhe->rqhe', probabilities, value_rows.reshape(head_shape), precision=lax.Precision.HIGHEST).reshape(row_count * seq_len, HEADS * HD)
    mixed = low(low_back(mixed))
    attended = low_back(matmul(mixed, w_out) + b_out)
    middle = start + attended
    normed2 = low(normalize(middle, ln2_gain, ln2_shift))
    upper = low_back(matmul(normed2, w_up) + b_up)
    hidden = low(jax.nn.gelu(upper, approximate=False))
    result = middle + matmul(hidden, w_down) + b_down
    return result.reshape(row_count, seq_len, model_width)

def reference(inputs, timesteps, segments, valid_mask, step_table, ln1_gain, ln1_shift, w_query, b_query, w_key, w_value, b_value, w_out, b_out, ln2_gain, ln2_shift, w_up, b_up, w_down, b_down, cotangent):
    params = tuple((item.astype(jnp.float32) for item in (ln1_gain, ln1_shift, w_query, b_query, w_key, w_value, b_value, w_out, b_out, ln2_gain, ln2_shift, w_up, b_up, w_down, b_down)))
    table = step_table.astype(jnp.float32)
    block_shape = (N_DP, ROWS_DEV, SEQ, D)
    masked_grad = cotangent.astype(jnp.float32) * valid_mask[:, :, None].astype(jnp.float32)
    pieces = (inputs.astype(jnp.float32).reshape(block_shape), timesteps.reshape(N_DP, ROWS_DEV), segments.reshape(N_DP, ROWS_DEV, SEQ), valid_mask.reshape(N_DP, ROWS_DEV, SEQ), masked_grad.reshape(block_shape))

    def scan_step(running, piece):
        block_inputs, block_steps, block_segments, block_valid, block_grad = piece

        def forward(weights, values, table_rows):
            return block_layer(weights, values, table_rows, block_steps, block_segments, block_valid)
        result, pullback = jax.vjp(forward, params, block_inputs, table)
        grad_params, grad_inputs, grad_table = pullback(block_grad)
        running = jax.tree.map(jnp.add, running, (grad_params, grad_table))
        return (running, (result.astype(jnp.bfloat16), grad_inputs.astype(jnp.bfloat16)))
    initial = jax.tree.map(jnp.zeros_like, (params, table))
    (grads, table_grad), (outputs, input_grads) = lax.scan(scan_step, initial, pieces)
    return (outputs.reshape(ROWS, SEQ, D), input_grads.reshape(ROWS, SEQ, D), grads[0], grads[1], grads[2], grads[3], grads[4], grads[5], grads[6], grads[7], grads[8], grads[9], grads[10], grads[11], grads[12], grads[13], grads[14], table_grad)
```

```python
import math

import jax
import jax.numpy as jnp
from jax import lax
from jax.sharding import PartitionSpec as P

HD = 64


EPSILON = 1e-05
CONTRACT_ROWS = (((0,), (0,)), ((), ()))
CONTRACT_COLS = (((1,), (1,)), ((), ()))


def normalize(values, gain, shift):
    average = jnp.mean(values, axis=-1, keepdims=True)
    centered = values - average
    variance = jnp.mean(centered * centered, axis=-1, keepdims=True)
    return centered * lax.rsqrt(variance + EPSILON) * gain + shift


def exact_gelu(values):
    return jax.nn.gelu(values, approximate=False)


def product(left, right):
    return jnp.dot(left, right, preferred_element_type=jnp.float32)


def over_rows(left, right):
    return lax.dot_general(left, right, CONTRACT_ROWS, preferred_element_type=jnp.float32)


def over_cols(left, right):
    return lax.dot_general(left, right, CONTRACT_COLS, preferred_element_type=jnp.float32)


def column_sum(values):
    return jnp.sum(values.astype(jnp.float32), axis=0)


def attention_scores(queries_split, keys_split, allowed):
    scaling = 1.0 / math.sqrt(HD)
    scores = (
        jnp.einsum("rqhe,rkhe->rhqk", queries_split, keys_split, preferred_element_type=jnp.float32)
        * scaling
    )
    return jnp.where(allowed[:, None], scores, -1e30)


def gather_whole(shard, sharded_dim, one):
    n_dp = lax.axis_size("dp")
    n_mp = lax.axis_size("mp")
    rows, cols = shard.shape
    piece_rows = rows // n_dp
    piece = lax.dynamic_slice_in_dim(shard, lax.axis_index("dp") * piece_rows, piece_rows, 0)
    piece = piece.astype(jnp.float32) * one
    pieces = lax.all_gather(piece, ("dp", "mp"), axis=0)
    pieces = (pieces * one).astype(shard.dtype).reshape(n_dp, n_mp, piece_rows, cols)
    if sharded_dim == 1:
        return pieces.transpose(0, 2, 1, 3).reshape(rows, n_mp * cols)
    return pieces.transpose(1, 0, 2, 3).reshape(n_mp * rows, cols)


def gather_vector(shard):
    return lax.all_gather(shard, "mp", axis=0, tiled=True)


def own_columns(values, width):
    return lax.dynamic_slice_in_dim(values, lax.axis_index("mp") * width, width, 1)


def on_device(
    inputs,
    timesteps,
    segments,
    valid_mask,
    step_table,
    ln1_gain,
    ln1_shift,
    w_query_shard,
    b_query_shard,
    w_key_shard,
    w_value_shard,
    b_value_shard,
    w_out_shard,
    b_out,
    ln2_gain,
    ln2_shift,
    w_up_shard,
    b_up_shard,
    w_down_shard,
    b_down,
    cotangent,
):
    row_count, seq_len, model_width = inputs.shape
    token_count = row_count * seq_len
    qkv_width = w_query_shard.shape[1]
    ff_width = w_up_shard.shape[1]
    one = 1.0 + 0.0 * ln1_gain[0]
    w_query = gather_whole(w_query_shard, 1, one)
    w_key = gather_whole(w_key_shard, 1, one)
    w_value = gather_whole(w_value_shard, 1, one)
    w_out = gather_whole(w_out_shard, 0, one)
    w_up = gather_whole(w_up_shard, 1, one)
    w_down = gather_whole(w_down_shard, 0, one)
    b_query = gather_vector(b_query_shard)
    b_value = gather_vector(b_value_shard)
    b_up = gather_vector(b_up_shard)
    heads = w_query.shape[1] // HD
    low_type = jnp.bfloat16
    scaling = 1.0 / math.sqrt(HD)
    head_shape = (row_count, seq_len, heads, HD)
    start = inputs.astype(jnp.float32) + step_table[timesteps].astype(jnp.float32)[:, None, :]
    start = start.reshape(token_count, model_width)
    normed, first_pull = jax.vjp(normalize, start, ln1_gain, ln1_shift)
    normed_low = normed.astype(low_type)
    queries = (product(normed_low, w_query) + b_query).astype(low_type)
    key_rows = product(normed_low, w_key).astype(low_type)
    value_rows = (product(normed_low, w_value) + b_value).astype(low_type)
    queries_split = queries.reshape(head_shape)
    keys_split = key_rows.reshape(head_shape)
    values_split = value_rows.reshape(head_shape)
    places = jnp.arange(seq_len, dtype=jnp.int32)
    diagonal = places[:, None] == places[None, :]
    allowed = (segments[:, :, None] == segments[:, None, :]) & (
        (valid_mask[:, None, :] > 0) | diagonal[None]
    )
    scores = attention_scores(queries_split, keys_split, allowed)
    row_max = jnp.max(scores, axis=-1, keepdims=True)
    powers = jnp.exp(scores - row_max)
    total = jnp.sum(powers, axis=-1, keepdims=True)
    log_total = row_max + jnp.log(total)
    probabilities = powers / total
    mixed = jnp.einsum(
        "rhqk,rkhe->rqhe",
        probabilities.astype(low_type),
        values_split,
        preferred_element_type=jnp.float32,
    )
    mixed = mixed.reshape(token_count, heads * HD).astype(low_type)
    attended = product(mixed, w_out) + b_out
    middle = start + attended
    normed2, second_pull = jax.vjp(normalize, middle, ln2_gain, ln2_shift)
    normed2_low = normed2.astype(low_type)
    upper = product(normed2_low, w_up) + b_up
    activated, gelu_pull = jax.vjp(exact_gelu, upper)
    hidden = activated.astype(low_type)
    lowered = product(hidden, w_down)
    output = (middle + lowered + b_down).astype(low_type).reshape(row_count, seq_len, model_width)
    grad_out = cotangent.reshape(token_count, model_width).astype(jnp.float32)
    grad_out = grad_out * valid_mask.reshape(token_count, 1).astype(jnp.float32)
    grad_out_low = grad_out.astype(low_type)
    grad_w_down = over_rows(own_columns(hidden, ff_width), grad_out_low)
    grad_b_down = jnp.sum(grad_out, axis=0)
    grad_hidden = over_cols(grad_out_low, w_down)
    (grad_upper,) = gelu_pull(grad_hidden)
    grad_upper_low = grad_upper.astype(low_type)
    own_grad_upper = own_columns(grad_upper_low, ff_width)
    grad_w_up = over_rows(normed2_low, own_grad_upper)
    grad_b_up = column_sum(own_grad_upper)
    grad_normed2 = over_cols(grad_upper_low, w_up)
    grad_mid_norm, grad_ln2_gain, grad_ln2_shift = second_pull(grad_normed2)
    grad_middle = grad_out + grad_mid_norm
    grad_mid_low = grad_middle.astype(low_type)
    grad_w_out = over_rows(own_columns(mixed, qkv_width), grad_mid_low)
    grad_b_out = column_sum(grad_mid_low)
    grad_mixed = over_cols(grad_mid_low, w_out).astype(low_type).reshape(head_shape)
    scores_again = attention_scores(queries_split, keys_split, allowed)
    soft_again = jnp.exp(scores_again - log_total)
    grad_soft = jnp.einsum(
        "rqhe,rkhe->rhqk", grad_mixed, values_split, preferred_element_type=jnp.float32
    )
    delta = jnp.sum(soft_again * grad_soft, axis=-1, keepdims=True)
    grad_scores = (soft_again * (grad_soft - delta)).astype(low_type)
    grad_queries = jnp.einsum(
        "rhqk,rkhe->rqhe", grad_scores, keys_split, preferred_element_type=jnp.float32
    )
    grad_queries = (grad_queries * scaling).reshape(token_count, heads * HD).astype(low_type)
    grad_keys = jnp.einsum(
        "rhqk,rqhe->rkhe", grad_scores, queries_split, preferred_element_type=jnp.float32
    )
    grad_keys = (grad_keys * scaling).reshape(token_count, heads * HD).astype(low_type)
    grad_values = jnp.einsum(
        "rhqk,rqhe->rkhe",
        soft_again.astype(low_type),
        grad_mixed,
        preferred_element_type=jnp.float32,
    )
    grad_values = grad_values.reshape(token_count, heads * HD).astype(low_type)
    own_grad_queries = own_columns(grad_queries, qkv_width)
    own_grad_values = own_columns(grad_values, qkv_width)
    grad_w_query = over_rows(normed_low, own_grad_queries)
    grad_b_query = column_sum(own_grad_queries)
    grad_w_key = over_rows(normed_low, own_columns(grad_keys, qkv_width))
    grad_w_value = over_rows(normed_low, own_grad_values)
    grad_b_value = column_sum(own_grad_values)
    grad_normed = (
        over_cols(grad_queries, w_query)
        + over_cols(grad_keys, w_key)
        + over_cols(grad_values, w_value)
    )
    grad_start_norm, grad_ln1_gain, grad_ln1_shift = first_pull(grad_normed)
    grad_start = grad_middle + grad_start_norm
    input_grad = grad_start.astype(low_type).reshape(row_count, seq_len, model_width)
    row_sums = jnp.sum(grad_start.reshape(row_count, seq_len, model_width), axis=1)
    column_count = model_width // lax.axis_size("mp")
    table_columns = own_columns(row_sums, column_count)
    step_count = step_table.shape[0]
    one_hot = (timesteps[:, None] == jnp.arange(step_count, dtype=jnp.int32)[None, :]).astype(
        jnp.float32
    )
    table_grad = lax.dot_general(
        one_hot,
        table_columns,
        CONTRACT_ROWS,
        precision=lax.Precision.HIGHEST,
        preferred_element_type=jnp.float32,
    )
    (
        grad_ln1_gain,
        grad_ln1_shift,
        grad_w_query,
        grad_b_query,
        grad_w_key,
        grad_w_value,
        grad_b_value,
        grad_w_out,
        grad_b_out,
        table_grad,
        grad_w_down,
        grad_b_down,
        grad_w_up,
        grad_b_up,
        grad_ln2_gain,
        grad_ln2_shift,
    ) = lax.psum(
        (
            grad_ln1_gain,
            grad_ln1_shift,
            grad_w_query,
            grad_b_query,
            grad_w_key,
            grad_w_value,
            grad_b_value,
            grad_w_out,
            grad_b_out,
            table_grad,
            grad_w_down,
            grad_b_down,
            grad_w_up,
            grad_b_up,
            grad_ln2_gain,
            grad_ln2_shift,
        ),
        "dp",
    )
    return (
        output,
        input_grad,
        grad_ln1_gain,
        grad_ln1_shift,
        grad_w_query,
        grad_b_query,
        grad_w_key,
        grad_w_value,
        grad_b_value,
        grad_w_out,
        grad_b_out,
        grad_ln2_gain,
        grad_ln2_shift,
        grad_w_up,
        grad_b_up,
        grad_w_down,
        grad_b_down,
        table_grad,
    )


def solution(mesh):
    in_specs = (
        P("dp", None, None),
        P("dp"),
        P("dp", None),
        P("dp", None),
        P(),
        P(),
        P(),
        P(None, "mp"),
        P("mp"),
        P(None, "mp"),
        P(None, "mp"),
        P("mp"),
        P("mp", None),
        P(),
        P(),
        P(),
        P(None, "mp"),
        P("mp"),
        P("mp", None),
        P(),
        P("dp", None, None),
    )
    out_specs = (
        P("dp", None, None),
        P("dp", None, None),
        P(),
        P(),
        P(None, "mp"),
        P("mp"),
        P(None, "mp"),
        P(None, "mp"),
        P("mp"),
        P("mp", None),
        P(),
        P(),
        P(),
        P(None, "mp"),
        P("mp"),
        P("mp", None),
        P(),
        P(None, "mp"),
    )
    return jax.shard_map(
        on_device, mesh=mesh, in_specs=in_specs, out_specs=out_specs, check_vma=False
    )
```

```python
import math

import jax
import jax.numpy as jnp
from jax import lax
from jax.sharding import PartitionSpec as P

HD = 64


EPSILON = 1e-05
CONTRACT_ROWS = (((0,), (0,)), ((), ()))
CONTRACT_COLS = (((1,), (1,)), ((), ()))


def normalize(values, gain, shift):
    average = jnp.mean(values, axis=-1, keepdims=True)
    centered = values - average
    variance = jnp.mean(centered * centered, axis=-1, keepdims=True)
    return centered * lax.rsqrt(variance + EPSILON) * gain + shift


def exact_gelu(values):
    return jax.nn.gelu(values, approximate=False)


def product(left, right):
    return jnp.dot(left, right, preferred_element_type=jnp.float32)


def over_rows(left, right):
    return lax.dot_general(left, right, CONTRACT_ROWS, preferred_element_type=jnp.float32)


def over_cols(left, right):
    return lax.dot_general(left, right, CONTRACT_COLS, preferred_element_type=jnp.float32)


def column_sum(values):
    return jnp.sum(values.astype(jnp.float32), axis=0)


def attention_scores(queries_split, keys_split, allowed):
    scaling = 1.0 / math.sqrt(HD)
    scores = (
        jnp.einsum("rqhe,rkhe->rhqk", queries_split, keys_split, preferred_element_type=jnp.float32)
        * scaling
    )
    return jnp.where(allowed[:, None], scores, -1e30)


def gather_pieces(blocks, one):
    n_dp = lax.axis_size("dp")
    d = lax.axis_index("dp")
    pieces = []
    for block in blocks:
        piece_rows = block.shape[0] // n_dp
        pieces.append(lax.dynamic_slice_in_dim(block, d * piece_rows, piece_rows, 0))
    sent = jnp.concatenate([p.astype(jnp.float32) for p in pieces], axis=0) * one
    got = lax.all_gather(sent, ("mp", "dp"), axis=0) * one
    n_mp = lax.axis_size("mp")
    got = got.reshape(n_mp, n_dp, *sent.shape)
    out, at = [], 0
    for p in pieces:
        rows = p.shape[0]
        out.append(got[:, :, at : at + rows])
        at += rows
    return out


def whole_rows(part, dtype):
    n_mp, n_dp, rows, width = part.shape
    return part.astype(dtype).reshape(n_mp * n_dp * rows, width)


def bias_block(vectors, width, n_dp):
    row = jnp.concatenate(vectors)
    row = jnp.pad(row, (0, width - row.shape[0]))
    return jnp.zeros((n_dp, width), jnp.float32).at[0].set(row)


def own_columns(values, width):
    return lax.dynamic_slice_in_dim(values, lax.axis_index("mp") * width, width, 1)


def on_device(
    inputs,
    timesteps,
    segments,
    valid_mask,
    step_table,
    ln1_gain,
    ln1_shift,
    w_query_shard,
    b_query_shard,
    w_key_shard,
    w_value_shard,
    b_value_shard,
    w_out_shard,
    b_out,
    ln2_gain,
    ln2_shift,
    w_up_shard,
    b_up_shard,
    w_down_shard,
    b_down,
    cotangent,
):
    row_count, seq_len, model_width = inputs.shape
    token_count = row_count * seq_len
    qkv_width = w_query_shard.shape[1]
    ff_width = w_up_shard.shape[1]
    one = 1.0 + 0.0 * ln1_gain[0]
    n_dp = lax.axis_size("dp")
    low_type = jnp.bfloat16
    q_part, k_part, v_part, qv_bias = gather_pieces(
        (
            w_query_shard.T,
            w_key_shard.T,
            w_value_shard.T,
            bias_block((b_query_shard, b_value_shard), model_width, n_dp),
        ),
        one,
    )
    w_query_t = whole_rows(q_part, low_type)
    w_key_t = whole_rows(k_part, low_type)
    w_value_t = whole_rows(v_part, low_type)
    b_query = qv_bias[:, 0, 0, :qkv_width].reshape(-1)
    b_value = qv_bias[:, 0, 0, qkv_width : 2 * qkv_width].reshape(-1)
    o_part, up_part, down_part, up_bias = gather_pieces(
        (
            w_out_shard,
            w_up_shard.T,
            w_down_shard,
            bias_block((b_up_shard,), model_width, n_dp),
        ),
        one,
    )
    w_out = whole_rows(o_part, low_type)
    w_up_t = whole_rows(up_part, low_type)
    w_down = whole_rows(down_part, low_type)
    b_up = up_bias[:, 0, 0, :].reshape(-1)
    heads = w_query_t.shape[0] // HD
    scaling = 1.0 / math.sqrt(HD)
    head_shape = (row_count, seq_len, heads, HD)
    start = inputs.astype(jnp.float32) + step_table[timesteps].astype(jnp.float32)[:, None, :]
    start = start.reshape(token_count, model_width)
    normed, first_pull = jax.vjp(normalize, start, ln1_gain, ln1_shift)
    normed_low = normed.astype(low_type)
    queries = (over_cols(normed_low, w_query_t) + b_query).astype(low_type)
    key_rows = over_cols(normed_low, w_key_t).astype(low_type)
    value_rows = (over_cols(normed_low, w_value_t) + b_value).astype(low_type)
    queries_split = queries.reshape(head_shape)
    keys_split = key_rows.reshape(head_shape)
    values_split = value_rows.reshape(head_shape)
    places = jnp.arange(seq_len, dtype=jnp.int32)
    diagonal = places[:, None] == places[None, :]
    allowed = (segments[:, :, None] == segments[:, None, :]) & (
        (valid_mask[:, None, :] > 0) | diagonal[None]
    )
    scores = attention_scores(queries_split, keys_split, allowed)
    row_max = jnp.max(scores, axis=-1, keepdims=True)
    powers = jnp.exp(scores - row_max)
    total = jnp.sum(powers, axis=-1, keepdims=True)
    log_total = row_max + jnp.log(total)
    probabilities = powers / total
    mixed = jnp.einsum(
        "rhqk,rkhe->rqhe",
        probabilities.astype(low_type),
        values_split,
        preferred_element_type=jnp.float32,
    )
    mixed = mixed.reshape(token_count, heads * HD).astype(low_type)
    attended = product(mixed, w_out) + b_out
    middle = start + attended
    normed2, second_pull = jax.vjp(normalize, middle, ln2_gain, ln2_shift)
    normed2_low = normed2.astype(low_type)
    upper = over_cols(normed2_low, w_up_t) + b_up
    activated, gelu_pull = jax.vjp(exact_gelu, upper)
    hidden = activated.astype(low_type)
    lowered = product(hidden, w_down)
    output = (middle + lowered + b_down).astype(low_type).reshape(row_count, seq_len, model_width)
    grad_out = cotangent.reshape(token_count, model_width).astype(jnp.float32)
    grad_out = grad_out * valid_mask.reshape(token_count, 1).astype(jnp.float32)
    grad_out_low = grad_out.astype(low_type)
    grad_w_down = over_rows(own_columns(hidden, ff_width), grad_out_low)
    grad_b_down = jnp.sum(grad_out, axis=0)
    grad_hidden = over_cols(grad_out_low, w_down)
    (grad_upper,) = gelu_pull(grad_hidden)
    grad_upper_low = grad_upper.astype(low_type)
    own_grad_upper = own_columns(grad_upper_low, ff_width)
    grad_w_up = over_rows(normed2_low, own_grad_upper)
    grad_b_up = column_sum(own_grad_upper)
    grad_normed2 = product(grad_upper_low, w_up_t)
    grad_mid_norm, grad_ln2_gain, grad_ln2_shift = second_pull(grad_normed2)
    grad_middle = grad_out + grad_mid_norm
    grad_mid_low = grad_middle.astype(low_type)
    grad_w_out = over_rows(own_columns(mixed, qkv_width), grad_mid_low)
    grad_b_out = column_sum(grad_mid_low)
    grad_mixed = over_cols(grad_mid_low, w_out).astype(low_type).reshape(head_shape)
    scores_again = attention_scores(queries_split, keys_split, allowed)
    soft_again = jnp.exp(scores_again - log_total)
    grad_soft = jnp.einsum(
        "rqhe,rkhe->rhqk", grad_mixed, values_split, preferred_element_type=jnp.float32
    )
    delta = jnp.sum(soft_again * grad_soft, axis=-1, keepdims=True)
    grad_scores = (soft_again * (grad_soft - delta)).astype(low_type)
    grad_queries = jnp.einsum(
        "rhqk,rkhe->rqhe", grad_scores, keys_split, preferred_element_type=jnp.float32
    )
    grad_queries = (grad_queries * scaling).reshape(token_count, heads * HD).astype(low_type)
    grad_keys = jnp.einsum(
        "rhqk,rqhe->rkhe", grad_scores, queries_split, preferred_element_type=jnp.float32
    )
    grad_keys = (grad_keys * scaling).reshape(token_count, heads * HD).astype(low_type)
    grad_values = jnp.einsum(
        "rhqk,rqhe->rkhe",
        soft_again.astype(low_type),
        grad_mixed,
        preferred_element_type=jnp.float32,
    )
    grad_values = grad_values.reshape(token_count, heads * HD).astype(low_type)
    own_grad_queries = own_columns(grad_queries, qkv_width)
    own_grad_values = own_columns(grad_values, qkv_width)
    grad_w_query = over_rows(normed_low, own_grad_queries)
    grad_b_query = column_sum(own_grad_queries)
    grad_w_key = over_rows(normed_low, own_columns(grad_keys, qkv_width))
    grad_w_value = over_rows(normed_low, own_grad_values)
    grad_b_value = column_sum(own_grad_values)
    grad_normed = (
        product(grad_queries, w_query_t)
        + product(grad_keys, w_key_t)
        + product(grad_values, w_value_t)
    )
    grad_start_norm, grad_ln1_gain, grad_ln1_shift = first_pull(grad_normed)
    grad_start = grad_middle + grad_start_norm
    input_grad = grad_start.astype(low_type).reshape(row_count, seq_len, model_width)
    row_sums = jnp.sum(grad_start.reshape(row_count, seq_len, model_width), axis=1)
    column_count = model_width // lax.axis_size("mp")
    table_columns = own_columns(row_sums, column_count)
    step_count = step_table.shape[0]
    one_hot = (timesteps[:, None] == jnp.arange(step_count, dtype=jnp.int32)[None, :]).astype(
        jnp.float32
    )
    table_grad = lax.dot_general(
        one_hot,
        table_columns,
        CONTRACT_ROWS,
        precision=lax.Precision.HIGHEST,
        preferred_element_type=jnp.float32,
    )
    small = (
        grad_ln1_gain,
        grad_ln1_shift,
        grad_b_query,
        grad_b_value,
        grad_b_out,
        grad_b_down,
        grad_b_up,
        grad_ln2_gain,
        grad_ln2_shift,
    )
    small_rows = jnp.concatenate(small).reshape(-1, column_count)
    packed = jnp.concatenate([table_grad, small_rows], axis=0)
    (
        grad_w_query,
        grad_w_key,
        grad_w_value,
        grad_w_out,
        packed,
        grad_w_down,
        grad_w_up,
    ) = lax.psum(
        (
            grad_w_query,
            grad_w_key,
            grad_w_value,
            grad_w_out,
            packed,
            grad_w_down,
            grad_w_up,
        ),
        "dp",
    )
    table_grad = packed[:step_count]
    flat_small = packed[step_count:].reshape(-1)
    unpacked, at = [], 0
    for item in small:
        unpacked.append(flat_small[at : at + item.shape[0]])
        at += item.shape[0]
    (
        grad_ln1_gain,
        grad_ln1_shift,
        grad_b_query,
        grad_b_value,
        grad_b_out,
        grad_b_down,
        grad_b_up,
        grad_ln2_gain,
        grad_ln2_shift,
    ) = unpacked
    return (
        output,
        input_grad,
        grad_ln1_gain,
        grad_ln1_shift,
        grad_w_query,
        grad_b_query,
        grad_w_key,
        grad_w_value,
        grad_b_value,
        grad_w_out,
        grad_b_out,
        grad_ln2_gain,
        grad_ln2_shift,
        grad_w_up,
        grad_b_up,
        grad_w_down,
        grad_b_down,
        table_grad,
    )


def solution(mesh):
    in_specs = (
        P("dp", None, None),
        P("dp"),
        P("dp", None),
        P("dp", None),
        P(),
        P(),
        P(),
        P(None, "mp"),
        P("mp"),
        P(None, "mp"),
        P(None, "mp"),
        P("mp"),
        P("mp", None),
        P(),
        P(),
        P(),
        P(None, "mp"),
        P("mp"),
        P("mp", None),
        P(),
        P("dp", None, None),
    )
    out_specs = (
        P("dp", None, None),
        P("dp", None, None),
        P(),
        P(),
        P(None, "mp"),
        P("mp"),
        P(None, "mp"),
        P(None, "mp"),
        P("mp"),
        P("mp", None),
        P(),
        P(),
        P(),
        P(None, "mp"),
        P("mp"),
        P("mp", None),
        P(),
        P(None, "mp"),
    )
    return jax.shard_map(
        on_device, mesh=mesh, in_specs=in_specs, out_specs=out_specs, check_vma=False
    )
```

```python
import math

import jax
import jax.numpy as jnp
from jax import lax
from jax.sharding import PartitionSpec as P

HD = 64


EPSILON = 1e-05
CONTRACT_ROWS = (((0,), (0,)), ((), ()))
CONTRACT_COLS = (((1,), (1,)), ((), ()))


def normalize(values, gain, shift):
    average = jnp.mean(values, axis=-1, keepdims=True)
    centered = values - average
    variance = jnp.mean(centered * centered, axis=-1, keepdims=True)
    return centered * lax.rsqrt(variance + EPSILON) * gain + shift


def exact_gelu(values):
    return jax.nn.gelu(values, approximate=False)


def product(left, right):
    return jnp.dot(left, right, preferred_element_type=jnp.float32)


def over_rows(left, right):
    return lax.dot_general(left, right, CONTRACT_ROWS, preferred_element_type=jnp.float32)


def over_cols(left, right):
    return lax.dot_general(left, right, CONTRACT_COLS, preferred_element_type=jnp.float32)


def column_sum(values):
    return jnp.sum(values.astype(jnp.float32), axis=0)


def attention_scores(queries_split, keys_split, allowed):
    scaling = 1.0 / math.sqrt(HD)
    scores = (
        jnp.einsum("rqhe,rkhe->rhqk", queries_split, keys_split, preferred_element_type=jnp.float32)
        * scaling
    )
    return jnp.where(allowed[:, None], scores, -1e30)


def gather_pieces(blocks, one):
    n_dp = lax.axis_size("dp")
    d = lax.axis_index("dp")
    pieces = []
    for block in blocks:
        piece_rows = block.shape[0] // n_dp
        pieces.append(lax.dynamic_slice_in_dim(block, d * piece_rows, piece_rows, 0))
    sent = jnp.concatenate([p.astype(jnp.float32) for p in pieces], axis=0) * one
    got = lax.all_gather(sent, ("mp", "dp"), axis=0) * one
    n_mp = lax.axis_size("mp")
    got = got.reshape(n_mp, n_dp, *sent.shape)
    out, at = [], 0
    for p in pieces:
        rows = p.shape[0]
        out.append(got[:, :, at : at + rows])
        at += rows
    return out


def whole_rows(part, dtype):
    n_mp, n_dp, rows, width = part.shape
    return part.astype(dtype).reshape(n_mp * n_dp * rows, width)


def bias_block(vectors, width, n_dp):
    row = jnp.concatenate(vectors)
    row = jnp.pad(row, (0, width - row.shape[0]))
    return jnp.zeros((n_dp, width), jnp.float32).at[0].set(row)


def own_columns(values, width):
    return lax.dynamic_slice_in_dim(values, lax.axis_index("mp") * width, width, 1)


def on_device(
    inputs,
    timesteps,
    segments,
    valid_mask,
    step_table,
    ln1_gain,
    ln1_shift,
    w_query_shard,
    b_query_shard,
    w_key_shard,
    w_value_shard,
    b_value_shard,
    w_out_shard,
    b_out,
    ln2_gain,
    ln2_shift,
    w_up_shard,
    b_up_shard,
    w_down_shard,
    b_down,
    cotangent,
):
    row_count, seq_len, model_width = inputs.shape
    token_count = row_count * seq_len
    qkv_width = w_query_shard.shape[1]
    ff_width = w_up_shard.shape[1]
    one = 1.0 + 0.0 * ln1_gain[0]
    n_dp = lax.axis_size("dp")
    low_type = jnp.bfloat16
    q_part, k_part, v_part, qv_bias = gather_pieces(
        (
            w_query_shard.T,
            w_key_shard.T,
            w_value_shard.T,
            bias_block((b_query_shard, b_value_shard), model_width, n_dp),
        ),
        one,
    )
    w_query_t = whole_rows(q_part, low_type)
    w_key_t = whole_rows(k_part, low_type)
    w_value_t = whole_rows(v_part, low_type)
    b_query = qv_bias[:, 0, 0, :qkv_width].reshape(-1)
    b_value = qv_bias[:, 0, 0, qkv_width : 2 * qkv_width].reshape(-1)
    o_part, up_part, down_part, up_bias = gather_pieces(
        (
            w_out_shard,
            w_up_shard.T,
            w_down_shard,
            bias_block((b_up_shard,), model_width, n_dp),
        ),
        one,
    )
    w_out = whole_rows(o_part, low_type)
    w_up_t = whole_rows(up_part, low_type)
    w_down = whole_rows(down_part, low_type)
    b_up = up_bias[:, 0, 0, :].reshape(-1)
    heads = w_query_t.shape[0] // HD
    scaling = 1.0 / math.sqrt(HD)
    head_shape = (row_count, seq_len, heads, HD)
    start = inputs.astype(jnp.float32) + step_table[timesteps].astype(jnp.float32)[:, None, :]
    start = start.reshape(token_count, model_width)
    normed, first_pull = jax.vjp(normalize, start, ln1_gain, ln1_shift)
    normed_low = normed.astype(low_type)
    queries = (over_cols(normed_low, w_query_t) + b_query).astype(low_type)
    key_rows = over_cols(normed_low, w_key_t).astype(low_type)
    value_rows = (over_cols(normed_low, w_value_t) + b_value).astype(low_type)
    queries_split = queries.reshape(head_shape)
    keys_split = key_rows.reshape(head_shape)
    values_split = value_rows.reshape(head_shape)
    places = jnp.arange(seq_len, dtype=jnp.int32)
    diagonal = places[:, None] == places[None, :]
    allowed = (segments[:, :, None] == segments[:, None, :]) & (
        (valid_mask[:, None, :] > 0) | diagonal[None]
    )
    scores = attention_scores(queries_split, keys_split, allowed)
    row_max = jnp.max(scores, axis=-1, keepdims=True)
    powers = jnp.exp(scores - row_max)
    total = jnp.sum(powers, axis=-1, keepdims=True)
    log_total = row_max + jnp.log(total)
    probabilities = powers / total
    mixed = jnp.einsum(
        "rhqk,rkhe->rqhe",
        probabilities.astype(low_type),
        values_split,
        preferred_element_type=jnp.float32,
    )
    mixed = mixed.reshape(token_count, heads * HD).astype(low_type)
    attended = product(mixed, w_out) + b_out
    middle = start + attended
    normed2, second_pull = jax.vjp(normalize, middle, ln2_gain, ln2_shift)
    normed2_low = normed2.astype(low_type)
    upper = over_cols(normed2_low, w_up_t) + b_up
    activated, gelu_pull = jax.vjp(exact_gelu, upper)
    hidden = activated.astype(low_type)
    lowered = product(hidden, w_down)
    output = (middle + lowered + b_down).astype(low_type).reshape(row_count, seq_len, model_width)
    grad_out = cotangent.reshape(token_count, model_width).astype(jnp.float32)
    grad_out = grad_out * valid_mask.reshape(token_count, 1).astype(jnp.float32)
    grad_out_low = grad_out.astype(low_type)
    grad_w_down = over_rows(own_columns(hidden, ff_width), grad_out_low)
    grad_b_down = jnp.sum(grad_out, axis=0)
    grad_hidden = over_cols(grad_out_low, w_down)
    (grad_upper,) = gelu_pull(grad_hidden)
    grad_upper_low = grad_upper.astype(low_type)
    own_grad_upper = own_columns(grad_upper_low, ff_width)
    grad_w_up = over_rows(normed2_low, own_grad_upper)
    grad_b_up = column_sum(own_grad_upper)
    ffn_grads, grad_upper_low = lax.optimization_barrier(
        (jnp.concatenate([grad_w_down, grad_w_up], axis=0), grad_upper_low)
    )
    ffn_grads = lax.psum(ffn_grads, "dp")
    grad_w_down, grad_w_up = ffn_grads[:ff_width], ffn_grads[ff_width:]
    grad_normed2 = product(grad_upper_low, w_up_t)
    grad_mid_norm, grad_ln2_gain, grad_ln2_shift = second_pull(grad_normed2)
    grad_middle = grad_out + grad_mid_norm
    grad_mid_low = grad_middle.astype(low_type)
    grad_w_out = over_rows(own_columns(mixed, qkv_width), grad_mid_low)
    grad_b_out = column_sum(grad_mid_low)
    grad_mixed = over_cols(grad_mid_low, w_out).astype(low_type).reshape(head_shape)
    scores_again = attention_scores(queries_split, keys_split, allowed)
    soft_again = jnp.exp(scores_again - log_total)
    grad_soft = jnp.einsum(
        "rqhe,rkhe->rhqk", grad_mixed, values_split, preferred_element_type=jnp.float32
    )
    delta = jnp.sum(soft_again * grad_soft, axis=-1, keepdims=True)
    grad_scores = (soft_again * (grad_soft - delta)).astype(low_type)
    grad_queries = jnp.einsum(
        "rhqk,rkhe->rqhe", grad_scores, keys_split, preferred_element_type=jnp.float32
    )
    grad_queries = (grad_queries * scaling).reshape(token_count, heads * HD).astype(low_type)
    grad_keys = jnp.einsum(
        "rhqk,rqhe->rkhe", grad_scores, queries_split, preferred_element_type=jnp.float32
    )
    grad_keys = (grad_keys * scaling).reshape(token_count, heads * HD).astype(low_type)
    grad_values = jnp.einsum(
        "rhqk,rqhe->rkhe",
        soft_again.astype(low_type),
        grad_mixed,
        preferred_element_type=jnp.float32,
    )
    grad_values = grad_values.reshape(token_count, heads * HD).astype(low_type)
    own_grad_queries = own_columns(grad_queries, qkv_width)
    own_grad_values = own_columns(grad_values, qkv_width)
    grad_w_query = over_rows(normed_low, own_grad_queries)
    grad_b_query = column_sum(own_grad_queries)
    grad_w_key = over_rows(normed_low, own_columns(grad_keys, qkv_width))
    grad_w_value = over_rows(normed_low, own_grad_values)
    grad_b_value = column_sum(own_grad_values)
    grad_normed = (
        product(grad_queries, w_query_t)
        + product(grad_keys, w_key_t)
        + product(grad_values, w_value_t)
    )
    grad_start_norm, grad_ln1_gain, grad_ln1_shift = first_pull(grad_normed)
    grad_start = grad_middle + grad_start_norm
    input_grad = grad_start.astype(low_type).reshape(row_count, seq_len, model_width)
    row_sums = jnp.sum(grad_start.reshape(row_count, seq_len, model_width), axis=1)
    column_count = model_width // lax.axis_size("mp")
    table_columns = own_columns(row_sums, column_count)
    step_count = step_table.shape[0]
    one_hot = (timesteps[:, None] == jnp.arange(step_count, dtype=jnp.int32)[None, :]).astype(
        jnp.float32
    )
    table_grad = lax.dot_general(
        one_hot,
        table_columns,
        CONTRACT_ROWS,
        precision=lax.Precision.HIGHEST,
        preferred_element_type=jnp.float32,
    )
    small = (
        grad_ln1_gain,
        grad_ln1_shift,
        grad_b_query,
        grad_b_value,
        grad_b_out,
        grad_b_down,
        grad_b_up,
        grad_ln2_gain,
        grad_ln2_shift,
    )
    small_rows = jnp.concatenate(small).reshape(-1, column_count)
    packed = jnp.concatenate([table_grad, small_rows], axis=0)
    tie = 0.0 * grad_w_up[0, 0]
    (
        grad_w_query,
        grad_w_key,
        grad_w_value,
        grad_w_out,
        packed,
    ) = lax.psum(
        (
            grad_w_query + tie,
            grad_w_key,
            grad_w_value,
            grad_w_out,
            packed,
        ),
        "dp",
    )
    table_grad = packed[:step_count]
    flat_small = packed[step_count:].reshape(-1)
    unpacked, at = [], 0
    for item in small:
        unpacked.append(flat_small[at : at + item.shape[0]])
        at += item.shape[0]
    (
        grad_ln1_gain,
        grad_ln1_shift,
        grad_b_query,
        grad_b_value,
        grad_b_out,
        grad_b_down,
        grad_b_up,
        grad_ln2_gain,
        grad_ln2_shift,
    ) = unpacked
    return (
        output,
        input_grad,
        grad_ln1_gain,
        grad_ln1_shift,
        grad_w_query,
        grad_b_query,
        grad_w_key,
        grad_w_value,
        grad_b_value,
        grad_w_out,
        grad_b_out,
        grad_ln2_gain,
        grad_ln2_shift,
        grad_w_up,
        grad_b_up,
        grad_w_down,
        grad_b_down,
        table_grad,
    )


def solution(mesh):
    in_specs = (
        P("dp", None, None),
        P("dp"),
        P("dp", None),
        P("dp", None),
        P(),
        P(),
        P(),
        P(None, "mp"),
        P("mp"),
        P(None, "mp"),
        P(None, "mp"),
        P("mp"),
        P("mp", None),
        P(),
        P(),
        P(),
        P(None, "mp"),
        P("mp"),
        P("mp", None),
        P(),
        P("dp", None, None),
    )
    out_specs = (
        P("dp", None, None),
        P("dp", None, None),
        P(),
        P(),
        P(None, "mp"),
        P("mp"),
        P(None, "mp"),
        P(None, "mp"),
        P("mp"),
        P("mp", None),
        P(),
        P(),
        P(),
        P(None, "mp"),
        P("mp"),
        P("mp", None),
        P(),
        P(None, "mp"),
    )
    return jax.shard_map(
        on_device, mesh=mesh, in_specs=in_specs, out_specs=out_specs, check_vma=False
    )
```

```python
import math

import jax
import jax.numpy as jnp
from jax import lax
from jax.sharding import PartitionSpec as P

HD = 64


EPSILON = 1e-05
CONTRACT_ROWS = (((0,), (0,)), ((), ()))
CONTRACT_COLS = (((1,), (1,)), ((), ()))


def normalize(values, gain, shift):
    average = jnp.mean(values, axis=-1, keepdims=True)
    centered = values - average
    variance = jnp.mean(centered * centered, axis=-1, keepdims=True)
    return centered * lax.rsqrt(variance + EPSILON) * gain + shift


def exact_gelu(values):
    return 0.5 * values * (1.0 + lax.erf(values * math.sqrt(0.5)))


def product(left, right):
    return jnp.dot(left, right, preferred_element_type=jnp.float32)


def over_rows(left, right):
    return lax.dot_general(left, right, CONTRACT_ROWS, preferred_element_type=jnp.float32)


def over_cols(left, right):
    return lax.dot_general(left, right, CONTRACT_COLS, preferred_element_type=jnp.float32)


def column_sum(values):
    return jnp.sum(values.astype(jnp.float32), axis=0)


def attention_scores(queries_split, keys_split, allowed):
    scaling = 1.0 / math.sqrt(HD)
    scores = (
        jnp.einsum("rqhe,rkhe->rhqk", queries_split, keys_split, preferred_element_type=jnp.float32)
        * scaling
    )
    return jnp.where(allowed[:, None], scores, -1e30)


def gather_pieces(blocks, one):
    n_dp = lax.axis_size("dp")
    d = lax.axis_index("dp")
    pieces = []
    for block in blocks:
        piece_rows = block.shape[0] // n_dp
        pieces.append(lax.dynamic_slice_in_dim(block, d * piece_rows, piece_rows, 0))
    sent = jnp.concatenate([p.astype(jnp.float32) for p in pieces], axis=0) * one
    got = lax.all_gather(sent, ("mp", "dp"), axis=0) * one
    n_mp = lax.axis_size("mp")
    got = got.reshape(n_mp, n_dp, *sent.shape)
    out, at = [], 0
    for p in pieces:
        rows = p.shape[0]
        out.append(got[:, :, at : at + rows])
        at += rows
    return out


def whole_rows(part, dtype):
    n_mp, n_dp, rows, width = part.shape
    return part.astype(dtype).reshape(n_mp * n_dp * rows, width)


def bias_block(vectors, width, n_dp):
    row = jnp.concatenate(vectors)
    row = jnp.pad(row, (0, width - row.shape[0]))
    return jnp.zeros((n_dp, width), jnp.float32).at[0].set(row)


def own_columns(values, width):
    return lax.dynamic_slice_in_dim(values, lax.axis_index("mp") * width, width, 1)


def on_device(
    inputs,
    timesteps,
    segments,
    valid_mask,
    step_table,
    ln1_gain,
    ln1_shift,
    w_query_shard,
    b_query_shard,
    w_key_shard,
    w_value_shard,
    b_value_shard,
    w_out_shard,
    b_out,
    ln2_gain,
    ln2_shift,
    w_up_shard,
    b_up_shard,
    w_down_shard,
    b_down,
    cotangent,
):
    row_count, seq_len, model_width = inputs.shape
    token_count = row_count * seq_len
    qkv_width = w_query_shard.shape[1]
    ff_width = w_up_shard.shape[1]
    one = 1.0 + 0.0 * ln1_gain[0]
    n_dp = lax.axis_size("dp")
    low_type = jnp.bfloat16
    q_part, k_part, v_part, qv_bias = gather_pieces(
        (
            w_query_shard.T,
            w_key_shard.T,
            w_value_shard.T,
            bias_block((b_query_shard, b_value_shard), model_width, n_dp),
        ),
        one,
    )
    w_query_t = whole_rows(q_part, low_type)
    w_key_t = whole_rows(k_part, low_type)
    w_value_t = whole_rows(v_part, low_type)
    b_query = qv_bias[:, 0, 0, :qkv_width].reshape(-1)
    b_value = qv_bias[:, 0, 0, qkv_width : 2 * qkv_width].reshape(-1)
    o_part, up_part, down_part, up_bias = gather_pieces(
        (
            w_out_shard,
            w_up_shard.T,
            w_down_shard,
            bias_block((b_up_shard,), model_width, n_dp),
        ),
        one,
    )
    w_out = whole_rows(o_part, low_type)
    w_up_t = whole_rows(up_part, low_type)
    w_down = whole_rows(down_part, low_type)
    b_up = up_bias[:, 0, 0, :].reshape(-1)
    heads = w_query_t.shape[0] // HD
    scaling = 1.0 / math.sqrt(HD)
    head_shape = (row_count, seq_len, heads, HD)
    start = inputs.astype(jnp.float32) + step_table[timesteps].astype(jnp.float32)[:, None, :]
    start = start.reshape(token_count, model_width)
    normed, first_pull = jax.vjp(normalize, start, ln1_gain, ln1_shift)
    normed_low = normed.astype(low_type)
    queries = (over_cols(normed_low, w_query_t) + b_query).astype(low_type)
    key_rows = over_cols(normed_low, w_key_t).astype(low_type)
    value_rows = (over_cols(normed_low, w_value_t) + b_value).astype(low_type)
    queries_split = queries.reshape(head_shape)
    keys_split = key_rows.reshape(head_shape)
    values_split = value_rows.reshape(head_shape)
    places = jnp.arange(seq_len, dtype=jnp.int32)
    diagonal = places[:, None] == places[None, :]
    allowed = (segments[:, :, None] == segments[:, None, :]) & (
        (valid_mask[:, None, :] > 0) | diagonal[None]
    )
    scores = attention_scores(queries_split, keys_split, allowed)
    row_max = jnp.max(scores, axis=-1, keepdims=True)
    powers = jnp.exp(scores - row_max)
    total = jnp.sum(powers, axis=-1, keepdims=True)
    log_total = row_max + jnp.log(total)
    probabilities = powers / total
    mixed = jnp.einsum(
        "rhqk,rkhe->rqhe",
        probabilities.astype(low_type),
        values_split,
        preferred_element_type=jnp.float32,
    )
    mixed = mixed.reshape(token_count, heads * HD).astype(low_type)
    attended = product(mixed, w_out) + b_out
    middle = start + attended
    normed2, second_pull = jax.vjp(normalize, middle, ln2_gain, ln2_shift)
    normed2_low = normed2.astype(low_type)
    upper = over_cols(normed2_low, w_up_t) + b_up
    activated, gelu_pull = jax.vjp(exact_gelu, upper)
    hidden = activated.astype(low_type)
    lowered = product(hidden, w_down)
    output = (middle + lowered + b_down).astype(low_type).reshape(row_count, seq_len, model_width)
    grad_out = cotangent.reshape(token_count, model_width).astype(jnp.float32)
    grad_out = grad_out * valid_mask.reshape(token_count, 1).astype(jnp.float32)
    grad_out_low = grad_out.astype(low_type)
    grad_w_down = over_rows(own_columns(hidden, ff_width), grad_out_low)
    grad_b_down = jnp.sum(grad_out, axis=0)
    grad_hidden = over_cols(grad_out_low, w_down)
    (grad_upper,) = gelu_pull(grad_hidden)
    grad_upper_low = grad_upper.astype(low_type)
    own_grad_upper = own_columns(grad_upper_low, ff_width)
    grad_w_up = over_rows(normed2_low, own_grad_upper)
    grad_b_up = column_sum(own_grad_upper)
    grad_normed2 = product(grad_upper_low, w_up_t)
    grad_mid_norm, grad_ln2_gain, grad_ln2_shift = second_pull(grad_normed2)
    grad_middle = grad_out + grad_mid_norm
    grad_mid_low = grad_middle.astype(low_type)
    grad_w_out = over_rows(own_columns(mixed, qkv_width), grad_mid_low)
    grad_b_out = column_sum(grad_mid_low)
    grad_mixed = over_cols(grad_mid_low, w_out).astype(low_type).reshape(head_shape)
    scores_again = attention_scores(queries_split, keys_split, allowed)
    soft_again = jnp.exp(scores_again - log_total)
    grad_soft = jnp.einsum(
        "rqhe,rkhe->rhqk", grad_mixed, values_split, preferred_element_type=jnp.float32
    )
    delta = jnp.sum(soft_again * grad_soft, axis=-1, keepdims=True)
    grad_scores = (soft_again * (grad_soft - delta)).astype(low_type)
    grad_queries = jnp.einsum(
        "rhqk,rkhe->rqhe", grad_scores, keys_split, preferred_element_type=jnp.float32
    )
    grad_queries = (grad_queries * scaling).reshape(token_count, heads * HD).astype(low_type)
    grad_keys = jnp.einsum(
        "rhqk,rqhe->rkhe", grad_scores, queries_split, preferred_element_type=jnp.float32
    )
    grad_keys = (grad_keys * scaling).reshape(token_count, heads * HD).astype(low_type)
    grad_values = jnp.einsum(
        "rhqk,rqhe->rkhe",
        soft_again.astype(low_type),
        grad_mixed,
        preferred_element_type=jnp.float32,
    )
    grad_values = grad_values.reshape(token_count, heads * HD).astype(low_type)
    own_grad_queries = own_columns(grad_queries, qkv_width)
    own_grad_values = own_columns(grad_values, qkv_width)
    grad_w_query = over_rows(normed_low, own_grad_queries)
    grad_b_query = column_sum(own_grad_queries)
    grad_w_key = over_rows(normed_low, own_columns(grad_keys, qkv_width))
    grad_w_value = over_rows(normed_low, own_grad_values)
    grad_b_value = column_sum(own_grad_values)
    grad_normed = (
        product(grad_queries, w_query_t)
        + product(grad_keys, w_key_t)
        + product(grad_values, w_value_t)
    )
    grad_start_norm, grad_ln1_gain, grad_ln1_shift = first_pull(grad_normed)
    grad_start = grad_middle + grad_start_norm
    input_grad = grad_start.astype(low_type).reshape(row_count, seq_len, model_width)
    row_sums = jnp.sum(grad_start.reshape(row_count, seq_len, model_width), axis=1)
    column_count = model_width // lax.axis_size("mp")
    table_columns = own_columns(row_sums, column_count)
    step_count = step_table.shape[0]
    one_hot = (timesteps[:, None] == jnp.arange(step_count, dtype=jnp.int32)[None, :]).astype(
        jnp.float32
    )
    table_grad = lax.dot_general(
        one_hot,
        table_columns,
        CONTRACT_ROWS,
        precision=lax.Precision.HIGHEST,
        preferred_element_type=jnp.float32,
    )
    small = (
        grad_ln1_gain,
        grad_ln1_shift,
        grad_b_query,
        grad_b_value,
        grad_b_out,
        grad_b_down,
        grad_b_up,
        grad_ln2_gain,
        grad_ln2_shift,
    )
    small_rows = jnp.concatenate(small).reshape(-1, column_count)
    packed = jnp.concatenate([table_grad, small_rows], axis=0)
    (
        grad_w_query,
        grad_w_key,
        grad_w_value,
        grad_w_out,
        packed,
        grad_w_down,
        grad_w_up,
    ) = lax.psum(
        (
            grad_w_query,
            grad_w_key,
            grad_w_value,
            grad_w_out,
            packed,
            grad_w_down,
            grad_w_up,
        ),
        "dp",
    )
    table_grad = packed[:step_count]
    flat_small = packed[step_count:].reshape(-1)
    unpacked, at = [], 0
    for item in small:
        unpacked.append(flat_small[at : at + item.shape[0]])
        at += item.shape[0]
    (
        grad_ln1_gain,
        grad_ln1_shift,
        grad_b_query,
        grad_b_value,
        grad_b_out,
        grad_b_down,
        grad_b_up,
        grad_ln2_gain,
        grad_ln2_shift,
    ) = unpacked
    return (
        output,
        input_grad,
        grad_ln1_gain,
        grad_ln1_shift,
        grad_w_query,
        grad_b_query,
        grad_w_key,
        grad_w_value,
        grad_b_value,
        grad_w_out,
        grad_b_out,
        grad_ln2_gain,
        grad_ln2_shift,
        grad_w_up,
        grad_b_up,
        grad_w_down,
        grad_b_down,
        table_grad,
    )


def solution(mesh):
    in_specs = (
        P("dp", None, None),
        P("dp"),
        P("dp", None),
        P("dp", None),
        P(),
        P(),
        P(),
        P(None, "mp"),
        P("mp"),
        P(None, "mp"),
        P(None, "mp"),
        P("mp"),
        P("mp", None),
        P(),
        P(),
        P(),
        P(None, "mp"),
        P("mp"),
        P("mp", None),
        P(),
        P("dp", None, None),
    )
    out_specs = (
        P("dp", None, None),
        P("dp", None, None),
        P(),
        P(),
        P(None, "mp"),
        P("mp"),
        P(None, "mp"),
        P(None, "mp"),
        P("mp"),
        P("mp", None),
        P(),
        P(),
        P(),
        P(None, "mp"),
        P("mp"),
        P("mp", None),
        P(),
        P(None, "mp"),
    )
    return jax.shard_map(
        on_device, mesh=mesh, in_specs=in_specs, out_specs=out_specs, check_vma=False
    )
```

```python
import math

import jax
import jax.numpy as jnp
from jax import lax
from jax.sharding import Mesh, PartitionSpec as P

HD = 64


EPSILON = 1e-05
CONTRACT_ROWS = (((0,), (0,)), ((), ()))
CONTRACT_COLS = (((1,), (1,)), ((), ()))


def normalize(values, gain, shift):
    average = jnp.mean(values, axis=-1, keepdims=True)
    centered = values - average
    variance = jnp.mean(centered * centered, axis=-1, keepdims=True)
    return centered * lax.rsqrt(variance + EPSILON) * gain + shift


def exact_gelu(values):
    return 0.5 * values * (1.0 + lax.erf(values * math.sqrt(0.5)))


def product(left, right):
    return jnp.dot(left, right, preferred_element_type=jnp.float32)


def over_rows(left, right):
    return lax.dot_general(left, right, CONTRACT_ROWS, preferred_element_type=jnp.float32)


def over_cols(left, right):
    return lax.dot_general(left, right, CONTRACT_COLS, preferred_element_type=jnp.float32)


def column_sum(values):
    return jnp.sum(values.astype(jnp.float32), axis=0)


def attention_scores(queries_split, keys_split, allowed):
    scaling = 1.0 / math.sqrt(HD)
    scores = (
        jnp.einsum("rqhe,rkhe->rhqk", queries_split, keys_split, preferred_element_type=jnp.float32)
        * scaling
    )
    return jnp.where(allowed[:, None], scores, -1e30)


DP = ("dpo", "core")


def gather_pieces(blocks, one):
    n_dpo = lax.axis_size("dpo")
    n_mp = lax.axis_size("mp")
    c = lax.axis_index("core")
    j = lax.axis_index("dpo")
    pieces = []
    for block in blocks:
        piece_rows = block.shape[0] // (2 * n_dpo)
        at = (c * n_dpo + j) * piece_rows
        pieces.append(lax.dynamic_slice_in_dim(block, at, piece_rows, 0))
    sent = jnp.concatenate([p.astype(jnp.float32) for p in pieces], axis=0) * one
    half = lax.all_gather(sent, ("mp", "dpo"), axis=0) * one
    other = lax.ppermute(half, "core", [(0, 1), (1, 0)]) * one
    mine_first = jnp.stack([half, other])
    other_first = jnp.stack([other, half])
    both = jnp.where(c == 0, mine_first, other_first)
    both = both.reshape(2, n_mp, n_dpo, *sent.shape).transpose(1, 0, 2, 3, 4)
    out, at = [], 0
    for p in pieces:
        rows = p.shape[0]
        out.append(both[:, :, :, at : at + rows])
        at += rows
    return out


def whole_rows(part, dtype):
    n_mp, n_core, n_dpo, rows, width = part.shape
    return part.astype(dtype).reshape(n_mp * n_core * n_dpo * rows, width)


def bias_block(vectors, width, n_pieces):
    row = jnp.concatenate(vectors)
    row = jnp.pad(row, (0, width - row.shape[0]))
    return jnp.zeros((n_pieces, width), jnp.float32).at[0].set(row)


def own_columns(values, width):
    return lax.dynamic_slice_in_dim(values, lax.axis_index("mp") * width, width, 1)


def on_device(
    inputs,
    timesteps,
    segments,
    valid_mask,
    step_table,
    ln1_gain,
    ln1_shift,
    w_query_shard,
    b_query_shard,
    w_key_shard,
    w_value_shard,
    b_value_shard,
    w_out_shard,
    b_out,
    ln2_gain,
    ln2_shift,
    w_up_shard,
    b_up_shard,
    w_down_shard,
    b_down,
    cotangent,
):
    row_count, seq_len, model_width = inputs.shape
    token_count = row_count * seq_len
    qkv_width = w_query_shard.shape[1]
    ff_width = w_up_shard.shape[1]
    one = 1.0 + 0.0 * ln1_gain[0]
    n_dp = lax.axis_size("dpo") * lax.axis_size("core")
    low_type = jnp.bfloat16
    q_part, k_part, v_part, qv_bias = gather_pieces(
        (
            w_query_shard.T,
            w_key_shard.T,
            w_value_shard.T,
            bias_block((b_query_shard, b_value_shard), model_width, n_dp),
        ),
        one,
    )
    w_query_t = whole_rows(q_part, low_type)
    w_key_t = whole_rows(k_part, low_type)
    w_value_t = whole_rows(v_part, low_type)
    b_query = qv_bias[:, 0, 0, 0, :qkv_width].reshape(-1)
    b_value = qv_bias[:, 0, 0, 0, qkv_width : 2 * qkv_width].reshape(-1)
    o_part, up_part, down_part, up_bias = gather_pieces(
        (
            w_out_shard,
            w_up_shard.T,
            w_down_shard,
            bias_block((b_up_shard,), model_width, n_dp),
        ),
        one,
    )
    w_out = whole_rows(o_part, low_type)
    w_up_t = whole_rows(up_part, low_type)
    w_down = whole_rows(down_part, low_type)
    b_up = up_bias[:, 0, 0, 0, :].reshape(-1)
    heads = w_query_t.shape[0] // HD
    scaling = 1.0 / math.sqrt(HD)
    head_shape = (row_count, seq_len, heads, HD)
    start = inputs.astype(jnp.float32) + step_table[timesteps].astype(jnp.float32)[:, None, :]
    start = start.reshape(token_count, model_width)
    normed, first_pull = jax.vjp(normalize, start, ln1_gain, ln1_shift)
    normed_low = normed.astype(low_type)
    queries = (over_cols(normed_low, w_query_t) + b_query).astype(low_type)
    key_rows = over_cols(normed_low, w_key_t).astype(low_type)
    value_rows = (over_cols(normed_low, w_value_t) + b_value).astype(low_type)
    queries_split = queries.reshape(head_shape)
    keys_split = key_rows.reshape(head_shape)
    values_split = value_rows.reshape(head_shape)
    places = jnp.arange(seq_len, dtype=jnp.int32)
    diagonal = places[:, None] == places[None, :]
    allowed = (segments[:, :, None] == segments[:, None, :]) & (
        (valid_mask[:, None, :] > 0) | diagonal[None]
    )
    scores = attention_scores(queries_split, keys_split, allowed)
    row_max = jnp.max(scores, axis=-1, keepdims=True)
    powers = jnp.exp(scores - row_max)
    total = jnp.sum(powers, axis=-1, keepdims=True)
    log_total = row_max + jnp.log(total)
    probabilities = powers / total
    mixed = jnp.einsum(
        "rhqk,rkhe->rqhe",
        probabilities.astype(low_type),
        values_split,
        preferred_element_type=jnp.float32,
    )
    mixed = mixed.reshape(token_count, heads * HD).astype(low_type)
    attended = product(mixed, w_out) + b_out
    middle = start + attended
    normed2, second_pull = jax.vjp(normalize, middle, ln2_gain, ln2_shift)
    normed2_low = normed2.astype(low_type)
    upper = over_cols(normed2_low, w_up_t) + b_up
    activated, gelu_pull = jax.vjp(exact_gelu, upper)
    hidden = activated.astype(low_type)
    lowered = product(hidden, w_down)
    output = (middle + lowered + b_down).astype(low_type).reshape(row_count, seq_len, model_width)
    grad_out = cotangent.reshape(token_count, model_width).astype(jnp.float32)
    grad_out = grad_out * valid_mask.reshape(token_count, 1).astype(jnp.float32)
    grad_out_low = grad_out.astype(low_type)
    grad_w_down = over_rows(own_columns(hidden, ff_width), grad_out_low)
    grad_b_down = jnp.sum(grad_out, axis=0)
    grad_hidden = over_cols(grad_out_low, w_down)
    (grad_upper,) = gelu_pull(grad_hidden)
    grad_upper_low = grad_upper.astype(low_type)
    own_grad_upper = own_columns(grad_upper_low, ff_width)
    grad_w_up = over_rows(normed2_low, own_grad_upper)
    grad_b_up = column_sum(own_grad_upper)
    grad_normed2 = product(grad_upper_low, w_up_t)
    grad_mid_norm, grad_ln2_gain, grad_ln2_shift = second_pull(grad_normed2)
    grad_middle = grad_out + grad_mid_norm
    grad_mid_low = grad_middle.astype(low_type)
    grad_w_out = over_rows(own_columns(mixed, qkv_width), grad_mid_low)
    grad_b_out = column_sum(grad_mid_low)
    grad_mixed = over_cols(grad_mid_low, w_out).astype(low_type).reshape(head_shape)
    scores_again = attention_scores(queries_split, keys_split, allowed)
    soft_again = jnp.exp(scores_again - log_total)
    grad_soft = jnp.einsum(
        "rqhe,rkhe->rhqk", grad_mixed, values_split, preferred_element_type=jnp.float32
    )
    delta = jnp.sum(soft_again * grad_soft, axis=-1, keepdims=True)
    grad_scores = (soft_again * (grad_soft - delta)).astype(low_type)
    grad_queries = jnp.einsum(
        "rhqk,rkhe->rqhe", grad_scores, keys_split, preferred_element_type=jnp.float32
    )
    grad_queries = (grad_queries * scaling).reshape(token_count, heads * HD).astype(low_type)
    grad_keys = jnp.einsum(
        "rhqk,rqhe->rkhe", grad_scores, queries_split, preferred_element_type=jnp.float32
    )
    grad_keys = (grad_keys * scaling).reshape(token_count, heads * HD).astype(low_type)
    grad_values = jnp.einsum(
        "rhqk,rqhe->rkhe",
        soft_again.astype(low_type),
        grad_mixed,
        preferred_element_type=jnp.float32,
    )
    grad_values = grad_values.reshape(token_count, heads * HD).astype(low_type)
    own_grad_queries = own_columns(grad_queries, qkv_width)
    own_grad_values = own_columns(grad_values, qkv_width)
    grad_w_query = over_rows(normed_low, own_grad_queries)
    grad_b_query = column_sum(own_grad_queries)
    grad_w_key = over_rows(normed_low, own_columns(grad_keys, qkv_width))
    grad_w_value = over_rows(normed_low, own_grad_values)
    grad_b_value = column_sum(own_grad_values)
    grad_normed = (
        product(grad_queries, w_query_t)
        + product(grad_keys, w_key_t)
        + product(grad_values, w_value_t)
    )
    grad_start_norm, grad_ln1_gain, grad_ln1_shift = first_pull(grad_normed)
    grad_start = grad_middle + grad_start_norm
    input_grad = grad_start.astype(low_type).reshape(row_count, seq_len, model_width)
    row_sums = jnp.sum(grad_start.reshape(row_count, seq_len, model_width), axis=1)
    column_count = model_width // lax.axis_size("mp")
    table_columns = own_columns(row_sums, column_count)
    step_count = step_table.shape[0]
    one_hot = (timesteps[:, None] == jnp.arange(step_count, dtype=jnp.int32)[None, :]).astype(
        jnp.float32
    )
    table_grad = lax.dot_general(
        one_hot,
        table_columns,
        CONTRACT_ROWS,
        precision=lax.Precision.HIGHEST,
        preferred_element_type=jnp.float32,
    )
    small = (
        grad_ln1_gain,
        grad_ln1_shift,
        grad_b_query,
        grad_b_value,
        grad_b_out,
        grad_b_down,
        grad_b_up,
        grad_ln2_gain,
        grad_ln2_shift,
    )
    small_rows = jnp.concatenate(small).reshape(-1, column_count)
    packed = jnp.concatenate([table_grad, small_rows], axis=0)
    (
        grad_w_query,
        grad_w_key,
        grad_w_value,
        grad_w_out,
        packed,
        grad_w_down,
        grad_w_up,
    ) = lax.psum(
        (
            grad_w_query,
            grad_w_key,
            grad_w_value,
            grad_w_out,
            packed,
            grad_w_down,
            grad_w_up,
        ),
        DP,
    )
    table_grad = packed[:step_count]
    flat_small = packed[step_count:].reshape(-1)
    unpacked, at = [], 0
    for item in small:
        unpacked.append(flat_small[at : at + item.shape[0]])
        at += item.shape[0]
    (
        grad_ln1_gain,
        grad_ln1_shift,
        grad_b_query,
        grad_b_value,
        grad_b_out,
        grad_b_down,
        grad_b_up,
        grad_ln2_gain,
        grad_ln2_shift,
    ) = unpacked
    return (
        output,
        input_grad,
        grad_ln1_gain,
        grad_ln1_shift,
        grad_w_query,
        grad_b_query,
        grad_w_key,
        grad_w_value,
        grad_b_value,
        grad_w_out,
        grad_b_out,
        grad_ln2_gain,
        grad_ln2_shift,
        grad_w_up,
        grad_b_up,
        grad_w_down,
        grad_b_down,
        table_grad,
    )


def solution(mesh):
    in_specs = (
        P(DP, None, None),
        P(DP),
        P(DP, None),
        P(DP, None),
        P(),
        P(),
        P(),
        P(None, "mp"),
        P("mp"),
        P(None, "mp"),
        P(None, "mp"),
        P("mp"),
        P("mp", None),
        P(),
        P(),
        P(),
        P(None, "mp"),
        P("mp"),
        P("mp", None),
        P(),
        P(DP, None, None),
    )
    out_specs = (
        P(DP, None, None),
        P(DP, None, None),
        P(),
        P(),
        P(None, "mp"),
        P("mp"),
        P(None, "mp"),
        P(None, "mp"),
        P("mp"),
        P("mp", None),
        P(),
        P(),
        P(),
        P(None, "mp"),
        P("mp"),
        P("mp", None),
        P(),
        P(None, "mp"),
    )
    n_dp, n_mp = mesh.devices.shape
    split = Mesh(mesh.devices.reshape(n_dp // 2, 2, n_mp), ("dpo", "core", "mp"))
    return jax.shard_map(
        on_device, mesh=split, in_specs=in_specs, out_specs=out_specs, check_vma=False
    )
```

```python
import math

import jax
import jax.numpy as jnp
from jax import lax
from jax.sharding import PartitionSpec as P


HD = 64


EPSILON = 1e-05
CONTRACT_ROWS = (((0,), (0,)), ((), ()))
CONTRACT_COLS = (((1,), (1,)), ((), ()))


def normalize(values, gain, shift):
    average = jnp.mean(values, axis=-1, keepdims=True)
    centered = values - average
    variance = jnp.mean(centered * centered, axis=-1, keepdims=True)
    return centered * lax.rsqrt(variance + EPSILON) * gain + shift


def exact_gelu(values):
    return 0.5 * values * (1.0 + lax.erf(values * math.sqrt(0.5)))


def product(left, right):
    return jnp.dot(left, right, preferred_element_type=jnp.float32)


def over_rows(left, right):
    return lax.dot_general(left, right, CONTRACT_ROWS, preferred_element_type=jnp.float32)


def over_cols(left, right):
    return lax.dot_general(left, right, CONTRACT_COLS, preferred_element_type=jnp.float32)


def column_sum(values):
    return jnp.sum(values.astype(jnp.float32), axis=0)


def attention_scores(queries_split, keys_split, allowed):
    scaling = 1.0 / math.sqrt(HD)
    scores = (
        jnp.einsum("rqhe,rkhe->rhqk", queries_split, keys_split, preferred_element_type=jnp.float32)
        * scaling
    )
    return jnp.where(allowed[:, None], scores, -1e30)


def gather_pieces(blocks, one):
    n_dp = lax.axis_size("dp")
    d = lax.axis_index("dp")
    pieces = []
    for block in blocks:
        piece_rows = block.shape[0] // n_dp
        pieces.append(lax.dynamic_slice_in_dim(block, d * piece_rows, piece_rows, 0))
    sent = jnp.concatenate([p.astype(jnp.float32) for p in pieces], axis=0) * one
    got = lax.all_gather(sent, ("mp", "dp"), axis=0) * one
    n_mp = lax.axis_size("mp")
    got = got.reshape(n_mp, n_dp, *sent.shape)
    out, at = [], 0
    for p in pieces:
        rows = p.shape[0]
        out.append(got[:, :, at : at + rows])
        at += rows
    return out


def whole_rows(part, dtype):
    n_mp, n_dp, rows, width = part.shape
    return part.astype(dtype).reshape(n_mp * n_dp * rows, width)


def bias_block(vectors, width, n_dp):
    row = jnp.concatenate(vectors)
    row = jnp.pad(row, (0, width - row.shape[0]))
    return jnp.zeros((n_dp, width), jnp.float32).at[0].set(row)


def own_columns(values, width):
    return lax.dynamic_slice_in_dim(values, lax.axis_index("mp") * width, width, 1)


def on_device(
    inputs,
    timesteps,
    segments,
    valid_mask,
    step_table,
    ln1_gain,
    ln1_shift,
    w_query_shard,
    b_query_shard,
    w_key_shard,
    w_value_shard,
    b_value_shard,
    w_out_shard,
    b_out,
    ln2_gain,
    ln2_shift,
    w_up_shard,
    b_up_shard,
    w_down_shard,
    b_down,
    cotangent,
):
    row_count, seq_len, model_width = inputs.shape
    token_count = row_count * seq_len
    qkv_width = w_query_shard.shape[1]
    ff_width = w_up_shard.shape[1]
    one = 1.0 + 0.0 * ln1_gain[0]
    n_dp = lax.axis_size("dp")
    low_type = jnp.bfloat16
    q_part, k_part, v_part, qv_bias = gather_pieces(
        (
            w_query_shard.T,
            w_key_shard.T,
            w_value_shard.T,
            bias_block((b_query_shard, b_value_shard), model_width, n_dp),
        ),
        one,
    )
    w_query_t = whole_rows(q_part, low_type)
    w_key_t = whole_rows(k_part, low_type)
    w_value_t = whole_rows(v_part, low_type)
    b_query = qv_bias[:, 0, 0, :qkv_width].reshape(-1)
    b_value = qv_bias[:, 0, 0, qkv_width : 2 * qkv_width].reshape(-1)
    o_part, up_part, down_part, up_bias = gather_pieces(
        (
            w_out_shard,
            w_up_shard.T,
            w_down_shard,
            bias_block((b_up_shard,), model_width, n_dp),
        ),
        one,
    )
    w_out = whole_rows(o_part, low_type)
    w_up_t = whole_rows(up_part, low_type)
    w_down = whole_rows(down_part, low_type)
    b_up = up_bias[:, 0, 0, :].reshape(-1)
    heads = w_query_t.shape[0] // HD
    scaling = 1.0 / math.sqrt(HD)
    head_shape = (row_count, seq_len, heads, HD)
    start = inputs.astype(jnp.float32) + step_table[timesteps].astype(jnp.float32)[:, None, :]
    start = start.reshape(token_count, model_width)
    normed, first_pull = jax.vjp(normalize, start, ln1_gain, ln1_shift)
    normed_low = normed.astype(low_type)
    queries = (over_cols(normed_low, w_query_t) + b_query).astype(low_type)
    key_rows = over_cols(normed_low, w_key_t).astype(low_type)
    value_rows = (over_cols(normed_low, w_value_t) + b_value).astype(low_type)
    queries_split = queries.reshape(head_shape)
    keys_split = key_rows.reshape(head_shape)
    values_split = value_rows.reshape(head_shape)
    places = jnp.arange(seq_len, dtype=jnp.int32)
    diagonal = places[:, None] == places[None, :]
    allowed = (segments[:, :, None] == segments[:, None, :]) & (
        (valid_mask[:, None, :] > 0) | diagonal[None]
    )
    scores = attention_scores(queries_split, keys_split, allowed)
    row_max = jnp.max(scores, axis=-1, keepdims=True)
    powers = jnp.exp(scores - row_max)
    total = jnp.sum(powers, axis=-1, keepdims=True)
    log_total = row_max + jnp.log(total)
    probabilities = powers / total
    mixed = jnp.einsum(
        "rhqk,rkhe->rqhe",
        probabilities.astype(low_type),
        values_split,
        preferred_element_type=jnp.float32,
    )
    mixed = mixed.reshape(token_count, heads * HD).astype(low_type)
    attended = product(mixed, w_out) + b_out
    middle = start + attended
    normed2, second_pull = jax.vjp(normalize, middle, ln2_gain, ln2_shift)
    normed2_low = normed2.astype(low_type)
    upper = over_cols(normed2_low, w_up_t) + b_up
    activated, gelu_pull = jax.vjp(exact_gelu, upper)
    hidden = activated.astype(low_type)
    lowered = product(hidden, w_down)
    output = (middle + lowered + b_down).astype(low_type).reshape(row_count, seq_len, model_width)
    grad_out = cotangent.reshape(token_count, model_width).astype(jnp.float32)
    grad_out = grad_out * valid_mask.reshape(token_count, 1).astype(jnp.float32)
    grad_out_low = grad_out.astype(low_type)
    grad_out, grad_out_low = lax.optimization_barrier((grad_out, grad_out_low))
    grad_w_down = over_rows(own_columns(hidden, ff_width), grad_out_low)
    grad_b_down = jnp.sum(grad_out, axis=0)
    grad_hidden = over_cols(grad_out_low, w_down)
    (grad_upper,) = gelu_pull(grad_hidden)
    grad_upper_low = grad_upper.astype(low_type)
    own_grad_upper = own_columns(grad_upper_low, ff_width)
    grad_w_up = over_rows(normed2_low, own_grad_upper)
    grad_b_up = column_sum(own_grad_upper)
    ffn_grads = lax.psum(jnp.concatenate([grad_w_down, grad_w_up], axis=0), "dp")
    grad_w_down, grad_w_up = ffn_grads[:ff_width], ffn_grads[ff_width:]
    grad_normed2 = product(grad_upper_low, w_up_t)
    grad_mid_norm, grad_ln2_gain, grad_ln2_shift = second_pull(grad_normed2)
    grad_middle = grad_out + grad_mid_norm
    grad_mid_low = grad_middle.astype(low_type)
    grad_w_out = over_rows(own_columns(mixed, qkv_width), grad_mid_low)
    grad_b_out = column_sum(grad_mid_low)
    grad_mixed = over_cols(grad_mid_low, w_out).astype(low_type).reshape(head_shape)
    scores_again = attention_scores(queries_split, keys_split, allowed)
    soft_again = jnp.exp(scores_again - log_total)
    grad_soft = jnp.einsum(
        "rqhe,rkhe->rhqk", grad_mixed, values_split, preferred_element_type=jnp.float32
    )
    delta = jnp.sum(soft_again * grad_soft, axis=-1, keepdims=True)
    grad_scores = (soft_again * (grad_soft - delta)).astype(low_type)
    grad_queries = jnp.einsum(
        "rhqk,rkhe->rqhe", grad_scores, keys_split, preferred_element_type=jnp.float32
    )
    grad_queries = (grad_queries * scaling).reshape(token_count, heads * HD).astype(low_type)
    grad_keys = jnp.einsum(
        "rhqk,rqhe->rkhe", grad_scores, queries_split, preferred_element_type=jnp.float32
    )
    grad_keys = (grad_keys * scaling).reshape(token_count, heads * HD).astype(low_type)
    grad_values = jnp.einsum(
        "rhqk,rqhe->rkhe",
        soft_again.astype(low_type),
        grad_mixed,
        preferred_element_type=jnp.float32,
    )
    grad_values = grad_values.reshape(token_count, heads * HD).astype(low_type)
    own_grad_queries = own_columns(grad_queries, qkv_width)
    own_grad_values = own_columns(grad_values, qkv_width)
    grad_w_query = over_rows(normed_low, own_grad_queries)
    grad_b_query = column_sum(own_grad_queries)
    grad_w_key = over_rows(normed_low, own_columns(grad_keys, qkv_width))
    grad_w_value = over_rows(normed_low, own_grad_values)
    grad_b_value = column_sum(own_grad_values)
    grad_normed = (
        product(grad_queries, w_query_t)
        + product(grad_keys, w_key_t)
        + product(grad_values, w_value_t)
    )
    grad_start_norm, grad_ln1_gain, grad_ln1_shift = first_pull(grad_normed)
    grad_start = grad_middle + grad_start_norm
    input_grad = grad_start.astype(low_type).reshape(row_count, seq_len, model_width)
    row_sums = jnp.sum(grad_start.reshape(row_count, seq_len, model_width), axis=1)
    column_count = model_width // lax.axis_size("mp")
    table_columns = own_columns(row_sums, column_count)
    step_count = step_table.shape[0]
    one_hot = (timesteps[:, None] == jnp.arange(step_count, dtype=jnp.int32)[None, :]).astype(
        jnp.float32
    )
    table_grad = lax.dot_general(
        one_hot,
        table_columns,
        CONTRACT_ROWS,
        precision=lax.Precision.HIGHEST,
        preferred_element_type=jnp.float32,
    )
    small = (
        grad_ln1_gain,
        grad_ln1_shift,
        grad_b_query,
        grad_b_value,
        grad_b_out,
        grad_b_down,
        grad_b_up,
        grad_ln2_gain,
        grad_ln2_shift,
    )
    small_rows = jnp.concatenate(small).reshape(-1, column_count)
    packed = jnp.concatenate([table_grad, small_rows], axis=0)
    tie = 0.0 * ffn_grads[0, 0]
    (
        grad_w_query,
        grad_w_key,
        grad_w_value,
        grad_w_out,
        packed,
    ) = lax.psum(
        (
            grad_w_query + tie,
            grad_w_key,
            grad_w_value,
            grad_w_out,
            packed,
        ),
        "dp",
    )
    table_grad = packed[:step_count]
    flat_small = packed[step_count:].reshape(-1)
    unpacked, at = [], 0
    for item in small:
        unpacked.append(flat_small[at : at + item.shape[0]])
        at += item.shape[0]
    (
        grad_ln1_gain,
        grad_ln1_shift,
        grad_b_query,
        grad_b_value,
        grad_b_out,
        grad_b_down,
        grad_b_up,
        grad_ln2_gain,
        grad_ln2_shift,
    ) = unpacked
    return (
        output,
        input_grad,
        grad_ln1_gain,
        grad_ln1_shift,
        grad_w_query,
        grad_b_query,
        grad_w_key,
        grad_w_value,
        grad_b_value,
        grad_w_out,
        grad_b_out,
        grad_ln2_gain,
        grad_ln2_shift,
        grad_w_up,
        grad_b_up,
        grad_w_down,
        grad_b_down,
        table_grad,
    )


def solution(mesh):
    in_specs = (
        P("dp", None, None),
        P("dp"),
        P("dp", None),
        P("dp", None),
        P(),
        P(),
        P(),
        P(None, "mp"),
        P("mp"),
        P(None, "mp"),
        P(None, "mp"),
        P("mp"),
        P("mp", None),
        P(),
        P(),
        P(),
        P(None, "mp"),
        P("mp"),
        P("mp", None),
        P(),
        P("dp", None, None),
    )
    out_specs = (
        P("dp", None, None),
        P("dp", None, None),
        P(),
        P(),
        P(None, "mp"),
        P("mp"),
        P(None, "mp"),
        P(None, "mp"),
        P("mp"),
        P("mp", None),
        P(),
        P(),
        P(),
        P(None, "mp"),
        P("mp"),
        P("mp", None),
        P(),
        P(None, "mp"),
    )

    return jax.shard_map(
        on_device, mesh=mesh, in_specs=in_specs, out_specs=out_specs, check_vma=False
    )
```

```python
import math

import jax
import jax.numpy as jnp
from jax import lax
from jax.experimental import pallas as pl
from jax.sharding import PartitionSpec as P


HD = 64
SCALE = 1.0 / math.sqrt(HD)


EPSILON = 1e-05
CONTRACT_ROWS = (((0,), (0,)), ((), ()))
CONTRACT_COLS = (((1,), (1,)), ((), ()))


def normalize(values, gain, shift):
    average = jnp.mean(values, axis=-1, keepdims=True)
    centered = values - average
    variance = jnp.mean(centered * centered, axis=-1, keepdims=True)
    return centered * lax.rsqrt(variance + EPSILON) * gain + shift


def exact_gelu(values):
    return 0.5 * values * (1.0 + lax.erf(values * math.sqrt(0.5)))


def product(left, right):
    return jnp.dot(left, right, preferred_element_type=jnp.float32)


def over_rows(left, right):
    return lax.dot_general(left, right, CONTRACT_ROWS, preferred_element_type=jnp.float32)


def over_cols(left, right):
    return lax.dot_general(left, right, CONTRACT_COLS, preferred_element_type=jnp.float32)


def column_sum(values):
    return jnp.sum(values.astype(jnp.float32), axis=0)


NT = (((1,), (1,)), ((), ()))
TN = (((0,), (0,)), ((), ()))


def _allowed(segc_ref, segr_ref, valid_ref, seq):
    rows = lax.broadcasted_iota(jnp.int32, (seq, seq), 0)
    cols = lax.broadcasted_iota(jnp.int32, (seq, seq), 1)
    return (segc_ref[0] == segr_ref[0]) & ((valid_ref[0] > 0) | (rows == cols))


def _fwd_kernel(q_ref, k_ref, v_ref, segc_ref, segr_ref, valid_ref, o_ref, lse_ref):
    seq, width = q_ref.shape
    allowed = _allowed(segc_ref, segr_ref, valid_ref, seq)
    outs, lses = [], []
    for h in range(width // HD):
        cols = slice(h * HD, (h + 1) * HD)
        qh, kh, vh = q_ref[:, cols], k_ref[:, cols], v_ref[:, cols]
        s = lax.dot_general(qh, kh, NT, preferred_element_type=jnp.float32) * SCALE
        s = jnp.where(allowed, s, -1e30)
        m = jnp.max(s, axis=-1, keepdims=True)
        p = jnp.exp(s - m)
        total = jnp.sum(p, axis=-1, keepdims=True)
        prob = p / total
        o = jnp.dot(prob.astype(jnp.bfloat16), vh, preferred_element_type=jnp.float32)
        outs.append(o.astype(jnp.bfloat16))
        lses.append(m + jnp.log(total))
    o_ref[...] = jnp.concatenate(outs, axis=1)
    lse_ref[0] = jnp.concatenate(lses, axis=1)


def _bwd_kernel(q_ref, k_ref, v_ref, g_ref, lse_ref, segc_ref, segr_ref, valid_ref,
                dq_ref, dk_ref, dv_ref):
    seq, width = q_ref.shape
    allowed = _allowed(segc_ref, segr_ref, valid_ref, seq)
    lse = lse_ref[0]
    dqs, dks, dvs = [], [], []
    for h in range(width // HD):
        cols = slice(h * HD, (h + 1) * HD)
        qh, kh, vh, gh = q_ref[:, cols], k_ref[:, cols], v_ref[:, cols], g_ref[:, cols]
        s = lax.dot_general(qh, kh, NT, preferred_element_type=jnp.float32) * SCALE
        s = jnp.where(allowed, s, -1e30)
        p = jnp.exp(s - lse[:, h : h + 1])
        gs = lax.dot_general(gh, vh, NT, preferred_element_type=jnp.float32)
        delta = jnp.sum(p * gs, axis=-1, keepdims=True)
        ds = (p * (gs - delta)).astype(jnp.bfloat16)
        dq = jnp.dot(ds, kh, preferred_element_type=jnp.float32) * SCALE
        dk = lax.dot_general(ds, qh, TN, preferred_element_type=jnp.float32) * SCALE
        dv = lax.dot_general(p.astype(jnp.bfloat16), gh, TN, preferred_element_type=jnp.float32)
        dqs.append(dq.astype(jnp.bfloat16))
        dks.append(dk.astype(jnp.bfloat16))
        dvs.append(dv.astype(jnp.bfloat16))
    dq_ref[...] = jnp.concatenate(dqs, axis=1)
    dk_ref[...] = jnp.concatenate(dks, axis=1)
    dv_ref[...] = jnp.concatenate(dvs, axis=1)


def _mask_specs(seq):
    return [
        pl.BlockSpec((1, seq, 1), lambda r: (r, 0, 0)),
        pl.BlockSpec((1, 1, seq), lambda r: (r, 0, 0)),
        pl.BlockSpec((1, 1, seq), lambda r: (r, 0, 0)),
    ]


def attention_forward(q, k, v, segments, valid_mask):
    rows, seq = segments.shape
    width = q.shape[1]
    heads = width // HD
    tile = pl.BlockSpec((seq, width), lambda r: (r, 0))
    flops = rows * heads * 4 * seq * seq * HD
    return pl.pallas_call(
        _fwd_kernel,
        grid=(rows,),
        in_specs=[tile, tile, tile] + _mask_specs(seq),
        out_specs=[tile, pl.BlockSpec((1, seq, heads), lambda r: (r, 0, 0))],
        out_shape=[
            jax.ShapeDtypeStruct(q.shape, jnp.bfloat16),
            jax.ShapeDtypeStruct((rows, seq, heads), jnp.float32),
        ],
        cost_estimate=pl.CostEstimate(
            flops=flops, transcendentals=rows * heads * seq * seq, bytes_accessed=4 * q.size * 2
        ),
        name="attention_forward",
    )(q, k, v, segments[:, :, None], segments[:, None, :], valid_mask[:, None, :])


def attention_backward(q, k, v, grad_mixed, lse, segments, valid_mask):
    rows, seq = segments.shape
    width = q.shape[1]
    heads = width // HD
    tile = pl.BlockSpec((seq, width), lambda r: (r, 0))
    flops = rows * heads * 10 * seq * seq * HD
    out = jax.ShapeDtypeStruct(q.shape, jnp.bfloat16)
    return pl.pallas_call(
        _bwd_kernel,
        grid=(rows,),
        in_specs=[tile, tile, tile, tile, pl.BlockSpec((1, seq, heads), lambda r: (r, 0, 0))]
        + _mask_specs(seq),
        out_specs=[tile, tile, tile],
        out_shape=[out, out, out],
        cost_estimate=pl.CostEstimate(
            flops=flops, transcendentals=rows * heads * seq * seq, bytes_accessed=7 * q.size * 2
        ),
        name="attention_backward",
    )(q, k, v, grad_mixed, lse, segments[:, :, None], segments[:, None, :], valid_mask[:, None, :])


def gather_pieces(blocks, one):
    n_dp = lax.axis_size("dp")
    d = lax.axis_index("dp")
    pieces = []
    for block in blocks:
        piece_rows = block.shape[0] // n_dp
        pieces.append(lax.dynamic_slice_in_dim(block, d * piece_rows, piece_rows, 0))
    sent = jnp.concatenate([p.astype(jnp.float32) for p in pieces], axis=0) * one
    got = lax.all_gather(sent, ("mp", "dp"), axis=0) * one
    n_mp = lax.axis_size("mp")
    got = got.reshape(n_mp, n_dp, *sent.shape)
    out, at = [], 0
    for p in pieces:
        rows = p.shape[0]
        out.append(got[:, :, at : at + rows])
        at += rows
    return out


def whole_rows(part, dtype):
    n_mp, n_dp, rows, width = part.shape
    return part.astype(dtype).reshape(n_mp * n_dp * rows, width)


def bias_block(vectors, width, n_dp):
    row = jnp.concatenate(vectors)
    row = jnp.pad(row, (0, width - row.shape[0]))
    return jnp.zeros((n_dp, width), jnp.float32).at[0].set(row)


def own_columns(values, width):
    return lax.dynamic_slice_in_dim(values, lax.axis_index("mp") * width, width, 1)


def on_device(
    inputs,
    timesteps,
    segments,
    valid_mask,
    step_table,
    ln1_gain,
    ln1_shift,
    w_query_shard,
    b_query_shard,
    w_key_shard,
    w_value_shard,
    b_value_shard,
    w_out_shard,
    b_out,
    ln2_gain,
    ln2_shift,
    w_up_shard,
    b_up_shard,
    w_down_shard,
    b_down,
    cotangent,
):
    row_count, seq_len, model_width = inputs.shape
    token_count = row_count * seq_len
    qkv_width = w_query_shard.shape[1]
    ff_width = w_up_shard.shape[1]
    one = 1.0 + 0.0 * ln1_gain[0]
    n_dp = lax.axis_size("dp")
    low_type = jnp.bfloat16
    q_part, k_part, v_part, qv_bias = gather_pieces(
        (
            w_query_shard.T,
            w_key_shard.T,
            w_value_shard.T,
            bias_block((b_query_shard, b_value_shard), model_width, n_dp),
        ),
        one,
    )
    w_query_t = whole_rows(q_part, low_type)
    w_key_t = whole_rows(k_part, low_type)
    w_value_t = whole_rows(v_part, low_type)
    b_query = qv_bias[:, 0, 0, :qkv_width].reshape(-1)
    b_value = qv_bias[:, 0, 0, qkv_width : 2 * qkv_width].reshape(-1)
    o_part, up_part, down_part, up_bias = gather_pieces(
        (
            w_out_shard,
            w_up_shard.T,
            w_down_shard,
            bias_block((b_up_shard,), model_width, n_dp),
        ),
        one,
    )
    w_out = whole_rows(o_part, low_type)
    w_up_t = whole_rows(up_part, low_type)
    w_down = whole_rows(down_part, low_type)
    b_up = up_bias[:, 0, 0, :].reshape(-1)
    start = inputs.astype(jnp.float32) + step_table[timesteps].astype(jnp.float32)[:, None, :]
    start = start.reshape(token_count, model_width)
    normed, first_pull = jax.vjp(normalize, start, ln1_gain, ln1_shift)
    normed_low = normed.astype(low_type)
    queries = (over_cols(normed_low, w_query_t) + b_query).astype(low_type)
    key_rows = over_cols(normed_low, w_key_t).astype(low_type)
    value_rows = (over_cols(normed_low, w_value_t) + b_value).astype(low_type)
    mixed, log_total = attention_forward(queries, key_rows, value_rows, segments, valid_mask)
    attended = product(mixed, w_out) + b_out
    middle = start + attended
    normed2, second_pull = jax.vjp(normalize, middle, ln2_gain, ln2_shift)
    normed2_low = normed2.astype(low_type)
    upper = over_cols(normed2_low, w_up_t) + b_up
    activated, gelu_pull = jax.vjp(exact_gelu, upper)
    hidden = activated.astype(low_type)
    lowered = product(hidden, w_down)
    output = (middle + lowered + b_down).astype(low_type).reshape(row_count, seq_len, model_width)
    grad_out = cotangent.reshape(token_count, model_width).astype(jnp.float32)
    grad_out = grad_out * valid_mask.reshape(token_count, 1).astype(jnp.float32)
    grad_out_low = grad_out.astype(low_type)
    grad_out, grad_out_low = lax.optimization_barrier((grad_out, grad_out_low))
    grad_w_down = over_rows(own_columns(hidden, ff_width), grad_out_low)
    grad_b_down = jnp.sum(grad_out, axis=0)
    grad_hidden = over_cols(grad_out_low, w_down)
    (grad_upper,) = gelu_pull(grad_hidden)
    grad_upper_low = grad_upper.astype(low_type)
    own_grad_upper = own_columns(grad_upper_low, ff_width)
    grad_w_up = over_rows(normed2_low, own_grad_upper)
    grad_b_up = column_sum(own_grad_upper)
    ffn_grads = lax.psum(jnp.concatenate([grad_w_down, grad_w_up], axis=0), "dp")
    grad_w_down, grad_w_up = ffn_grads[:ff_width], ffn_grads[ff_width:]
    grad_normed2 = product(grad_upper_low, w_up_t)
    grad_mid_norm, grad_ln2_gain, grad_ln2_shift = second_pull(grad_normed2)
    grad_middle = grad_out + grad_mid_norm
    grad_mid_low = grad_middle.astype(low_type)
    grad_w_out = over_rows(own_columns(mixed, qkv_width), grad_mid_low)
    grad_b_out = column_sum(grad_mid_low)
    grad_mixed = over_cols(grad_mid_low, w_out).astype(low_type)
    grad_queries, grad_keys, grad_values = attention_backward(
        queries, key_rows, value_rows, grad_mixed, log_total, segments, valid_mask
    )
    own_grad_queries = own_columns(grad_queries, qkv_width)
    own_grad_values = own_columns(grad_values, qkv_width)
    grad_w_query = over_rows(normed_low, own_grad_queries)
    grad_b_query = column_sum(own_grad_queries)
    grad_w_key = over_rows(normed_low, own_columns(grad_keys, qkv_width))
    grad_w_value = over_rows(normed_low, own_grad_values)
    grad_b_value = column_sum(own_grad_values)
    grad_normed = (
        product(grad_queries, w_query_t)
        + product(grad_keys, w_key_t)
        + product(grad_values, w_value_t)
    )
    grad_start_norm, grad_ln1_gain, grad_ln1_shift = first_pull(grad_normed)
    grad_start = grad_middle + grad_start_norm
    input_grad = grad_start.astype(low_type).reshape(row_count, seq_len, model_width)
    row_sums = jnp.sum(grad_start.reshape(row_count, seq_len, model_width), axis=1)
    column_count = model_width // lax.axis_size("mp")
    table_columns = own_columns(row_sums, column_count)
    step_count = step_table.shape[0]
    one_hot = (timesteps[:, None] == jnp.arange(step_count, dtype=jnp.int32)[None, :]).astype(
        jnp.float32
    )
    table_grad = lax.dot_general(
        one_hot,
        table_columns,
        CONTRACT_ROWS,
        precision=lax.Precision.HIGHEST,
        preferred_element_type=jnp.float32,
    )
    small = (
        grad_ln1_gain,
        grad_ln1_shift,
        grad_b_query,
        grad_b_value,
        grad_b_out,
        grad_b_down,
        grad_b_up,
        grad_ln2_gain,
        grad_ln2_shift,
    )
    small_rows = jnp.concatenate(small).reshape(-1, column_count)
    packed = jnp.concatenate([table_grad, small_rows], axis=0)
    tie = 0.0 * ffn_grads[0, 0]
    (
        grad_w_query,
        grad_w_key,
        grad_w_value,
        grad_w_out,
        packed,
    ) = lax.psum(
        (
            grad_w_query + tie,
            grad_w_key,
            grad_w_value,
            grad_w_out,
            packed,
        ),
        "dp",
    )
    table_grad = packed[:step_count]
    flat_small = packed[step_count:].reshape(-1)
    unpacked, at = [], 0
    for item in small:
        unpacked.append(flat_small[at : at + item.shape[0]])
        at += item.shape[0]
    (
        grad_ln1_gain,
        grad_ln1_shift,
        grad_b_query,
        grad_b_value,
        grad_b_out,
        grad_b_down,
        grad_b_up,
        grad_ln2_gain,
        grad_ln2_shift,
    ) = unpacked
    return (
        output,
        input_grad,
        grad_ln1_gain,
        grad_ln1_shift,
        grad_w_query,
        grad_b_query,
        grad_w_key,
        grad_w_value,
        grad_b_value,
        grad_w_out,
        grad_b_out,
        grad_ln2_gain,
        grad_ln2_shift,
        grad_w_up,
        grad_b_up,
        grad_w_down,
        grad_b_down,
        table_grad,
    )


def solution(mesh):
    in_specs = (
        P("dp", None, None),
        P("dp"),
        P("dp", None),
        P("dp", None),
        P(),
        P(),
        P(),
        P(None, "mp"),
        P("mp"),
        P(None, "mp"),
        P(None, "mp"),
        P("mp"),
        P("mp", None),
        P(),
        P(),
        P(),
        P(None, "mp"),
        P("mp"),
        P("mp", None),
        P(),
        P("dp", None, None),
    )
    out_specs = (
        P("dp", None, None),
        P("dp", None, None),
        P(),
        P(),
        P(None, "mp"),
        P("mp"),
        P(None, "mp"),
        P(None, "mp"),
        P("mp"),
        P("mp", None),
        P(),
        P(),
        P(),
        P(None, "mp"),
        P("mp"),
        P("mp", None),
        P(),
        P(None, "mp"),
    )

    return jax.shard_map(
        on_device, mesh=mesh, in_specs=in_specs, out_specs=out_specs, check_vma=False
    )
```

```python
import math

import jax
import jax.numpy as jnp
from jax import lax
from jax.sharding import PartitionSpec as P


HD = 64


EPSILON = 1e-05
CONTRACT_ROWS = (((0,), (0,)), ((), ()))
CONTRACT_COLS = (((1,), (1,)), ((), ()))


def normalize(values, gain, shift):
    average = jnp.mean(values, axis=-1, keepdims=True)
    centered = values - average
    variance = jnp.mean(centered * centered, axis=-1, keepdims=True)
    return centered * lax.rsqrt(variance + EPSILON) * gain + shift


def exact_gelu(values):
    return 0.5 * values * (1.0 + lax.erf(values * math.sqrt(0.5)))


def product(left, right):
    return jnp.dot(left, right, preferred_element_type=jnp.float32)


def over_rows(left, right):
    return lax.dot_general(left, right, CONTRACT_ROWS, preferred_element_type=jnp.float32)


def over_cols(left, right):
    return lax.dot_general(left, right, CONTRACT_COLS, preferred_element_type=jnp.float32)


def column_sum(values):
    return jnp.sum(values.astype(jnp.float32), axis=0)


def attention_scores(queries_split, keys_split, allowed):
    scaling = 1.0 / math.sqrt(HD)
    scores = (
        jnp.einsum("rqhe,rkhe->rhqk", queries_split, keys_split, preferred_element_type=jnp.float32)
        * scaling
    )
    return jnp.where(allowed[:, None], scores, -1e30)


def gather_pieces(blocks, one):
    n_dp = lax.axis_size("dp")
    d = lax.axis_index("dp")
    pieces = []
    for block in blocks:
        piece_rows = block.shape[0] // n_dp
        pieces.append(lax.dynamic_slice_in_dim(block, d * piece_rows, piece_rows, 0))
    sent = jnp.concatenate([p.astype(jnp.float32) for p in pieces], axis=0) * one
    got = lax.all_gather(sent, ("mp", "dp"), axis=0) * one
    n_mp = lax.axis_size("mp")
    got = got.reshape(n_mp, n_dp, *sent.shape)
    out, at = [], 0
    for p in pieces:
        rows = p.shape[0]
        out.append(got[:, :, at : at + rows])
        at += rows
    return out


def whole_rows(part, dtype):
    n_mp, n_dp, rows, width = part.shape
    return part.astype(dtype).reshape(n_mp * n_dp * rows, width)


def bias_block(vectors, width, n_dp):
    row = jnp.concatenate(vectors)
    row = jnp.pad(row, (0, width - row.shape[0]))
    return jnp.zeros((n_dp, width), jnp.float32).at[0].set(row)


def own_columns(values, width):
    return lax.dynamic_slice_in_dim(values, lax.axis_index("mp") * width, width, 1)


def on_device(
    inputs,
    timesteps,
    segments,
    valid_mask,
    step_table,
    ln1_gain,
    ln1_shift,
    w_query_shard,
    b_query_shard,
    w_key_shard,
    w_value_shard,
    b_value_shard,
    w_out_shard,
    b_out,
    ln2_gain,
    ln2_shift,
    w_up_shard,
    b_up_shard,
    w_down_shard,
    b_down,
    cotangent,
):
    row_count, seq_len, model_width = inputs.shape
    token_count = row_count * seq_len
    qkv_width = w_query_shard.shape[1]
    ff_width = w_up_shard.shape[1]
    one = 1.0 + 0.0 * ln1_gain[0]
    n_dp = lax.axis_size("dp")
    n_mp = lax.axis_size("mp")
    low_type = jnp.bfloat16
    q_part, k_part, v_part, o_part, qv_bias = gather_pieces(
        (
            w_query_shard.T,
            w_key_shard.T,
            w_value_shard.T,
            w_out_shard,
            bias_block((b_query_shard, b_value_shard), model_width, n_dp),
        ),
        one,
    )
    w_query_t = whole_rows(q_part, low_type)
    w_key_t = whole_rows(k_part, low_type)
    w_value_t = whole_rows(v_part, low_type)
    b_query = qv_bias[:, 0, 0, :qkv_width].reshape(-1)
    b_value = qv_bias[:, 0, 0, qkv_width : 2 * qkv_width].reshape(-1)
    up_part, down_part, up_bias = gather_pieces(
        (
            w_up_shard.T,
            w_down_shard,
            bias_block((b_up_shard,), model_width, n_dp),
        ),
        one,
    )
    w_out = whole_rows(o_part, low_type)
    others = (lax.axis_index("mp") + jnp.arange(1, n_mp, dtype=jnp.int32)) % n_mp
    w_up_others = whole_rows(jnp.take(up_part, others, axis=0), low_type)
    w_down_others = whole_rows(jnp.take(down_part, others, axis=0), low_type)
    b_up_others = jnp.take(up_bias[:, 0, 0, :], others, axis=0).reshape(-1)
    heads = w_query_t.shape[0] // HD
    scaling = 1.0 / math.sqrt(HD)
    head_shape = (row_count, seq_len, heads, HD)
    start = inputs.astype(jnp.float32) + step_table[timesteps].astype(jnp.float32)[:, None, :]
    start = start.reshape(token_count, model_width)
    normed, first_pull = jax.vjp(normalize, start, ln1_gain, ln1_shift)
    normed_low = normed.astype(low_type)
    queries = (over_cols(normed_low, w_query_t) + b_query).astype(low_type)
    key_rows = over_cols(normed_low, w_key_t).astype(low_type)
    value_rows = (over_cols(normed_low, w_value_t) + b_value).astype(low_type)
    queries_split = queries.reshape(head_shape)
    keys_split = key_rows.reshape(head_shape)
    values_split = value_rows.reshape(head_shape)
    places = jnp.arange(seq_len, dtype=jnp.int32)
    diagonal = places[:, None] == places[None, :]
    allowed = (segments[:, :, None] == segments[:, None, :]) & (
        (valid_mask[:, None, :] > 0) | diagonal[None]
    )
    scores = attention_scores(queries_split, keys_split, allowed)
    row_max = jnp.max(scores, axis=-1, keepdims=True)
    powers = jnp.exp(scores - row_max)
    total = jnp.sum(powers, axis=-1, keepdims=True)
    log_total = row_max + jnp.log(total)
    probabilities = powers / total
    mixed = jnp.einsum(
        "rhqk,rkhe->rqhe",
        probabilities.astype(low_type),
        values_split,
        preferred_element_type=jnp.float32,
    )
    mixed = mixed.reshape(token_count, heads * HD).astype(low_type)
    attended = product(mixed, w_out) + b_out
    middle = start + attended
    normed2, second_pull = jax.vjp(normalize, middle, ln2_gain, ln2_shift)
    normed2_low = normed2.astype(low_type)
    upper_own = product(normed2_low, w_up_shard) + b_up_shard
    activated_own, gelu_pull_own = jax.vjp(exact_gelu, upper_own)
    hidden_own = activated_own.astype(low_type)
    lowered_own = product(hidden_own, w_down_shard)
    grad_out = cotangent.reshape(token_count, model_width).astype(jnp.float32)
    grad_out = grad_out * valid_mask.reshape(token_count, 1).astype(jnp.float32)
    grad_out_low = grad_out.astype(low_type)
    grad_out, grad_out_low = lax.optimization_barrier((grad_out, grad_out_low))
    grad_w_down = over_rows(hidden_own, grad_out_low)
    grad_b_down = jnp.sum(grad_out, axis=0)
    (grad_upper_own,) = gelu_pull_own(over_cols(grad_out_low, w_down_shard))
    grad_upper_own = grad_upper_own.astype(low_type)
    grad_w_up = over_rows(normed2_low, grad_upper_own)
    grad_b_up = column_sum(grad_upper_own)
    ffn_grads = lax.psum(jnp.concatenate([grad_w_down, grad_w_up], axis=0), "dp")
    grad_w_down, grad_w_up = ffn_grads[:ff_width], ffn_grads[ff_width:]
    grad_normed2_own = over_cols(grad_upper_own, w_up_shard)
    upper = over_cols(normed2_low, w_up_others) + b_up_others
    activated, gelu_pull = jax.vjp(exact_gelu, upper)
    hidden = activated.astype(low_type)
    lowered = lowered_own + product(hidden, w_down_others)
    output = (middle + lowered + b_down).astype(low_type).reshape(row_count, seq_len, model_width)
    (grad_upper,) = gelu_pull(over_cols(grad_out_low, w_down_others))
    grad_upper_low = grad_upper.astype(low_type)
    grad_normed2 = grad_normed2_own + product(grad_upper_low, w_up_others)
    grad_mid_norm, grad_ln2_gain, grad_ln2_shift = second_pull(grad_normed2)
    grad_middle = grad_out + grad_mid_norm
    grad_mid_low = grad_middle.astype(low_type)
    grad_w_out = over_rows(own_columns(mixed, qkv_width), grad_mid_low)
    grad_b_out = column_sum(grad_mid_low)
    grad_mixed = over_cols(grad_mid_low, w_out).astype(low_type).reshape(head_shape)
    scores_again = attention_scores(queries_split, keys_split, allowed)
    soft_again = jnp.exp(scores_again - log_total)
    grad_soft = jnp.einsum(
        "rqhe,rkhe->rhqk", grad_mixed, values_split, preferred_element_type=jnp.float32
    )
    delta = jnp.sum(soft_again * grad_soft, axis=-1, keepdims=True)
    grad_scores = (soft_again * (grad_soft - delta)).astype(low_type)
    grad_queries = jnp.einsum(
        "rhqk,rkhe->rqhe", grad_scores, keys_split, preferred_element_type=jnp.float32
    )
    grad_queries = (grad_queries * scaling).reshape(token_count, heads * HD).astype(low_type)
    grad_keys = jnp.einsum(
        "rhqk,rqhe->rkhe", grad_scores, queries_split, preferred_element_type=jnp.float32
    )
    grad_keys = (grad_keys * scaling).reshape(token_count, heads * HD).astype(low_type)
    grad_values = jnp.einsum(
        "rhqk,rqhe->rkhe",
        soft_again.astype(low_type),
        grad_mixed,
        preferred_element_type=jnp.float32,
    )
    grad_values = grad_values.reshape(token_count, heads * HD).astype(low_type)
    own_grad_queries = own_columns(grad_queries, qkv_width)
    own_grad_values = own_columns(grad_values, qkv_width)
    grad_w_query = over_rows(normed_low, own_grad_queries)
    grad_b_query = column_sum(own_grad_queries)
    grad_w_key = over_rows(normed_low, own_columns(grad_keys, qkv_width))
    grad_w_value = over_rows(normed_low, own_grad_values)
    grad_b_value = column_sum(own_grad_values)
    grad_normed = (
        product(grad_queries, w_query_t)
        + product(grad_keys, w_key_t)
        + product(grad_values, w_value_t)
    )
    grad_start_norm, grad_ln1_gain, grad_ln1_shift = first_pull(grad_normed)
    grad_start = grad_middle + grad_start_norm
    input_grad = grad_start.astype(low_type).reshape(row_count, seq_len, model_width)
    row_sums = jnp.sum(grad_start.reshape(row_count, seq_len, model_width), axis=1)
    column_count = model_width // lax.axis_size("mp")
    table_columns = own_columns(row_sums, column_count)
    step_count = step_table.shape[0]
    one_hot = (timesteps[:, None] == jnp.arange(step_count, dtype=jnp.int32)[None, :]).astype(
        jnp.float32
    )
    table_grad = lax.dot_general(
        one_hot,
        table_columns,
        CONTRACT_ROWS,
        precision=lax.Precision.HIGHEST,
        preferred_element_type=jnp.float32,
    )
    small = (
        grad_ln1_gain,
        grad_ln1_shift,
        grad_b_query,
        grad_b_value,
        grad_b_out,
        grad_b_down,
        grad_b_up,
        grad_ln2_gain,
        grad_ln2_shift,
    )
    small_rows = jnp.concatenate(small).reshape(-1, column_count)
    packed = jnp.concatenate([table_grad, small_rows], axis=0)
    tie = 0.0 * ffn_grads[0, 0]
    (
        grad_w_query,
        grad_w_key,
        grad_w_value,
        grad_w_out,
        packed,
    ) = lax.psum(
        (
            grad_w_query + tie,
            grad_w_key,
            grad_w_value,
            grad_w_out,
            packed,
        ),
        "dp",
    )
    table_grad = packed[:step_count]
    flat_small = packed[step_count:].reshape(-1)
    unpacked, at = [], 0
    for item in small:
        unpacked.append(flat_small[at : at + item.shape[0]])
        at += item.shape[0]
    (
        grad_ln1_gain,
        grad_ln1_shift,
        grad_b_query,
        grad_b_value,
        grad_b_out,
        grad_b_down,
        grad_b_up,
        grad_ln2_gain,
        grad_ln2_shift,
    ) = unpacked
    return (
        output,
        input_grad,
        grad_ln1_gain,
        grad_ln1_shift,
        grad_w_query,
        grad_b_query,
        grad_w_key,
        grad_w_value,
        grad_b_value,
        grad_w_out,
        grad_b_out,
        grad_ln2_gain,
        grad_ln2_shift,
        grad_w_up,
        grad_b_up,
        grad_w_down,
        grad_b_down,
        table_grad,
    )


def solution(mesh):
    in_specs = (
        P("dp", None, None),
        P("dp"),
        P("dp", None),
        P("dp", None),
        P(),
        P(),
        P(),
        P(None, "mp"),
        P("mp"),
        P(None, "mp"),
        P(None, "mp"),
        P("mp"),
        P("mp", None),
        P(),
        P(),
        P(),
        P(None, "mp"),
        P("mp"),
        P("mp", None),
        P(),
        P("dp", None, None),
    )
    out_specs = (
        P("dp", None, None),
        P("dp", None, None),
        P(),
        P(),
        P(None, "mp"),
        P("mp"),
        P(None, "mp"),
        P(None, "mp"),
        P("mp"),
        P("mp", None),
        P(),
        P(),
        P(),
        P(None, "mp"),
        P("mp"),
        P("mp", None),
        P(),
        P(None, "mp"),
    )

    return jax.shard_map(
        on_device, mesh=mesh, in_specs=in_specs, out_specs=out_specs, check_vma=False
    )
```

```python
import math

import jax
import jax.numpy as jnp
from jax import lax
from jax.sharding import PartitionSpec as P


HD = 64


EPSILON = 1e-05
CONTRACT_ROWS = (((0,), (0,)), ((), ()))
CONTRACT_COLS = (((1,), (1,)), ((), ()))


def normalize(values, gain, shift):
    average = jnp.mean(values, axis=-1, keepdims=True)
    centered = values - average
    variance = jnp.mean(centered * centered, axis=-1, keepdims=True)
    return centered * lax.rsqrt(variance + EPSILON) * gain + shift


def exact_gelu(values):
    return 0.5 * values * (1.0 + lax.erf(values * math.sqrt(0.5)))


def product(left, right):
    return jnp.dot(left, right, preferred_element_type=jnp.float32)


def over_rows(left, right):
    return lax.dot_general(left, right, CONTRACT_ROWS, preferred_element_type=jnp.float32)


def over_cols(left, right):
    return lax.dot_general(left, right, CONTRACT_COLS, preferred_element_type=jnp.float32)


def column_sum(values):
    return jnp.sum(values.astype(jnp.float32), axis=0)


def attention_scores(queries_split, keys_split, allowed):
    scaling = 1.0 / math.sqrt(HD)
    scores = (
        jnp.einsum("rqhe,rkhe->rhqk", queries_split, keys_split, preferred_element_type=jnp.float32)
        * scaling
    )
    return jnp.where(allowed[:, None], scores, -1e30)


def gather_pieces(blocks, one):
    n_dp = lax.axis_size("dp")
    d = lax.axis_index("dp")
    pieces = []
    for block in blocks:
        piece_rows = block.shape[0] // n_dp
        pieces.append(lax.dynamic_slice_in_dim(block, d * piece_rows, piece_rows, 0))
    sent = jnp.concatenate([p.astype(jnp.float32) for p in pieces], axis=0) * one
    got = lax.all_gather(sent, ("mp", "dp"), axis=0)
    n_mp = lax.axis_size("mp")
    got = got.reshape(n_mp, n_dp, *sent.shape)
    out, at = [], 0
    for p in pieces:
        rows = p.shape[0]
        out.append(got[:, :, at : at + rows])
        at += rows
    return out


def whole_rows(part, one, dtype):
    n_mp, n_dp, rows, width = part.shape
    return (part * one).astype(dtype).reshape(n_mp * n_dp * rows, width)


def other_rows(part, one, dtype):
    n_mp, n_dp, rows, width = part.shape
    me = lax.axis_index("mp")
    blocks = [
        lax.dynamic_index_in_dim(part, (me + step) % n_mp, 0, keepdims=False)
        for step in range(1, n_mp)
    ]
    return (jnp.stack(blocks) * one).astype(dtype).reshape((n_mp - 1) * n_dp * rows, width)


def bias_block(vectors, width, n_dp):
    row = jnp.concatenate(vectors)
    row = jnp.pad(row, (0, width - row.shape[0]))
    return jnp.zeros((n_dp, width), jnp.float32).at[0].set(row)


def own_columns(values, width):
    return lax.dynamic_slice_in_dim(values, lax.axis_index("mp") * width, width, 1)


def on_device(
    inputs,
    timesteps,
    segments,
    valid_mask,
    step_table,
    ln1_gain,
    ln1_shift,
    w_query_shard,
    b_query_shard,
    w_key_shard,
    w_value_shard,
    b_value_shard,
    w_out_shard,
    b_out,
    ln2_gain,
    ln2_shift,
    w_up_shard,
    b_up_shard,
    w_down_shard,
    b_down,
    cotangent,
):
    row_count, seq_len, model_width = inputs.shape
    token_count = row_count * seq_len
    qkv_width = w_query_shard.shape[1]
    ff_width = w_up_shard.shape[1]
    one = 1.0 + 0.0 * ln1_gain[0]
    n_dp = lax.axis_size("dp")
    low_type = jnp.bfloat16
    q_part, k_part, v_part, o_part, qv_bias = gather_pieces(
        (
            w_query_shard.T,
            w_key_shard.T,
            w_value_shard.T,
            w_out_shard,
            bias_block((b_query_shard, b_value_shard), model_width, n_dp),
        ),
        one,
    )
    w_query_t = whole_rows(q_part, one, low_type)
    w_key_t = whole_rows(k_part, one, low_type)
    w_value_t = whole_rows(v_part, one, low_type)
    b_query = (qv_bias[:, 0, 0, :qkv_width] * one).reshape(-1)
    b_value = (qv_bias[:, 0, 0, qkv_width : 2 * qkv_width] * one).reshape(-1)
    up_part, down_part, up_bias = gather_pieces(
        (
            w_up_shard.T,
            w_down_shard,
            bias_block((b_up_shard,), model_width, n_dp),
        ),
        one,
    )
    w_out = whole_rows(o_part, one, low_type)
    w_up_others = other_rows(up_part, one, low_type)
    w_down_others = other_rows(down_part, one, low_type)
    b_up_others = other_rows(up_bias[:, :1, :1, :], one, jnp.float32).reshape(-1)
    heads = w_query_t.shape[0] // HD
    scaling = 1.0 / math.sqrt(HD)
    head_shape = (row_count, seq_len, heads, HD)
    start = inputs.astype(jnp.float32) + step_table[timesteps].astype(jnp.float32)[:, None, :]
    start = start.reshape(token_count, model_width)
    normed, first_pull = jax.vjp(normalize, start, ln1_gain, ln1_shift)
    normed_low = normed.astype(low_type)
    queries = (over_cols(normed_low, w_query_t) + b_query).astype(low_type)
    key_rows = over_cols(normed_low, w_key_t).astype(low_type)
    value_rows = (over_cols(normed_low, w_value_t) + b_value).astype(low_type)
    queries_split = queries.reshape(head_shape)
    keys_split = key_rows.reshape(head_shape)
    values_split = value_rows.reshape(head_shape)
    places = jnp.arange(seq_len, dtype=jnp.int32)
    diagonal = places[:, None] == places[None, :]
    allowed = (segments[:, :, None] == segments[:, None, :]) & (
        (valid_mask[:, None, :] > 0) | diagonal[None]
    )
    scores = attention_scores(queries_split, keys_split, allowed)
    row_max = jnp.max(scores, axis=-1, keepdims=True)
    powers = jnp.exp(scores - row_max)
    total = jnp.sum(powers, axis=-1, keepdims=True)
    log_total = row_max + jnp.log(total)
    probabilities = powers / total
    mixed = jnp.einsum(
        "rhqk,rkhe->rqhe",
        probabilities.astype(low_type),
        values_split,
        preferred_element_type=jnp.float32,
    )
    mixed = mixed.reshape(token_count, heads * HD).astype(low_type)
    attended = product(mixed, w_out) + b_out
    middle = start + attended
    normed2, second_pull = jax.vjp(normalize, middle, ln2_gain, ln2_shift)
    normed2_low = normed2.astype(low_type)
    upper_own = product(normed2_low, w_up_shard) + b_up_shard
    activated_own, gelu_pull_own = jax.vjp(exact_gelu, upper_own)
    hidden_own = activated_own.astype(low_type)
    lowered_own = product(hidden_own, w_down_shard)
    grad_out = cotangent.reshape(token_count, model_width).astype(jnp.float32)
    grad_out = grad_out * valid_mask.reshape(token_count, 1).astype(jnp.float32)
    grad_out_low = grad_out.astype(low_type)
    grad_out, grad_out_low = lax.optimization_barrier((grad_out, grad_out_low))
    grad_w_down = over_rows(hidden_own, grad_out_low)
    grad_b_down = jnp.sum(grad_out, axis=0)
    (grad_upper_own,) = gelu_pull_own(over_cols(grad_out_low, w_down_shard))
    grad_upper_own = grad_upper_own.astype(low_type)
    grad_w_up = over_rows(normed2_low, grad_upper_own)
    grad_b_up = column_sum(grad_upper_own)
    ffn_grads = lax.psum(jnp.concatenate([grad_w_down, grad_w_up], axis=0), "dp")
    grad_w_down, grad_w_up = ffn_grads[:ff_width], ffn_grads[ff_width:]
    grad_normed2_own = over_cols(grad_upper_own, w_up_shard)
    upper = over_cols(normed2_low, w_up_others) + b_up_others
    activated, gelu_pull = jax.vjp(exact_gelu, upper)
    hidden = lax.optimization_barrier(activated.astype(low_type))
    lowered = lowered_own + product(hidden, w_down_others)
    output = (middle + lowered + b_down).astype(low_type)
    output = output.reshape(row_count, seq_len, model_width)
    (grad_upper,) = gelu_pull(over_cols(grad_out_low, w_down_others))
    grad_upper_low = lax.optimization_barrier(grad_upper.astype(low_type))
    grad_normed2 = grad_normed2_own + product(grad_upper_low, w_up_others)
    grad_mid_norm, grad_ln2_gain, grad_ln2_shift = second_pull(grad_normed2)
    grad_middle = grad_out + grad_mid_norm
    grad_mid_low = grad_middle.astype(low_type)
    grad_w_out = over_rows(own_columns(mixed, qkv_width), grad_mid_low)
    grad_b_out = column_sum(grad_mid_low)
    grad_mixed = over_cols(grad_mid_low, w_out).astype(low_type).reshape(head_shape)
    scores_again = attention_scores(queries_split, keys_split, allowed)
    soft_again = jnp.exp(scores_again - log_total)
    grad_soft = jnp.einsum(
        "rqhe,rkhe->rhqk", grad_mixed, values_split, preferred_element_type=jnp.float32
    )
    delta = jnp.sum(soft_again * grad_soft, axis=-1, keepdims=True)
    grad_scores = (soft_again * (grad_soft - delta)).astype(low_type)
    grad_queries = jnp.einsum(
        "rhqk,rkhe->rqhe", grad_scores, keys_split, preferred_element_type=jnp.float32
    )
    grad_queries = (grad_queries * scaling).reshape(token_count, heads * HD).astype(low_type)
    grad_keys = jnp.einsum(
        "rhqk,rqhe->rkhe", grad_scores, queries_split, preferred_element_type=jnp.float32
    )
    grad_keys = (grad_keys * scaling).reshape(token_count, heads * HD).astype(low_type)
    grad_values = jnp.einsum(
        "rhqk,rqhe->rkhe",
        soft_again.astype(low_type),
        grad_mixed,
        preferred_element_type=jnp.float32,
    )
    grad_values = grad_values.reshape(token_count, heads * HD).astype(low_type)
    own_grad_queries = own_columns(grad_queries, qkv_width)
    own_grad_values = own_columns(grad_values, qkv_width)
    grad_w_query = over_rows(normed_low, own_grad_queries)
    grad_b_query = column_sum(own_grad_queries)
    grad_w_key = over_rows(normed_low, own_columns(grad_keys, qkv_width))
    grad_w_value = over_rows(normed_low, own_grad_values)
    grad_b_value = column_sum(own_grad_values)
    grad_normed = (
        product(grad_queries, w_query_t)
        + product(grad_keys, w_key_t)
        + product(grad_values, w_value_t)
    )
    grad_start_norm, grad_ln1_gain, grad_ln1_shift = first_pull(grad_normed)
    grad_start = grad_middle + grad_start_norm
    input_grad = grad_start.astype(low_type).reshape(row_count, seq_len, model_width)
    row_sums = jnp.sum(grad_start.reshape(row_count, seq_len, model_width), axis=1)
    column_count = model_width // lax.axis_size("mp")
    table_columns = own_columns(row_sums, column_count)
    step_count = step_table.shape[0]
    one_hot = (timesteps[:, None] == jnp.arange(step_count, dtype=jnp.int32)[None, :]).astype(
        jnp.float32
    )
    table_grad = lax.dot_general(
        one_hot,
        table_columns,
        CONTRACT_ROWS,
        precision=lax.Precision.HIGHEST,
        preferred_element_type=jnp.float32,
    )
    small = (
        grad_ln1_gain,
        grad_ln1_shift,
        grad_b_query,
        grad_b_value,
        grad_b_out,
        grad_b_down,
        grad_b_up,
        grad_ln2_gain,
        grad_ln2_shift,
    )
    small_rows = jnp.concatenate(small).reshape(-1, column_count)
    packed = jnp.concatenate([table_grad, small_rows], axis=0)
    tie = 0.0 * ffn_grads[0, 0]
    (
        grad_w_query,
        grad_w_key,
        grad_w_value,
        grad_w_out,
        packed,
    ) = lax.psum(
        (
            grad_w_query + tie,
            grad_w_key,
            grad_w_value,
            grad_w_out,
            packed,
        ),
        "dp",
    )
    table_grad = packed[:step_count]
    flat_small = packed[step_count:].reshape(-1)
    unpacked, at = [], 0
    for item in small:
        unpacked.append(flat_small[at : at + item.shape[0]])
        at += item.shape[0]
    (
        grad_ln1_gain,
        grad_ln1_shift,
        grad_b_query,
        grad_b_value,
        grad_b_out,
        grad_b_down,
        grad_b_up,
        grad_ln2_gain,
        grad_ln2_shift,
    ) = unpacked
    return (
        output,
        input_grad,
        grad_ln1_gain,
        grad_ln1_shift,
        grad_w_query,
        grad_b_query,
        grad_w_key,
        grad_w_value,
        grad_b_value,
        grad_w_out,
        grad_b_out,
        grad_ln2_gain,
        grad_ln2_shift,
        grad_w_up,
        grad_b_up,
        grad_w_down,
        grad_b_down,
        table_grad,
    )


def solution(mesh):
    in_specs = (
        P("dp", None, None),
        P("dp"),
        P("dp", None),
        P("dp", None),
        P(),
        P(),
        P(),
        P(None, "mp"),
        P("mp"),
        P(None, "mp"),
        P(None, "mp"),
        P("mp"),
        P("mp", None),
        P(),
        P(),
        P(),
        P(None, "mp"),
        P("mp"),
        P("mp", None),
        P(),
        P("dp", None, None),
    )
    out_specs = (
        P("dp", None, None),
        P("dp", None, None),
        P(),
        P(),
        P(None, "mp"),
        P("mp"),
        P(None, "mp"),
        P(None, "mp"),
        P("mp"),
        P("mp", None),
        P(),
        P(),
        P(),
        P(None, "mp"),
        P("mp"),
        P("mp", None),
        P(),
        P(None, "mp"),
    )

    return jax.shard_map(
        on_device, mesh=mesh, in_specs=in_specs, out_specs=out_specs, check_vma=False
    )
```

```python
import math

import jax
import jax.numpy as jnp
from jax import lax
from jax.sharding import PartitionSpec as P


HD = 64


EPSILON = 1e-05
CONTRACT_ROWS = (((0,), (0,)), ((), ()))
CONTRACT_COLS = (((1,), (1,)), ((), ()))


def normalize(values, gain, shift):
    average = jnp.mean(values, axis=-1, keepdims=True)
    centered = values - average
    variance = jnp.mean(centered * centered, axis=-1, keepdims=True)
    return centered * lax.rsqrt(variance + EPSILON) * gain + shift


def exact_gelu(values):
    return 0.5 * values * (1.0 + lax.erf(values * math.sqrt(0.5)))


def product(left, right):
    return jnp.dot(left, right, preferred_element_type=jnp.float32)


def over_rows(left, right):
    return lax.dot_general(left, right, CONTRACT_ROWS, preferred_element_type=jnp.float32)


def over_cols(left, right):
    return lax.dot_general(left, right, CONTRACT_COLS, preferred_element_type=jnp.float32)


def column_sum(values):
    return jnp.sum(values.astype(jnp.float32), axis=0)


def attention_scores(queries_split, keys_split, allowed):
    scaling = 1.0 / math.sqrt(HD)
    scores = (
        jnp.einsum("rqhe,rkhe->rhqk", queries_split, keys_split, preferred_element_type=jnp.float32)
        * scaling
    )
    return jnp.where(allowed[:, None], scores, -1e30)


def gather_pieces(blocks, one):
    n_dp = lax.axis_size("dp")
    d = lax.axis_index("dp")
    pieces = []
    for block in blocks:
        piece_rows = block.shape[0] // n_dp
        pieces.append(lax.dynamic_slice_in_dim(block, d * piece_rows, piece_rows, 0))
    sent = jnp.concatenate([p.astype(jnp.float32) for p in pieces], axis=0) * one
    got = lax.all_gather(sent, ("mp", "dp"), axis=0)
    n_mp = lax.axis_size("mp")
    got = got.reshape(n_mp, n_dp, *sent.shape)
    out, at = [], 0
    for p in pieces:
        rows = p.shape[0]
        out.append(got[:, :, at : at + rows])
        at += rows
    return out


def whole_rows(part, one, dtype):
    n_mp, n_dp, rows, width = part.shape
    return (part * one).astype(dtype).reshape(n_mp * n_dp * rows, width)


def other_rows(part, one, dtype):
    n_mp, n_dp, rows, width = part.shape
    me = lax.axis_index("mp")
    blocks = [
        lax.dynamic_index_in_dim(part, (me + step) % n_mp, 0, keepdims=False)
        for step in range(1, n_mp)
    ]
    return (jnp.stack(blocks) * one).astype(dtype).reshape((n_mp - 1) * n_dp * rows, width)


def bias_block(vectors, width, n_dp):
    row = jnp.concatenate(vectors)
    row = jnp.pad(row, (0, width - row.shape[0]))
    return jnp.zeros((n_dp, width), jnp.float32).at[0].set(row)


def own_columns(values, width):
    return lax.dynamic_slice_in_dim(values, lax.axis_index("mp") * width, width, 1)


def on_device(
    inputs,
    timesteps,
    segments,
    valid_mask,
    step_table,
    ln1_gain,
    ln1_shift,
    w_query_shard,
    b_query_shard,
    w_key_shard,
    w_value_shard,
    b_value_shard,
    w_out_shard,
    b_out,
    ln2_gain,
    ln2_shift,
    w_up_shard,
    b_up_shard,
    w_down_shard,
    b_down,
    cotangent,
):
    row_count, seq_len, model_width = inputs.shape
    token_count = row_count * seq_len
    qkv_width = w_query_shard.shape[1]
    ff_width = w_up_shard.shape[1]
    one = 1.0 + 0.0 * ln1_gain[0]
    n_dp = lax.axis_size("dp")
    low_type = jnp.bfloat16
    q_part, k_part, v_part, o_part, qv_bias = gather_pieces(
        (
            w_query_shard.T,
            w_key_shard.T,
            w_value_shard.T,
            w_out_shard,
            bias_block((b_query_shard, b_value_shard), model_width, n_dp),
        ),
        one,
    )
    w_query_t = whole_rows(q_part, one, low_type)
    w_key_t = whole_rows(k_part, one, low_type)
    w_value_t = whole_rows(v_part, one, low_type)
    b_query = (qv_bias[:, 0, 0, :qkv_width] * one).reshape(-1)
    b_value = (qv_bias[:, 0, 0, qkv_width : 2 * qkv_width] * one).reshape(-1)
    up_part, down_part, up_bias = gather_pieces(
        (
            w_up_shard.T,
            w_down_shard,
            bias_block((b_up_shard,), model_width, n_dp),
        ),
        one,
    )
    w_out = whole_rows(o_part, one, low_type)
    w_up_others = other_rows(up_part, one, low_type)
    w_down_others = other_rows(down_part, one, low_type)
    b_up_others = other_rows(up_bias[:, :1, :1, :], one, jnp.float32).reshape(-1)
    heads = w_query_t.shape[0] // HD
    scaling = 1.0 / math.sqrt(HD)
    head_shape = (row_count, seq_len, heads, HD)
    start = inputs.astype(jnp.float32) + step_table[timesteps].astype(jnp.float32)[:, None, :]
    start = start.reshape(token_count, model_width)
    normed, first_pull = jax.vjp(normalize, start, ln1_gain, ln1_shift)
    normed_low = normed.astype(low_type)
    queries = (over_cols(normed_low, w_query_t) + b_query).astype(low_type)
    key_rows = over_cols(normed_low, w_key_t).astype(low_type)
    value_rows = (over_cols(normed_low, w_value_t) + b_value).astype(low_type)
    queries_split = queries.reshape(head_shape)
    keys_split = key_rows.reshape(head_shape)
    values_split = value_rows.reshape(head_shape)
    places = jnp.arange(seq_len, dtype=jnp.int32)
    diagonal = places[:, None] == places[None, :]
    allowed = (segments[:, :, None] == segments[:, None, :]) & (
        (valid_mask[:, None, :] > 0) | diagonal[None]
    )
    scores = attention_scores(queries_split, keys_split, allowed)
    row_max = jnp.max(scores, axis=-1, keepdims=True)
    powers = jnp.exp(scores - row_max)
    total = jnp.sum(powers, axis=-1, keepdims=True)
    log_total = row_max + jnp.log(total)
    probabilities = powers / total
    probabilities_low = probabilities.astype(low_type)
    mixed = jnp.einsum(
        "rhqk,rkhe->rqhe",
        probabilities_low,
        values_split,
        preferred_element_type=jnp.float32,
    )
    mixed = mixed.reshape(token_count, heads * HD).astype(low_type)
    attended = product(mixed, w_out) + b_out
    middle = start + attended
    normed2, second_pull = jax.vjp(normalize, middle, ln2_gain, ln2_shift)
    normed2_low = normed2.astype(low_type)
    upper_own = product(normed2_low, w_up_shard) + b_up_shard
    activated_own, gelu_pull_own = jax.vjp(exact_gelu, upper_own)
    hidden_own = activated_own.astype(low_type)
    lowered_own = product(hidden_own, w_down_shard)
    grad_out = cotangent.reshape(token_count, model_width).astype(jnp.float32)
    grad_out = grad_out * valid_mask.reshape(token_count, 1).astype(jnp.float32)
    grad_out_low = grad_out.astype(low_type)
    grad_out, grad_out_low = lax.optimization_barrier((grad_out, grad_out_low))
    grad_w_down = over_rows(hidden_own, grad_out_low)
    grad_b_down = jnp.sum(grad_out, axis=0)
    (grad_upper_own,) = gelu_pull_own(over_cols(grad_out_low, w_down_shard))
    grad_upper_own = grad_upper_own.astype(low_type)
    grad_w_up = over_rows(normed2_low, grad_upper_own)
    grad_b_up = column_sum(grad_upper_own)
    ffn_grads = lax.psum(jnp.concatenate([grad_w_down, grad_w_up], axis=0), "dp")
    grad_w_down, grad_w_up = ffn_grads[:ff_width], ffn_grads[ff_width:]
    grad_normed2_own = over_cols(grad_upper_own, w_up_shard)
    upper = over_cols(normed2_low, w_up_others) + b_up_others
    activated, gelu_pull = jax.vjp(exact_gelu, upper)
    hidden = lax.optimization_barrier(activated.astype(low_type))
    lowered = lowered_own + product(hidden, w_down_others)
    output = (middle + lowered + b_down).astype(low_type)
    output = output.reshape(row_count, seq_len, model_width)
    (grad_upper,) = gelu_pull(over_cols(grad_out_low, w_down_others))
    grad_upper_low = lax.optimization_barrier(grad_upper.astype(low_type))
    grad_normed2 = grad_normed2_own + product(grad_upper_low, w_up_others)
    grad_mid_norm, grad_ln2_gain, grad_ln2_shift = second_pull(grad_normed2)
    grad_middle = grad_out + grad_mid_norm
    grad_mid_low = grad_middle.astype(low_type)
    grad_w_out = over_rows(own_columns(mixed, qkv_width), grad_mid_low)
    grad_b_out = column_sum(grad_mid_low)
    grad_mixed = over_cols(grad_mid_low, w_out).astype(low_type).reshape(head_shape)
    soft_again = probabilities
    grad_soft = jnp.einsum(
        "rqhe,rkhe->rhqk", grad_mixed, values_split, preferred_element_type=jnp.float32
    )
    delta = jnp.sum(soft_again * grad_soft, axis=-1, keepdims=True)
    grad_scores = (soft_again * (grad_soft - delta)).astype(low_type)
    grad_queries = jnp.einsum(
        "rhqk,rkhe->rqhe", grad_scores, keys_split, preferred_element_type=jnp.float32
    )
    grad_queries = (grad_queries * scaling).reshape(token_count, heads * HD).astype(low_type)
    grad_keys = jnp.einsum(
        "rhqk,rqhe->rkhe", grad_scores, queries_split, preferred_element_type=jnp.float32
    )
    grad_keys = (grad_keys * scaling).reshape(token_count, heads * HD).astype(low_type)
    grad_values = jnp.einsum(
        "rhqk,rqhe->rkhe",
        probabilities_low,
        grad_mixed,
        preferred_element_type=jnp.float32,
    )
    grad_values = grad_values.reshape(token_count, heads * HD).astype(low_type)
    own_grad_queries = own_columns(grad_queries, qkv_width)
    own_grad_values = own_columns(grad_values, qkv_width)
    grad_w_query = over_rows(normed_low, own_grad_queries)
    grad_b_query = column_sum(own_grad_queries)
    grad_w_key = over_rows(normed_low, own_columns(grad_keys, qkv_width))
    grad_w_value = over_rows(normed_low, own_grad_values)
    grad_b_value = column_sum(own_grad_values)
    grad_normed = (
        product(grad_queries, w_query_t)
        + product(grad_keys, w_key_t)
        + product(grad_values, w_value_t)
    )
    grad_start_norm, grad_ln1_gain, grad_ln1_shift = first_pull(grad_normed)
    grad_start = grad_middle + grad_start_norm
    input_grad = grad_start.astype(low_type).reshape(row_count, seq_len, model_width)
    row_sums = jnp.sum(grad_start.reshape(row_count, seq_len, model_width), axis=1)
    column_count = model_width // lax.axis_size("mp")
    table_columns = own_columns(row_sums, column_count)
    step_count = step_table.shape[0]
    one_hot = (timesteps[:, None] == jnp.arange(step_count, dtype=jnp.int32)[None, :]).astype(
        jnp.float32
    )
    table_grad = lax.dot_general(
        one_hot,
        table_columns,
        CONTRACT_ROWS,
        precision=lax.Precision.HIGHEST,
        preferred_element_type=jnp.float32,
    )
    small = (
        grad_ln1_gain,
        grad_ln1_shift,
        grad_b_query,
        grad_b_value,
        grad_b_out,
        grad_b_down,
        grad_b_up,
        grad_ln2_gain,
        grad_ln2_shift,
    )
    small_rows = jnp.concatenate(small).reshape(-1, column_count)
    packed = jnp.concatenate([table_grad, small_rows], axis=0)
    tie = 0.0 * ffn_grads[0, 0]
    (
        grad_w_query,
        grad_w_key,
        grad_w_value,
        grad_w_out,
        packed,
    ) = lax.psum(
        (
            grad_w_query + tie,
            grad_w_key,
            grad_w_value,
            grad_w_out,
            packed,
        ),
        "dp",
    )
    table_grad = packed[:step_count]
    flat_small = packed[step_count:].reshape(-1)
    unpacked, at = [], 0
    for item in small:
        unpacked.append(flat_small[at : at + item.shape[0]])
        at += item.shape[0]
    (
        grad_ln1_gain,
        grad_ln1_shift,
        grad_b_query,
        grad_b_value,
        grad_b_out,
        grad_b_down,
        grad_b_up,
        grad_ln2_gain,
        grad_ln2_shift,
    ) = unpacked
    return (
        output,
        input_grad,
        grad_ln1_gain,
        grad_ln1_shift,
        grad_w_query,
        grad_b_query,
        grad_w_key,
        grad_w_value,
        grad_b_value,
        grad_w_out,
        grad_b_out,
        grad_ln2_gain,
        grad_ln2_shift,
        grad_w_up,
        grad_b_up,
        grad_w_down,
        grad_b_down,
        table_grad,
    )


def solution(mesh):
    in_specs = (
        P("dp", None, None),
        P("dp"),
        P("dp", None),
        P("dp", None),
        P(),
        P(),
        P(),
        P(None, "mp"),
        P("mp"),
        P(None, "mp"),
        P(None, "mp"),
        P("mp"),
        P("mp", None),
        P(),
        P(),
        P(),
        P(None, "mp"),
        P("mp"),
        P("mp", None),
        P(),
        P("dp", None, None),
    )
    out_specs = (
        P("dp", None, None),
        P("dp", None, None),
        P(),
        P(),
        P(None, "mp"),
        P("mp"),
        P(None, "mp"),
        P(None, "mp"),
        P("mp"),
        P("mp", None),
        P(),
        P(),
        P(),
        P(None, "mp"),
        P("mp"),
        P("mp", None),
        P(),
        P(None, "mp"),
    )

    return jax.shard_map(
        on_device, mesh=mesh, in_specs=in_specs, out_specs=out_specs, check_vma=False
    )
```

```python
import math

import jax
import jax.numpy as jnp
from jax import lax
from jax.sharding import PartitionSpec as P


HD = 64


EPSILON = 1e-05
CONTRACT_ROWS = (((0,), (0,)), ((), ()))
CONTRACT_COLS = (((1,), (1,)), ((), ()))


def normalize(values, gain, shift):
    average = jnp.mean(values, axis=-1, keepdims=True)
    centered = values - average
    variance = jnp.mean(centered * centered, axis=-1, keepdims=True)
    return centered * lax.rsqrt(variance + EPSILON) * gain + shift


def exact_gelu(values):
    return 0.5 * values * (1.0 + lax.erf(values * math.sqrt(0.5)))


def product(left, right):
    return jnp.dot(left, right, preferred_element_type=jnp.float32)


def over_rows(left, right):
    return lax.dot_general(left, right, CONTRACT_ROWS, preferred_element_type=jnp.float32)


def over_cols(left, right):
    return lax.dot_general(left, right, CONTRACT_COLS, preferred_element_type=jnp.float32)


def column_sum(values):
    return jnp.sum(values.astype(jnp.float32), axis=0)


def attention_scores(queries_split, keys_split, allowed):
    scaling = 1.0 / math.sqrt(HD)
    scores = (
        jnp.einsum("rqhe,rkhe->rhqk", queries_split, keys_split, preferred_element_type=jnp.float32)
        * scaling
    )
    return jnp.where(allowed[:, None], scores, -1e30)


def gather_pieces(blocks, one):
    n_dp = lax.axis_size("dp")
    d = lax.axis_index("dp")
    pieces = []
    for block in blocks:
        piece_rows = block.shape[0] // n_dp
        pieces.append(lax.dynamic_slice_in_dim(block, d * piece_rows, piece_rows, 0))
    sent = jnp.concatenate([p.astype(jnp.float32) for p in pieces], axis=0) * one
    got = lax.all_gather(sent, ("mp", "dp"), axis=0)
    n_mp = lax.axis_size("mp")
    got = got.reshape(n_mp, n_dp, *sent.shape)
    out, at = [], 0
    for p in pieces:
        rows = p.shape[0]
        out.append(got[:, :, at : at + rows])
        at += rows
    return out


def whole_rows(part, one, dtype):
    n_mp, n_dp, rows, width = part.shape
    return (part * one).astype(dtype).reshape(n_mp * n_dp * rows, width)


def other_rows(part, one, dtype):
    n_mp, n_dp, rows, width = part.shape
    me = lax.axis_index("mp")
    blocks = [
        lax.dynamic_index_in_dim(part, (me + step) % n_mp, 0, keepdims=False)
        for step in range(1, n_mp)
    ]
    return (jnp.stack(blocks) * one).astype(dtype).reshape((n_mp - 1) * n_dp * rows, width)


def gather_biases(shards):
    n_mp = lax.axis_size("mp")
    me = lax.axis_index("mp")
    own = jnp.concatenate(shards)
    got = [own] + [
        lax.ppermute(own, "mp", [(i, (i + step) % n_mp) for i in range(n_mp)])
        for step in range(1, n_mp)
    ]
    got = jnp.stack(got)
    by_shard = jnp.take(got, (me - jnp.arange(n_mp)) % n_mp, axis=0)
    by_other = jnp.take(got, (-jnp.arange(1, n_mp)) % n_mp, axis=0)
    out, at = [], 0
    for i, shard in enumerate(shards):
        width = shard.shape[0]
        source = by_other if i == len(shards) - 1 else by_shard
        out.append(source[:, at : at + width].reshape(-1))
        at += width
    return out


def own_columns(values, width):
    return lax.dynamic_slice_in_dim(values, lax.axis_index("mp") * width, width, 1)


def on_device(
    inputs,
    timesteps,
    segments,
    valid_mask,
    step_table,
    ln1_gain,
    ln1_shift,
    w_query_shard,
    b_query_shard,
    w_key_shard,
    w_value_shard,
    b_value_shard,
    w_out_shard,
    b_out,
    ln2_gain,
    ln2_shift,
    w_up_shard,
    b_up_shard,
    w_down_shard,
    b_down,
    cotangent,
):
    row_count, seq_len, model_width = inputs.shape
    token_count = row_count * seq_len
    qkv_width = w_query_shard.shape[1]
    ff_width = w_up_shard.shape[1]
    one = 1.0 + 0.0 * ln1_gain[0]
    low_type = jnp.bfloat16
    q_part, k_part, v_part, o_part = gather_pieces(
        (
            w_query_shard.T,
            w_key_shard.T,
            w_value_shard.T,
            w_out_shard,
        ),
        one,
    )
    w_query_t = whole_rows(q_part, one, low_type)
    w_key_t = whole_rows(k_part, one, low_type)
    w_value_t = whole_rows(v_part, one, low_type)
    b_query, b_value, b_up_others = gather_biases(
        (b_query_shard, b_value_shard, b_up_shard)
    )
    up_part, down_part = gather_pieces(
        (
            w_up_shard.T,
            w_down_shard,
        ),
        one,
    )
    w_out = whole_rows(o_part, one, low_type)
    w_up_others = other_rows(up_part, one, low_type)
    w_down_others = other_rows(down_part, one, low_type)
    heads = w_query_t.shape[0] // HD
    scaling = 1.0 / math.sqrt(HD)
    head_shape = (row_count, seq_len, heads, HD)
    start = inputs.astype(jnp.float32) + step_table[timesteps].astype(jnp.float32)[:, None, :]
    start = start.reshape(token_count, model_width)
    normed, first_pull = jax.vjp(normalize, start, ln1_gain, ln1_shift)
    normed_low = normed.astype(low_type)
    queries = (over_cols(normed_low, w_query_t) + b_query).astype(low_type)
    key_rows = over_cols(normed_low, w_key_t).astype(low_type)
    value_rows = (over_cols(normed_low, w_value_t) + b_value).astype(low_type)
    queries_split = queries.reshape(head_shape)
    keys_split = key_rows.reshape(head_shape)
    values_split = value_rows.reshape(head_shape)
    places = jnp.arange(seq_len, dtype=jnp.int32)
    diagonal = places[:, None] == places[None, :]
    allowed = (segments[:, :, None] == segments[:, None, :]) & (
        (valid_mask[:, None, :] > 0) | diagonal[None]
    )
    scores = attention_scores(queries_split, keys_split, allowed)
    row_max = jnp.max(scores, axis=-1, keepdims=True)
    powers = jnp.exp(scores - row_max)
    total = jnp.sum(powers, axis=-1, keepdims=True)
    log_total = row_max + jnp.log(total)
    probabilities = powers / total
    probabilities_low = probabilities.astype(low_type)
    mixed = jnp.einsum(
        "rhqk,rkhe->rqhe",
        probabilities_low,
        values_split,
        preferred_element_type=jnp.float32,
    )
    mixed = mixed.reshape(token_count, heads * HD).astype(low_type)
    attended = product(mixed, w_out) + b_out
    middle = start + attended
    normed2, second_pull = jax.vjp(normalize, middle, ln2_gain, ln2_shift)
    normed2_low = normed2.astype(low_type)
    upper_own = product(normed2_low, w_up_shard) + b_up_shard
    activated_own, gelu_pull_own = jax.vjp(exact_gelu, upper_own)
    hidden_own = activated_own.astype(low_type)
    lowered_own = product(hidden_own, w_down_shard)
    grad_out = cotangent.reshape(token_count, model_width).astype(jnp.float32)
    grad_out = grad_out * valid_mask.reshape(token_count, 1).astype(jnp.float32)
    grad_out_low = grad_out.astype(low_type)
    grad_out, grad_out_low = lax.optimization_barrier((grad_out, grad_out_low))
    grad_w_down = over_rows(hidden_own, grad_out_low)
    grad_b_down = jnp.sum(grad_out, axis=0)
    (grad_upper_own,) = gelu_pull_own(over_cols(grad_out_low, w_down_shard))
    grad_upper_own = grad_upper_own.astype(low_type)
    grad_w_up = over_rows(normed2_low, grad_upper_own)
    grad_b_up = column_sum(grad_upper_own)
    ffn_grads = lax.psum(jnp.concatenate([grad_w_down, grad_w_up], axis=0), "dp")
    grad_w_down, grad_w_up = ffn_grads[:ff_width], ffn_grads[ff_width:]
    grad_normed2_own = over_cols(grad_upper_own, w_up_shard)
    upper = over_cols(normed2_low, w_up_others) + b_up_others
    activated, gelu_pull = jax.vjp(exact_gelu, upper)
    hidden = lax.optimization_barrier(activated.astype(low_type))
    lowered = lowered_own + product(hidden, w_down_others)
    output = (middle + lowered + b_down).astype(low_type)
    output = output.reshape(row_count, seq_len, model_width)
    (grad_upper,) = gelu_pull(over_cols(grad_out_low, w_down_others))
    grad_upper_low = lax.optimization_barrier(grad_upper.astype(low_type))
    grad_normed2 = grad_normed2_own + product(grad_upper_low, w_up_others)
    grad_mid_norm, grad_ln2_gain, grad_ln2_shift = second_pull(grad_normed2)
    grad_middle = grad_out + grad_mid_norm
    grad_mid_low = grad_middle.astype(low_type)
    grad_w_out = over_rows(own_columns(mixed, qkv_width), grad_mid_low)
    grad_b_out = column_sum(grad_mid_low)
    grad_mixed = over_cols(grad_mid_low, w_out).astype(low_type).reshape(head_shape)
    soft_again = probabilities
    grad_soft = jnp.einsum(
        "rqhe,rkhe->rhqk", grad_mixed, values_split, preferred_element_type=jnp.float32
    )
    delta = jnp.sum(soft_again * grad_soft, axis=-1, keepdims=True)
    grad_scores = (soft_again * (grad_soft - delta)).astype(low_type)
    grad_queries = jnp.einsum(
        "rhqk,rkhe->rqhe", grad_scores, keys_split, preferred_element_type=jnp.float32
    )
    grad_queries = (grad_queries * scaling).reshape(token_count, heads * HD).astype(low_type)
    grad_keys = jnp.einsum(
        "rhqk,rqhe->rkhe", grad_scores, queries_split, preferred_element_type=jnp.float32
    )
    grad_keys = (grad_keys * scaling).reshape(token_count, heads * HD).astype(low_type)
    grad_values = jnp.einsum(
        "rhqk,rqhe->rkhe",
        probabilities_low,
        grad_mixed,
        preferred_element_type=jnp.float32,
    )
    grad_values = grad_values.reshape(token_count, heads * HD).astype(low_type)
    own_grad_queries = own_columns(grad_queries, qkv_width)
    own_grad_values = own_columns(grad_values, qkv_width)
    grad_w_query = over_rows(normed_low, own_grad_queries)
    grad_b_query = column_sum(own_grad_queries)
    grad_w_key = over_rows(normed_low, own_columns(grad_keys, qkv_width))
    grad_w_value = over_rows(normed_low, own_grad_values)
    grad_b_value = column_sum(own_grad_values)
    grad_normed = (
        product(grad_queries, w_query_t)
        + product(grad_keys, w_key_t)
        + product(grad_values, w_value_t)
    )
    grad_start_norm, grad_ln1_gain, grad_ln1_shift = first_pull(grad_normed)
    grad_start = grad_middle + grad_start_norm
    input_grad = grad_start.astype(low_type).reshape(row_count, seq_len, model_width)
    row_sums = jnp.sum(grad_start.reshape(row_count, seq_len, model_width), axis=1)
    column_count = model_width // lax.axis_size("mp")
    table_columns = own_columns(row_sums, column_count)
    step_count = step_table.shape[0]
    one_hot = (timesteps[:, None] == jnp.arange(step_count, dtype=jnp.int32)[None, :]).astype(
        jnp.float32
    )
    table_grad = lax.dot_general(
        one_hot,
        table_columns,
        CONTRACT_ROWS,
        precision=lax.Precision.HIGHEST,
        preferred_element_type=jnp.float32,
    )
    small = (
        grad_ln1_gain,
        grad_ln1_shift,
        grad_b_query,
        grad_b_value,
        grad_b_out,
        grad_b_down,
        grad_b_up,
        grad_ln2_gain,
        grad_ln2_shift,
    )
    small_rows = jnp.concatenate(small).reshape(-1, column_count)
    packed = jnp.concatenate([table_grad, small_rows], axis=0)
    tie = 0.0 * ffn_grads[0, 0]
    (
        grad_w_query,
        grad_w_key,
        grad_w_value,
        grad_w_out,
        packed,
    ) = lax.psum(
        (
            grad_w_query + tie,
            grad_w_key,
            grad_w_value,
            grad_w_out,
            packed,
        ),
        "dp",
    )
    table_grad = packed[:step_count]
    flat_small = packed[step_count:].reshape(-1)
    unpacked, at = [], 0
    for item in small:
        unpacked.append(flat_small[at : at + item.shape[0]])
        at += item.shape[0]
    (
        grad_ln1_gain,
        grad_ln1_shift,
        grad_b_query,
        grad_b_value,
        grad_b_out,
        grad_b_down,
        grad_b_up,
        grad_ln2_gain,
        grad_ln2_shift,
    ) = unpacked
    return (
        output,
        input_grad,
        grad_ln1_gain,
        grad_ln1_shift,
        grad_w_query,
        grad_b_query,
        grad_w_key,
        grad_w_value,
        grad_b_value,
        grad_w_out,
        grad_b_out,
        grad_ln2_gain,
        grad_ln2_shift,
        grad_w_up,
        grad_b_up,
        grad_w_down,
        grad_b_down,
        table_grad,
    )


def solution(mesh):
    in_specs = (
        P("dp", None, None),
        P("dp"),
        P("dp", None),
        P("dp", None),
        P(),
        P(),
        P(),
        P(None, "mp"),
        P("mp"),
        P(None, "mp"),
        P(None, "mp"),
        P("mp"),
        P("mp", None),
        P(),
        P(),
        P(),
        P(None, "mp"),
        P("mp"),
        P("mp", None),
        P(),
        P("dp", None, None),
    )
    out_specs = (
        P("dp", None, None),
        P("dp", None, None),
        P(),
        P(),
        P(None, "mp"),
        P("mp"),
        P(None, "mp"),
        P(None, "mp"),
        P("mp"),
        P("mp", None),
        P(),
        P(),
        P(),
        P(None, "mp"),
        P("mp"),
        P("mp", None),
        P(),
        P(None, "mp"),
    )

    return jax.shard_map(
        on_device, mesh=mesh, in_specs=in_specs, out_specs=out_specs, check_vma=False
    )
```

```python
import math

import jax
import jax.numpy as jnp
from jax import lax
from jax.sharding import PartitionSpec as P


HD = 64


EPSILON = 1e-05
CONTRACT_ROWS = (((0,), (0,)), ((), ()))
CONTRACT_COLS = (((1,), (1,)), ((), ()))


def normalize(values, gain, shift):
    average = jnp.mean(values, axis=-1, keepdims=True)
    centered = values - average
    variance = jnp.mean(centered * centered, axis=-1, keepdims=True)
    return centered * lax.rsqrt(variance + EPSILON) * gain + shift


def exact_gelu(values):
    return 0.5 * values * (1.0 + lax.erf(values * math.sqrt(0.5)))


def product(left, right):
    return jnp.dot(left, right, preferred_element_type=jnp.float32)


def over_rows(left, right):
    return lax.dot_general(left, right, CONTRACT_ROWS, preferred_element_type=jnp.float32)


def over_cols(left, right):
    return lax.dot_general(left, right, CONTRACT_COLS, preferred_element_type=jnp.float32)


def column_sum(values):
    return jnp.sum(values.astype(jnp.float32), axis=0)


def attention_scores(queries_split, keys_split, allowed):
    scaling = 1.0 / math.sqrt(HD)
    scores = (
        jnp.einsum("rqhe,rkhe->rhqk", queries_split, keys_split, preferred_element_type=jnp.float32)
        * scaling
    )
    return jnp.where(allowed[:, None], scores, -1e30)


def gather_pieces(blocks, one):
    n_dp = lax.axis_size("dp")
    d = lax.axis_index("dp")
    pieces = []
    for block in blocks:
        piece_rows = block.shape[0] // n_dp
        pieces.append(lax.dynamic_slice_in_dim(block, d * piece_rows, piece_rows, 0))
    sent = jnp.concatenate([p.astype(jnp.float32) for p in pieces], axis=0) * one
    got = lax.all_gather(sent, ("mp", "dp"), axis=0)
    n_mp = lax.axis_size("mp")
    got = got.reshape(n_mp, n_dp, *sent.shape)
    out, at = [], 0
    for p in pieces:
        rows = p.shape[0]
        out.append(got[:, :, at : at + rows])
        at += rows
    return out


def whole_rows(part, one, dtype):
    n_mp, n_dp, rows, width = part.shape
    return (part * one).astype(dtype).reshape(n_mp * n_dp * rows, width)


def other_rows(part, one, dtype):
    n_mp, n_dp, rows, width = part.shape
    me = lax.axis_index("mp")
    blocks = [
        lax.dynamic_index_in_dim(part, (me + step) % n_mp, 0, keepdims=False)
        for step in range(1, n_mp)
    ]
    return (jnp.stack(blocks) * one).astype(dtype).reshape((n_mp - 1) * n_dp * rows, width)


def gather_biases(shards):
    n_mp = lax.axis_size("mp")
    me = lax.axis_index("mp")
    own = jnp.concatenate(shards)
    got = [own] + [
        lax.ppermute(own, "mp", [(i, (i + step) % n_mp) for i in range(n_mp)])
        for step in range(1, n_mp)
    ]
    got = jnp.stack(got)
    by_shard = jnp.take(got, (me - jnp.arange(n_mp)) % n_mp, axis=0)
    by_other = jnp.take(got, (-jnp.arange(1, n_mp)) % n_mp, axis=0)
    out, at = [], 0
    for i, shard in enumerate(shards):
        width = shard.shape[0]
        source = by_other if i == len(shards) - 1 else by_shard
        out.append(source[:, at : at + width].reshape(-1))
        at += width
    return out


def own_columns(values, width):
    return lax.dynamic_slice_in_dim(values, lax.axis_index("mp") * width, width, 1)


def on_device(
    inputs,
    timesteps,
    segments,
    valid_mask,
    step_table,
    ln1_gain,
    ln1_shift,
    w_query_shard,
    b_query_shard,
    w_key_shard,
    w_value_shard,
    b_value_shard,
    w_out_shard,
    b_out,
    ln2_gain,
    ln2_shift,
    w_up_shard,
    b_up_shard,
    w_down_shard,
    b_down,
    cotangent,
):
    row_count, seq_len, model_width = inputs.shape
    token_count = row_count * seq_len
    qkv_width = w_query_shard.shape[1]
    ff_width = w_up_shard.shape[1]
    one = 1.0 + 0.0 * ln1_gain[0]
    low_type = jnp.bfloat16
    q_part, k_part, v_part, o_part = gather_pieces(
        (
            w_query_shard.T,
            w_key_shard.T,
            w_value_shard.T,
            w_out_shard,
        ),
        one,
    )
    w_query_t = whole_rows(q_part, one, low_type)
    w_key_t = whole_rows(k_part, one, low_type)
    w_value_t = whole_rows(v_part, one, low_type)
    b_query, b_value, b_up_others = gather_biases(
        (b_query_shard, b_value_shard, b_up_shard)
    )
    up_part, down_part = gather_pieces(
        (
            w_up_shard.T,
            w_down_shard,
        ),
        one,
    )
    w_out = whole_rows(o_part, one, low_type)
    w_up_others = other_rows(up_part, one, low_type)
    w_down_others = other_rows(down_part, one, low_type)
    heads = w_query_t.shape[0] // HD
    scaling = 1.0 / math.sqrt(HD)
    head_shape = (row_count, seq_len, heads, HD)
    start = inputs.astype(jnp.float32) + step_table[timesteps].astype(jnp.float32)[:, None, :]
    start = start.reshape(token_count, model_width)
    normed, first_pull = jax.vjp(normalize, start, ln1_gain, ln1_shift)
    normed_low = normed.astype(low_type)
    queries = (over_cols(normed_low, w_query_t) + b_query).astype(low_type)
    key_rows = over_cols(normed_low, w_key_t).astype(low_type)
    value_rows = (over_cols(normed_low, w_value_t) + b_value).astype(low_type)
    queries_split = queries.reshape(head_shape)
    keys_split = key_rows.reshape(head_shape)
    values_split = value_rows.reshape(head_shape)
    places = jnp.arange(seq_len, dtype=jnp.int32)
    diagonal = places[:, None] == places[None, :]
    allowed = (segments[:, :, None] == segments[:, None, :]) & (
        (valid_mask[:, None, :] > 0) | diagonal[None]
    )
    scores = attention_scores(queries_split, keys_split, allowed)
    row_max = jnp.max(scores, axis=-1, keepdims=True)
    powers = jnp.exp(scores - row_max)
    total = jnp.sum(powers, axis=-1, keepdims=True)
    log_total = row_max + jnp.log(total)
    probabilities = powers / total
    probabilities_low = probabilities.astype(low_type)
    mixed = jnp.einsum(
        "rhqk,rkhe->rqhe",
        probabilities_low,
        values_split,
        preferred_element_type=jnp.float32,
    )
    mixed = mixed.reshape(token_count, heads * HD).astype(low_type)
    attended = product(mixed, w_out) + b_out
    middle = start + attended
    normed2, second_pull = jax.vjp(normalize, middle, ln2_gain, ln2_shift)
    normed2_low = normed2.astype(low_type)
    upper_own = product(normed2_low, w_up_shard) + b_up_shard
    activated_own, gelu_pull_own = jax.vjp(exact_gelu, upper_own)
    hidden_own = activated_own.astype(low_type)
    lowered_own = product(hidden_own, w_down_shard)
    grad_out = cotangent.reshape(token_count, model_width).astype(jnp.float32)
    grad_out = grad_out * valid_mask.reshape(token_count, 1).astype(jnp.float32)
    grad_out_low = grad_out.astype(low_type)
    grad_b_down = jnp.sum(grad_out, axis=0)
    grad_out, grad_out_low, grad_b_down = lax.optimization_barrier(
        (grad_out, grad_out_low, grad_b_down)
    )
    grad_w_down = over_rows(hidden_own, grad_out_low)
    (grad_upper_own,) = gelu_pull_own(over_cols(grad_out_low, w_down_shard))
    grad_upper_own = grad_upper_own.astype(low_type)
    grad_w_up = over_rows(normed2_low, grad_upper_own)
    grad_b_up = column_sum(grad_upper_own)
    grad_normed2_own = over_cols(grad_upper_own, w_up_shard)
    upper = over_cols(normed2_low, w_up_others) + b_up_others
    activated, gelu_pull = jax.vjp(exact_gelu, upper)
    hidden = lax.optimization_barrier(activated.astype(low_type))
    lowered = lowered_own + product(hidden, w_down_others)
    output = (middle + lowered + b_down).astype(low_type)
    output = output.reshape(row_count, seq_len, model_width)
    (grad_upper,) = gelu_pull(over_cols(grad_out_low, w_down_others))
    grad_upper_low = lax.optimization_barrier(grad_upper.astype(low_type))
    grad_normed2 = grad_normed2_own + product(grad_upper_low, w_up_others)
    grad_mid_norm, grad_ln2_gain, grad_ln2_shift = second_pull(grad_normed2)
    grad_middle = grad_out + grad_mid_norm
    grad_mid_low = grad_middle.astype(low_type)
    grad_w_out = over_rows(own_columns(mixed, qkv_width), grad_mid_low)
    grad_b_out = column_sum(grad_mid_low)
    early_rows = jnp.stack(
        [grad_b_down, grad_b_up, grad_ln2_gain, grad_ln2_shift, grad_b_out]
    )
    early_rows = jnp.pad(early_rows, ((0, 8 - early_rows.shape[0]), (0, 0)))
    ffn_grads = lax.psum(
        jnp.concatenate([grad_w_down, grad_w_up, grad_w_out, early_rows], axis=0), "dp"
    )
    grad_w_down = ffn_grads[:ff_width]
    grad_w_up = ffn_grads[ff_width : 2 * ff_width]
    grad_w_out = ffn_grads[2 * ff_width : 2 * ff_width + qkv_width]
    early_rows = ffn_grads[2 * ff_width + qkv_width :]
    grad_b_down, grad_b_up, grad_ln2_gain, grad_ln2_shift, grad_b_out = [
        early_rows[i] for i in range(5)
    ]
    grad_mixed = over_cols(grad_mid_low, w_out).astype(low_type).reshape(head_shape)
    soft_again = probabilities
    grad_soft = jnp.einsum(
        "rqhe,rkhe->rhqk", grad_mixed, values_split, preferred_element_type=jnp.float32
    )
    delta = jnp.sum(soft_again * grad_soft, axis=-1, keepdims=True)
    grad_scores = (soft_again * (grad_soft - delta)).astype(low_type)
    grad_queries = jnp.einsum(
        "rhqk,rkhe->rqhe", grad_scores, keys_split, preferred_element_type=jnp.float32
    )
    grad_queries = (grad_queries * scaling).reshape(token_count, heads * HD).astype(low_type)
    grad_keys = jnp.einsum(
        "rhqk,rqhe->rkhe", grad_scores, queries_split, preferred_element_type=jnp.float32
    )
    grad_keys = (grad_keys * scaling).reshape(token_count, heads * HD).astype(low_type)
    grad_values = jnp.einsum(
        "rhqk,rqhe->rkhe",
        probabilities_low,
        grad_mixed,
        preferred_element_type=jnp.float32,
    )
    grad_values = grad_values.reshape(token_count, heads * HD).astype(low_type)
    own_grad_queries = own_columns(grad_queries, qkv_width)
    own_grad_values = own_columns(grad_values, qkv_width)
    grad_w_query = over_rows(normed_low, own_grad_queries)
    grad_b_query = column_sum(own_grad_queries)
    grad_w_key = over_rows(normed_low, own_columns(grad_keys, qkv_width))
    grad_w_value = over_rows(normed_low, own_grad_values)
    grad_b_value = column_sum(own_grad_values)
    grad_normed = (
        product(grad_queries, w_query_t)
        + product(grad_keys, w_key_t)
        + product(grad_values, w_value_t)
    )
    grad_start_norm, grad_ln1_gain, grad_ln1_shift = first_pull(grad_normed)
    grad_start = grad_middle + grad_start_norm
    input_grad = grad_start.astype(low_type).reshape(row_count, seq_len, model_width)
    row_sums = jnp.sum(grad_start.reshape(row_count, seq_len, model_width), axis=1)
    column_count = model_width // lax.axis_size("mp")
    table_columns = own_columns(row_sums, column_count)
    step_count = step_table.shape[0]
    one_hot = (timesteps[:, None] == jnp.arange(step_count, dtype=jnp.int32)[None, :]).astype(
        jnp.float32
    )
    table_grad = lax.dot_general(
        one_hot,
        table_columns,
        CONTRACT_ROWS,
        precision=lax.Precision.HIGHEST,
        preferred_element_type=jnp.float32,
    )
    small = (
        grad_ln1_gain,
        grad_ln1_shift,
        grad_b_query,
        grad_b_value,
    )
    small_rows = jnp.concatenate(small).reshape(-1, column_count)
    packed = jnp.concatenate([table_grad, small_rows], axis=0)
    tie = 0.0 * ffn_grads[0, 0]
    (
        grad_w_query,
        grad_w_key,
        grad_w_value,
        packed,
    ) = lax.psum(
        (
            grad_w_query + tie,
            grad_w_key,
            grad_w_value,
            packed,
        ),
        "dp",
    )
    table_grad = packed[:step_count]
    flat_small = packed[step_count:].reshape(-1)
    unpacked, at = [], 0
    for item in small:
        unpacked.append(flat_small[at : at + item.shape[0]])
        at += item.shape[0]
    grad_ln1_gain, grad_ln1_shift, grad_b_query, grad_b_value = unpacked
    return (
        output,
        input_grad,
        grad_ln1_gain,
        grad_ln1_shift,
        grad_w_query,
        grad_b_query,
        grad_w_key,
        grad_w_value,
        grad_b_value,
        grad_w_out,
        grad_b_out,
        grad_ln2_gain,
        grad_ln2_shift,
        grad_w_up,
        grad_b_up,
        grad_w_down,
        grad_b_down,
        table_grad,
    )


def solution(mesh):
    in_specs = (
        P("dp", None, None),
        P("dp"),
        P("dp", None),
        P("dp", None),
        P(),
        P(),
        P(),
        P(None, "mp"),
        P("mp"),
        P(None, "mp"),
        P(None, "mp"),
        P("mp"),
        P("mp", None),
        P(),
        P(),
        P(),
        P(None, "mp"),
        P("mp"),
        P("mp", None),
        P(),
        P("dp", None, None),
    )
    out_specs = (
        P("dp", None, None),
        P("dp", None, None),
        P(),
        P(),
        P(None, "mp"),
        P("mp"),
        P(None, "mp"),
        P(None, "mp"),
        P("mp"),
        P("mp", None),
        P(),
        P(),
        P(),
        P(None, "mp"),
        P("mp"),
        P("mp", None),
        P(),
        P(None, "mp"),
    )

    return jax.shard_map(
        on_device, mesh=mesh, in_specs=in_specs, out_specs=out_specs, check_vma=False
    )
```

```python
import math

import jax
import jax.numpy as jnp
from jax import lax
from jax.sharding import PartitionSpec as P


HD = 64


EPSILON = 1e-05
CONTRACT_ROWS = (((0,), (0,)), ((), ()))
CONTRACT_COLS = (((1,), (1,)), ((), ()))


def normalize(values, gain, shift):
    average = jnp.mean(values, axis=-1, keepdims=True)
    centered = values - average
    variance = jnp.mean(centered * centered, axis=-1, keepdims=True)
    return centered * lax.rsqrt(variance + EPSILON) * gain + shift


def exact_gelu(values):
    return 0.5 * values * (1.0 + lax.erf(values * math.sqrt(0.5)))


def product(left, right):
    return jnp.dot(left, right, preferred_element_type=jnp.float32)


def over_rows(left, right):
    return lax.dot_general(left, right, CONTRACT_ROWS, preferred_element_type=jnp.float32)


def over_cols(left, right):
    return lax.dot_general(left, right, CONTRACT_COLS, preferred_element_type=jnp.float32)


def column_sum(values):
    return jnp.sum(values.astype(jnp.float32), axis=0)


def attention_scores(queries_split, keys_split, allowed):
    scaling = 1.0 / math.sqrt(HD)
    scores = (
        jnp.einsum("rqhe,rkhe->rhqk", queries_split, keys_split, preferred_element_type=jnp.float32)
        * scaling
    )
    return jnp.where(allowed[:, None], scores, -1e30)


def gather_pieces(blocks, one):
    n_dp = lax.axis_size("dp")
    d = lax.axis_index("dp")
    pieces = []
    for block in blocks:
        piece_rows = block.shape[0] // n_dp
        pieces.append(lax.dynamic_slice_in_dim(block, d * piece_rows, piece_rows, 0))
    sent = jnp.concatenate([p.astype(jnp.float32) for p in pieces], axis=0) * one
    got = lax.all_gather(sent, ("mp", "dp"), axis=0)
    n_mp = lax.axis_size("mp")
    got = got.reshape(n_mp, n_dp, *sent.shape)
    out, at = [], 0
    for p in pieces:
        rows = p.shape[0]
        out.append(got[:, :, at : at + rows])
        at += rows
    return out


def whole_rows(part, one, dtype):
    n_mp, n_dp, rows, width = part.shape
    return (part * one).astype(dtype).reshape(n_mp * n_dp * rows, width)


def other_rows(part, one, dtype):
    n_mp, n_dp, rows, width = part.shape
    me = lax.axis_index("mp")
    blocks = [
        lax.dynamic_index_in_dim(part, (me + step) % n_mp, 0, keepdims=False)
        for step in range(1, n_mp)
    ]
    return (jnp.stack(blocks) * one).astype(dtype).reshape((n_mp - 1) * n_dp * rows, width)


def gather_by_permutes(shard, one, dtype):
    n_mp = lax.axis_size("mp")
    me = lax.axis_index("mp")
    own = shard.astype(jnp.float32) * one
    got = [own] + [
        lax.ppermute(own, "mp", [(i, (i + step) % n_mp) for i in range(n_mp)])
        for step in range(1, n_mp)
    ]
    got = jnp.stack(got) * one
    by_shard = jnp.take(got, (me - jnp.arange(n_mp)) % n_mp, axis=0)
    return by_shard.astype(dtype).reshape(n_mp * shard.shape[0], shard.shape[1])


def gather_biases(shards):
    n_mp = lax.axis_size("mp")
    me = lax.axis_index("mp")
    own = jnp.concatenate(shards)
    got = [own] + [
        lax.ppermute(own, "mp", [(i, (i + step) % n_mp) for i in range(n_mp)])
        for step in range(1, n_mp)
    ]
    got = jnp.stack(got)
    by_shard = jnp.take(got, (me - jnp.arange(n_mp)) % n_mp, axis=0)
    by_other = jnp.take(got, (-jnp.arange(1, n_mp)) % n_mp, axis=0)
    out, at = [], 0
    for i, shard in enumerate(shards):
        width = shard.shape[0]
        source = by_other if i == len(shards) - 1 else by_shard
        out.append(source[:, at : at + width].reshape(-1))
        at += width
    return out


def own_columns(values, width):
    return lax.dynamic_slice_in_dim(values, lax.axis_index("mp") * width, width, 1)


def on_device(
    inputs,
    timesteps,
    segments,
    valid_mask,
    step_table,
    ln1_gain,
    ln1_shift,
    w_query_shard,
    b_query_shard,
    w_key_shard,
    w_value_shard,
    b_value_shard,
    w_out_shard,
    b_out,
    ln2_gain,
    ln2_shift,
    w_up_shard,
    b_up_shard,
    w_down_shard,
    b_down,
    cotangent,
):
    row_count, seq_len, model_width = inputs.shape
    token_count = row_count * seq_len
    qkv_width = w_query_shard.shape[1]
    ff_width = w_up_shard.shape[1]
    one = 1.0 + 0.0 * ln1_gain[0]
    low_type = jnp.bfloat16
    q_part, k_part, v_part = gather_pieces(
        (
            w_query_shard.T,
            w_key_shard.T,
            w_value_shard.T,
        ),
        one,
    )
    w_query_t = whole_rows(q_part, one, low_type)
    w_key_t = whole_rows(k_part, one, low_type)
    w_value_t = whole_rows(v_part, one, low_type)
    b_query, b_value, b_up_others = gather_biases(
        (b_query_shard, b_value_shard, b_up_shard)
    )
    up_part, down_part = gather_pieces(
        (
            w_up_shard.T,
            w_down_shard,
        ),
        one,
    )
    w_out = gather_by_permutes(w_out_shard, one, low_type)
    w_up_others = other_rows(up_part, one, low_type)
    w_down_others = other_rows(down_part, one, low_type)
    heads = w_query_t.shape[0] // HD
    scaling = 1.0 / math.sqrt(HD)
    head_shape = (row_count, seq_len, heads, HD)
    start = inputs.astype(jnp.float32) + step_table[timesteps].astype(jnp.float32)[:, None, :]
    start = start.reshape(token_count, model_width)
    normed, first_pull = jax.vjp(normalize, start, ln1_gain, ln1_shift)
    normed_low = normed.astype(low_type)
    queries = (over_cols(normed_low, w_query_t) + b_query).astype(low_type)
    key_rows = over_cols(normed_low, w_key_t).astype(low_type)
    value_rows = (over_cols(normed_low, w_value_t) + b_value).astype(low_type)
    queries_split = queries.reshape(head_shape)
    keys_split = key_rows.reshape(head_shape)
    values_split = value_rows.reshape(head_shape)
    places = jnp.arange(seq_len, dtype=jnp.int32)
    diagonal = places[:, None] == places[None, :]
    allowed = (segments[:, :, None] == segments[:, None, :]) & (
        (valid_mask[:, None, :] > 0) | diagonal[None]
    )
    scores = attention_scores(queries_split, keys_split, allowed)
    row_max = jnp.max(scores, axis=-1, keepdims=True)
    powers = jnp.exp(scores - row_max)
    total = jnp.sum(powers, axis=-1, keepdims=True)
    log_total = row_max + jnp.log(total)
    probabilities = powers / total
    probabilities_low = probabilities.astype(low_type)
    mixed = jnp.einsum(
        "rhqk,rkhe->rqhe",
        probabilities_low,
        values_split,
        preferred_element_type=jnp.float32,
    )
    mixed = mixed.reshape(token_count, heads * HD).astype(low_type)
    attended = product(mixed, w_out) + b_out
    middle = start + attended
    normed2, second_pull = jax.vjp(normalize, middle, ln2_gain, ln2_shift)
    normed2_low = normed2.astype(low_type)
    upper_own = product(normed2_low, w_up_shard) + b_up_shard
    activated_own, gelu_pull_own = jax.vjp(exact_gelu, upper_own)
    hidden_own = activated_own.astype(low_type)
    lowered_own = product(hidden_own, w_down_shard)
    grad_out = cotangent.reshape(token_count, model_width).astype(jnp.float32)
    grad_out = grad_out * valid_mask.reshape(token_count, 1).astype(jnp.float32)
    grad_out_low = grad_out.astype(low_type)
    grad_out, grad_out_low = lax.optimization_barrier((grad_out, grad_out_low))
    grad_w_down = over_rows(hidden_own, grad_out_low)
    grad_b_down = jnp.sum(grad_out, axis=0)
    (grad_upper_own,) = gelu_pull_own(over_cols(grad_out_low, w_down_shard))
    grad_upper_own = grad_upper_own.astype(low_type)
    grad_w_up = over_rows(normed2_low, grad_upper_own)
    grad_b_up = column_sum(grad_upper_own)
    ffn_grads = lax.psum(jnp.concatenate([grad_w_down, grad_w_up], axis=0), "dp")
    grad_w_down, grad_w_up = ffn_grads[:ff_width], ffn_grads[ff_width:]
    grad_normed2_own = over_cols(grad_upper_own, w_up_shard)
    upper = over_cols(normed2_low, w_up_others) + b_up_others
    activated, gelu_pull = jax.vjp(exact_gelu, upper)
    hidden = lax.optimization_barrier(activated.astype(low_type))
    lowered = lowered_own + product(hidden, w_down_others)
    output = (middle + lowered + b_down).astype(low_type)
    output = output.reshape(row_count, seq_len, model_width)
    (grad_upper,) = gelu_pull(over_cols(grad_out_low, w_down_others))
    grad_upper_low = lax.optimization_barrier(grad_upper.astype(low_type))
    grad_normed2 = grad_normed2_own + product(grad_upper_low, w_up_others)
    grad_mid_norm, grad_ln2_gain, grad_ln2_shift = second_pull(grad_normed2)
    grad_middle = grad_out + grad_mid_norm
    grad_mid_low = grad_middle.astype(low_type)
    grad_w_out = over_rows(own_columns(mixed, qkv_width), grad_mid_low)
    grad_b_out = column_sum(grad_mid_low)
    grad_mixed = over_cols(grad_mid_low, w_out).astype(low_type).reshape(head_shape)
    soft_again = probabilities
    grad_soft = jnp.einsum(
        "rqhe,rkhe->rhqk", grad_mixed, values_split, preferred_element_type=jnp.float32
    )
    delta = jnp.sum(soft_again * grad_soft, axis=-1, keepdims=True)
    grad_scores = (soft_again * (grad_soft - delta)).astype(low_type)
    grad_queries = jnp.einsum(
        "rhqk,rkhe->rqhe", grad_scores, keys_split, preferred_element_type=jnp.float32
    )
    grad_queries = (grad_queries * scaling).reshape(token_count, heads * HD).astype(low_type)
    grad_keys = jnp.einsum(
        "rhqk,rqhe->rkhe", grad_scores, queries_split, preferred_element_type=jnp.float32
    )
    grad_keys = (grad_keys * scaling).reshape(token_count, heads * HD).astype(low_type)
    grad_values = jnp.einsum(
        "rhqk,rqhe->rkhe",
        probabilities_low,
        grad_mixed,
        preferred_element_type=jnp.float32,
    )
    grad_values = grad_values.reshape(token_count, heads * HD).astype(low_type)
    own_grad_queries = own_columns(grad_queries, qkv_width)
    own_grad_values = own_columns(grad_values, qkv_width)
    grad_w_query = over_rows(normed_low, own_grad_queries)
    grad_b_query = column_sum(own_grad_queries)
    grad_w_key = over_rows(normed_low, own_columns(grad_keys, qkv_width))
    grad_w_value = over_rows(normed_low, own_grad_values)
    grad_b_value = column_sum(own_grad_values)
    grad_normed = (
        product(grad_queries, w_query_t)
        + product(grad_keys, w_key_t)
        + product(grad_values, w_value_t)
    )
    grad_start_norm, grad_ln1_gain, grad_ln1_shift = first_pull(grad_normed)
    grad_start = grad_middle + grad_start_norm
    input_grad = grad_start.astype(low_type).reshape(row_count, seq_len, model_width)
    row_sums = jnp.sum(grad_start.reshape(row_count, seq_len, model_width), axis=1)
    column_count = model_width // lax.axis_size("mp")
    table_columns = own_columns(row_sums, column_count)
    step_count = step_table.shape[0]
    one_hot = (timesteps[:, None] == jnp.arange(step_count, dtype=jnp.int32)[None, :]).astype(
        jnp.float32
    )
    table_grad = lax.dot_general(
        one_hot,
        table_columns,
        CONTRACT_ROWS,
        precision=lax.Precision.HIGHEST,
        preferred_element_type=jnp.float32,
    )
    small = (
        grad_ln1_gain,
        grad_ln1_shift,
        grad_b_query,
        grad_b_value,
        grad_b_out,
        grad_b_down,
        grad_b_up,
        grad_ln2_gain,
        grad_ln2_shift,
    )
    small_rows = jnp.concatenate(small).reshape(-1, column_count)
    packed = jnp.concatenate([table_grad, small_rows], axis=0)
    tie = 0.0 * ffn_grads[0, 0]
    (
        grad_w_query,
        grad_w_key,
        grad_w_value,
        grad_w_out,
        packed,
    ) = lax.psum(
        (
            grad_w_query + tie,
            grad_w_key,
            grad_w_value,
            grad_w_out,
            packed,
        ),
        "dp",
    )
    table_grad = packed[:step_count]
    flat_small = packed[step_count:].reshape(-1)
    unpacked, at = [], 0
    for item in small:
        unpacked.append(flat_small[at : at + item.shape[0]])
        at += item.shape[0]
    (
        grad_ln1_gain,
        grad_ln1_shift,
        grad_b_query,
        grad_b_value,
        grad_b_out,
        grad_b_down,
        grad_b_up,
        grad_ln2_gain,
        grad_ln2_shift,
    ) = unpacked
    return (
        output,
        input_grad,
        grad_ln1_gain,
        grad_ln1_shift,
        grad_w_query,
        grad_b_query,
        grad_w_key,
        grad_w_value,
        grad_b_value,
        grad_w_out,
        grad_b_out,
        grad_ln2_gain,
        grad_ln2_shift,
        grad_w_up,
        grad_b_up,
        grad_w_down,
        grad_b_down,
        table_grad,
    )


def solution(mesh):
    in_specs = (
        P("dp", None, None),
        P("dp"),
        P("dp", None),
        P("dp", None),
        P(),
        P(),
        P(),
        P(None, "mp"),
        P("mp"),
        P(None, "mp"),
        P(None, "mp"),
        P("mp"),
        P("mp", None),
        P(),
        P(),
        P(),
        P(None, "mp"),
        P("mp"),
        P("mp", None),
        P(),
        P("dp", None, None),
    )
    out_specs = (
        P("dp", None, None),
        P("dp", None, None),
        P(),
        P(),
        P(None, "mp"),
        P("mp"),
        P(None, "mp"),
        P(None, "mp"),
        P("mp"),
        P("mp", None),
        P(),
        P(),
        P(),
        P(None, "mp"),
        P("mp"),
        P("mp", None),
        P(),
        P(None, "mp"),
    )

    return jax.shard_map(
        on_device, mesh=mesh, in_specs=in_specs, out_specs=out_specs, check_vma=False
    )
```

```python
import math

import jax
import jax.numpy as jnp
from jax import lax
from jax.sharding import PartitionSpec as P


HD = 64


EPSILON = 1e-05
CONTRACT_ROWS = (((0,), (0,)), ((), ()))
CONTRACT_COLS = (((1,), (1,)), ((), ()))


def normalize(values, gain, shift):
    average = jnp.mean(values, axis=-1, keepdims=True)
    centered = values - average
    variance = jnp.mean(centered * centered, axis=-1, keepdims=True)
    return centered * lax.rsqrt(variance + EPSILON) * gain + shift


def exact_gelu(values):
    return 0.5 * values * (1.0 + lax.erf(values * math.sqrt(0.5)))


def product(left, right):
    return jnp.dot(left, right, preferred_element_type=jnp.float32)


def over_rows(left, right):
    return lax.dot_general(left, right, CONTRACT_ROWS, preferred_element_type=jnp.float32)


def over_cols(left, right):
    return lax.dot_general(left, right, CONTRACT_COLS, preferred_element_type=jnp.float32)


def column_sum(values):
    return jnp.sum(values.astype(jnp.float32), axis=0)


def attention_scores(queries_split, keys_split, allowed):
    scaling = 1.0 / math.sqrt(HD)
    scores = (
        jnp.einsum("rqhe,rkhe->rhqk", queries_split, keys_split, preferred_element_type=jnp.float32)
        * scaling
    )
    return jnp.where(allowed[:, None], scores, -1e30)


def gather_pieces(blocks, one):
    n_dp = lax.axis_size("dp")
    d = lax.axis_index("dp")
    pieces = []
    for block in blocks:
        piece_rows = block.shape[0] // n_dp
        pieces.append(lax.dynamic_slice_in_dim(block, d * piece_rows, piece_rows, 0))
    sent = jnp.concatenate([p.astype(jnp.float32) for p in pieces], axis=0) * one
    got = lax.all_gather(sent, ("mp", "dp"), axis=0)
    n_mp = lax.axis_size("mp")
    got = got.reshape(n_mp, n_dp, *sent.shape)
    out, at = [], 0
    for p in pieces:
        rows = p.shape[0]
        out.append(got[:, :, at : at + rows])
        at += rows
    return out


def whole_rows(part, one, dtype):
    n_mp, n_dp, rows, width = part.shape
    return (part * one).astype(dtype).reshape(n_mp * n_dp * rows, width)


def other_rows(part, one, dtype):
    n_mp, n_dp, rows, width = part.shape
    me = lax.axis_index("mp")
    blocks = [
        lax.dynamic_index_in_dim(part, (me + step) % n_mp, 0, keepdims=False)
        for step in range(1, n_mp)
    ]
    return (jnp.stack(blocks) * one).astype(dtype).reshape((n_mp - 1) * n_dp * rows, width)


def sum_over_dp(values):
    n_dp = lax.axis_size("dp")
    if n_dp & (n_dp - 1):
        return lax.psum(values, "dp")
    step = 1
    while step < n_dp:
        values = values + lax.ppermute(values, "dp", [(i, i ^ step) for i in range(n_dp)])
        step *= 2
    return values


def gather_biases(shards):
    n_mp = lax.axis_size("mp")
    me = lax.axis_index("mp")
    own = jnp.concatenate(shards)
    got = [own] + [
        lax.ppermute(own, "mp", [(i, (i + step) % n_mp) for i in range(n_mp)])
        for step in range(1, n_mp)
    ]
    got = jnp.stack(got)
    by_shard = jnp.take(got, (me - jnp.arange(n_mp)) % n_mp, axis=0)
    by_other = jnp.take(got, (-jnp.arange(1, n_mp)) % n_mp, axis=0)
    out, at = [], 0
    for i, shard in enumerate(shards):
        width = shard.shape[0]
        source = by_other if i == len(shards) - 1 else by_shard
        out.append(source[:, at : at + width].reshape(-1))
        at += width
    return out


def own_columns(values, width):
    return lax.dynamic_slice_in_dim(values, lax.axis_index("mp") * width, width, 1)


def on_device(
    inputs,
    timesteps,
    segments,
    valid_mask,
    step_table,
    ln1_gain,
    ln1_shift,
    w_query_shard,
    b_query_shard,
    w_key_shard,
    w_value_shard,
    b_value_shard,
    w_out_shard,
    b_out,
    ln2_gain,
    ln2_shift,
    w_up_shard,
    b_up_shard,
    w_down_shard,
    b_down,
    cotangent,
):
    row_count, seq_len, model_width = inputs.shape
    token_count = row_count * seq_len
    qkv_width = w_query_shard.shape[1]
    ff_width = w_up_shard.shape[1]
    one = 1.0 + 0.0 * ln1_gain[0]
    low_type = jnp.bfloat16
    q_part, k_part, v_part, o_part = gather_pieces(
        (
            w_query_shard.T,
            w_key_shard.T,
            w_value_shard.T,
            w_out_shard,
        ),
        one,
    )
    w_query_t = whole_rows(q_part, one, low_type)
    w_key_t = whole_rows(k_part, one, low_type)
    w_value_t = whole_rows(v_part, one, low_type)
    b_query, b_value, b_up_others = gather_biases(
        (b_query_shard, b_value_shard, b_up_shard)
    )
    up_part, down_part = gather_pieces(
        (
            w_up_shard.T,
            w_down_shard,
        ),
        one,
    )
    w_out = whole_rows(o_part, one, low_type)
    w_up_others = other_rows(up_part, one, low_type)
    w_down_others = other_rows(down_part, one, low_type)
    heads = w_query_t.shape[0] // HD
    scaling = 1.0 / math.sqrt(HD)
    head_shape = (row_count, seq_len, heads, HD)
    start = inputs.astype(jnp.float32) + step_table[timesteps].astype(jnp.float32)[:, None, :]
    start = start.reshape(token_count, model_width)
    normed, first_pull = jax.vjp(normalize, start, ln1_gain, ln1_shift)
    normed_low = normed.astype(low_type)
    queries = (over_cols(normed_low, w_query_t) + b_query).astype(low_type)
    key_rows = over_cols(normed_low, w_key_t).astype(low_type)
    value_rows = (over_cols(normed_low, w_value_t) + b_value).astype(low_type)
    queries_split = queries.reshape(head_shape)
    keys_split = key_rows.reshape(head_shape)
    values_split = value_rows.reshape(head_shape)
    places = jnp.arange(seq_len, dtype=jnp.int32)
    diagonal = places[:, None] == places[None, :]
    allowed = (segments[:, :, None] == segments[:, None, :]) & (
        (valid_mask[:, None, :] > 0) | diagonal[None]
    )
    scores = attention_scores(queries_split, keys_split, allowed)
    row_max = jnp.max(scores, axis=-1, keepdims=True)
    powers = jnp.exp(scores - row_max)
    total = jnp.sum(powers, axis=-1, keepdims=True)
    log_total = row_max + jnp.log(total)
    probabilities = powers / total
    probabilities_low = probabilities.astype(low_type)
    mixed = jnp.einsum(
        "rhqk,rkhe->rqhe",
        probabilities_low,
        values_split,
        preferred_element_type=jnp.float32,
    )
    mixed = mixed.reshape(token_count, heads * HD).astype(low_type)
    attended = product(mixed, w_out) + b_out
    middle = start + attended
    normed2, second_pull = jax.vjp(normalize, middle, ln2_gain, ln2_shift)
    normed2_low = normed2.astype(low_type)
    upper_own = product(normed2_low, w_up_shard) + b_up_shard
    activated_own, gelu_pull_own = jax.vjp(exact_gelu, upper_own)
    hidden_own = activated_own.astype(low_type)
    lowered_own = product(hidden_own, w_down_shard)
    grad_out = cotangent.reshape(token_count, model_width).astype(jnp.float32)
    grad_out = grad_out * valid_mask.reshape(token_count, 1).astype(jnp.float32)
    grad_out_low = grad_out.astype(low_type)
    grad_out, grad_out_low = lax.optimization_barrier((grad_out, grad_out_low))
    grad_w_down = over_rows(hidden_own, grad_out_low)
    grad_b_down = jnp.sum(grad_out, axis=0)
    (grad_upper_own,) = gelu_pull_own(over_cols(grad_out_low, w_down_shard))
    grad_upper_own = grad_upper_own.astype(low_type)
    grad_w_up = over_rows(normed2_low, grad_upper_own)
    grad_b_up = column_sum(grad_upper_own)
    ffn_grads = lax.psum(jnp.concatenate([grad_w_down, grad_w_up], axis=0), "dp")
    grad_w_down, grad_w_up = ffn_grads[:ff_width], ffn_grads[ff_width:]
    grad_normed2_own = over_cols(grad_upper_own, w_up_shard)
    upper = over_cols(normed2_low, w_up_others) + b_up_others
    activated, gelu_pull = jax.vjp(exact_gelu, upper)
    hidden = lax.optimization_barrier(activated.astype(low_type))
    lowered = lowered_own + product(hidden, w_down_others)
    output = (middle + lowered + b_down).astype(low_type)
    output = output.reshape(row_count, seq_len, model_width)
    (grad_upper,) = gelu_pull(over_cols(grad_out_low, w_down_others))
    grad_upper_low = lax.optimization_barrier(grad_upper.astype(low_type))
    grad_normed2 = grad_normed2_own + product(grad_upper_low, w_up_others)
    grad_mid_norm, grad_ln2_gain, grad_ln2_shift = second_pull(grad_normed2)
    grad_middle = grad_out + grad_mid_norm
    grad_mid_low = grad_middle.astype(low_type)
    grad_w_out = over_rows(own_columns(mixed, qkv_width), grad_mid_low)
    grad_b_out = column_sum(grad_mid_low)
    grad_mixed = over_cols(grad_mid_low, w_out).astype(low_type).reshape(head_shape)
    soft_again = probabilities
    grad_soft = jnp.einsum(
        "rqhe,rkhe->rhqk", grad_mixed, values_split, preferred_element_type=jnp.float32
    )
    delta = jnp.sum(soft_again * grad_soft, axis=-1, keepdims=True)
    grad_scores = (soft_again * (grad_soft - delta)).astype(low_type)
    grad_queries = jnp.einsum(
        "rhqk,rkhe->rqhe", grad_scores, keys_split, preferred_element_type=jnp.float32
    )
    grad_queries = (grad_queries * scaling).reshape(token_count, heads * HD).astype(low_type)
    grad_keys = jnp.einsum(
        "rhqk,rqhe->rkhe", grad_scores, queries_split, preferred_element_type=jnp.float32
    )
    grad_keys = (grad_keys * scaling).reshape(token_count, heads * HD).astype(low_type)
    grad_values = jnp.einsum(
        "rhqk,rqhe->rkhe",
        probabilities_low,
        grad_mixed,
        preferred_element_type=jnp.float32,
    )
    grad_values = grad_values.reshape(token_count, heads * HD).astype(low_type)
    own_grad_queries = own_columns(grad_queries, qkv_width)
    own_grad_values = own_columns(grad_values, qkv_width)
    grad_w_query = over_rows(normed_low, own_grad_queries)
    grad_b_query = column_sum(own_grad_queries)
    grad_w_key = over_rows(normed_low, own_columns(grad_keys, qkv_width))
    grad_w_value = over_rows(normed_low, own_grad_values)
    grad_b_value = column_sum(own_grad_values)
    tie = 0.0 * ffn_grads[0, 0]
    grad_w_query, grad_w_key, grad_w_value, grad_w_out = lax.psum(
        (grad_w_query + tie, grad_w_key, grad_w_value, grad_w_out), "dp"
    )
    grad_normed = (
        product(grad_queries, w_query_t)
        + product(grad_keys, w_key_t)
        + product(grad_values, w_value_t)
    )
    grad_start_norm, grad_ln1_gain, grad_ln1_shift = first_pull(grad_normed)
    grad_start = grad_middle + grad_start_norm
    input_grad = grad_start.astype(low_type).reshape(row_count, seq_len, model_width)
    row_sums = jnp.sum(grad_start.reshape(row_count, seq_len, model_width), axis=1)
    column_count = model_width // lax.axis_size("mp")
    table_columns = own_columns(row_sums, column_count)
    step_count = step_table.shape[0]
    one_hot = (timesteps[:, None] == jnp.arange(step_count, dtype=jnp.int32)[None, :]).astype(
        jnp.float32
    )
    table_grad = lax.dot_general(
        one_hot,
        table_columns,
        CONTRACT_ROWS,
        precision=lax.Precision.HIGHEST,
        preferred_element_type=jnp.float32,
    )
    small = (
        grad_ln1_gain,
        grad_ln1_shift,
        grad_b_query,
        grad_b_value,
        grad_b_out,
        grad_b_down,
        grad_b_up,
        grad_ln2_gain,
        grad_ln2_shift,
    )
    small_rows = jnp.concatenate(small).reshape(-1, column_count)
    packed = jnp.concatenate([table_grad, small_rows], axis=0)
    packed = sum_over_dp(packed)
    table_grad = packed[:step_count]
    flat_small = packed[step_count:].reshape(-1)
    unpacked, at = [], 0
    for item in small:
        unpacked.append(flat_small[at : at + item.shape[0]])
        at += item.shape[0]
    (
        grad_ln1_gain,
        grad_ln1_shift,
        grad_b_query,
        grad_b_value,
        grad_b_out,
        grad_b_down,
        grad_b_up,
        grad_ln2_gain,
        grad_ln2_shift,
    ) = unpacked
    return (
        output,
        input_grad,
        grad_ln1_gain,
        grad_ln1_shift,
        grad_w_query,
        grad_b_query,
        grad_w_key,
        grad_w_value,
        grad_b_value,
        grad_w_out,
        grad_b_out,
        grad_ln2_gain,
        grad_ln2_shift,
        grad_w_up,
        grad_b_up,
        grad_w_down,
        grad_b_down,
        table_grad,
    )


def solution(mesh):
    in_specs = (
        P("dp", None, None),
        P("dp"),
        P("dp", None),
        P("dp", None),
        P(),
        P(),
        P(),
        P(None, "mp"),
        P("mp"),
        P(None, "mp"),
        P(None, "mp"),
        P("mp"),
        P("mp", None),
        P(),
        P(),
        P(),
        P(None, "mp"),
        P("mp"),
        P("mp", None),
        P(),
        P("dp", None, None),
    )
    out_specs = (
        P("dp", None, None),
        P("dp", None, None),
        P(),
        P(),
        P(None, "mp"),
        P("mp"),
        P(None, "mp"),
        P(None, "mp"),
        P("mp"),
        P("mp", None),
        P(),
        P(),
        P(),
        P(None, "mp"),
        P("mp"),
        P("mp", None),
        P(),
        P(None, "mp"),
    )

    return jax.shard_map(
        on_device, mesh=mesh, in_specs=in_specs, out_specs=out_specs, check_vma=False
    )
```

```python
import math

import jax
import jax.numpy as jnp
from jax import lax
from jax.sharding import PartitionSpec as P


HD = 64


EPSILON = 1e-05
CONTRACT_ROWS = (((0,), (0,)), ((), ()))
CONTRACT_COLS = (((1,), (1,)), ((), ()))


def normalize(values, gain, shift):
    average = jnp.mean(values, axis=-1, keepdims=True)
    centered = values - average
    variance = jnp.mean(centered * centered, axis=-1, keepdims=True)
    return centered * lax.rsqrt(variance + EPSILON) * gain + shift


def exact_gelu(values):
    return 0.5 * values * (1.0 + lax.erf(values * math.sqrt(0.5)))


def product(left, right):
    return jnp.dot(left, right, preferred_element_type=jnp.float32)


def over_rows(left, right):
    return lax.dot_general(left, right, CONTRACT_ROWS, preferred_element_type=jnp.float32)


def over_cols(left, right):
    return lax.dot_general(left, right, CONTRACT_COLS, preferred_element_type=jnp.float32)


def column_sum(values):
    return jnp.sum(values.astype(jnp.float32), axis=0)


def attention_scores(queries_split, keys_split, allowed):
    scaling = 1.0 / math.sqrt(HD)
    scores = (
        jnp.einsum("rqhe,rkhe->rhqk", queries_split, keys_split, preferred_element_type=jnp.float32)
        * scaling
    )
    return jnp.where(allowed[:, None], scores, -1e30)


def gather_pieces(blocks, one):
    n_dp = lax.axis_size("dp")
    d = lax.axis_index("dp")
    pieces = []
    for block in blocks:
        piece_rows = block.shape[0] // n_dp
        pieces.append(lax.dynamic_slice_in_dim(block, d * piece_rows, piece_rows, 0))
    sent = jnp.concatenate([p.astype(jnp.float32) for p in pieces], axis=0) * one
    got = lax.all_gather(sent, ("mp", "dp"), axis=0)
    n_mp = lax.axis_size("mp")
    got = got.reshape(n_mp, n_dp, *sent.shape)
    out, at = [], 0
    for p in pieces:
        rows = p.shape[0]
        out.append(got[:, :, at : at + rows])
        at += rows
    return out


def whole_rows(part, one, dtype):
    n_mp, n_dp, rows, width = part.shape
    return (part * one).astype(dtype).reshape(n_mp * n_dp * rows, width)


def other_rows(part, one, dtype):
    n_mp, n_dp, rows, width = part.shape
    me = lax.axis_index("mp")
    blocks = [
        lax.dynamic_index_in_dim(part, (me + step) % n_mp, 0, keepdims=False)
        for step in range(1, n_mp)
    ]
    return (jnp.stack(blocks) * one).astype(dtype).reshape((n_mp - 1) * n_dp * rows, width)


def gather_over_dp(block):
    n_dp = lax.axis_size("dp")
    if n_dp & (n_dp - 1):
        return lax.all_gather(block, "dp", axis=0, tiled=True)
    me = lax.axis_index("dp")
    step = 1
    while step < n_dp:
        other = lax.ppermute(block, "dp", [(i, i ^ step) for i in range(n_dp)])
        upper = (me & step) != 0
        block = jnp.where(
            upper,
            jnp.concatenate([other, block], axis=0),
            jnp.concatenate([block, other], axis=0),
        )
        step *= 2
    return block


def gather_biases(shards):
    n_mp = lax.axis_size("mp")
    me = lax.axis_index("mp")
    own = jnp.concatenate(shards)
    got = [own] + [
        lax.ppermute(own, "mp", [(i, (i + step) % n_mp) for i in range(n_mp)])
        for step in range(1, n_mp)
    ]
    got = jnp.stack(got)
    by_shard = jnp.take(got, (me - jnp.arange(n_mp)) % n_mp, axis=0)
    by_other = jnp.take(got, (-jnp.arange(1, n_mp)) % n_mp, axis=0)
    out, at = [], 0
    for i, shard in enumerate(shards):
        width = shard.shape[0]
        source = by_other if i == len(shards) - 1 else by_shard
        out.append(source[:, at : at + width].reshape(-1))
        at += width
    return out


def own_columns(values, width):
    return lax.dynamic_slice_in_dim(values, lax.axis_index("mp") * width, width, 1)


def on_device(
    inputs,
    timesteps,
    segments,
    valid_mask,
    step_table,
    ln1_gain,
    ln1_shift,
    w_query_shard,
    b_query_shard,
    w_key_shard,
    w_value_shard,
    b_value_shard,
    w_out_shard,
    b_out,
    ln2_gain,
    ln2_shift,
    w_up_shard,
    b_up_shard,
    w_down_shard,
    b_down,
    cotangent,
):
    row_count, seq_len, model_width = inputs.shape
    token_count = row_count * seq_len
    qkv_width = w_query_shard.shape[1]
    ff_width = w_up_shard.shape[1]
    one = 1.0 + 0.0 * ln1_gain[0]
    low_type = jnp.bfloat16
    q_part, k_part, v_part, o_part = gather_pieces(
        (
            w_query_shard.T,
            w_key_shard.T,
            w_value_shard.T,
            w_out_shard,
        ),
        one,
    )
    w_query_t = whole_rows(q_part, one, low_type)
    w_key_t = whole_rows(k_part, one, low_type)
    w_value_t = whole_rows(v_part, one, low_type)
    b_query, b_value, b_up_others = gather_biases(
        (b_query_shard, b_value_shard, b_up_shard)
    )
    up_part, down_part = gather_pieces(
        (
            w_up_shard.T,
            w_down_shard,
        ),
        one,
    )
    w_out = whole_rows(o_part, one, low_type)
    w_up_others = other_rows(up_part, one, low_type)
    w_down_others = other_rows(down_part, one, low_type)
    heads = w_query_t.shape[0] // HD
    scaling = 1.0 / math.sqrt(HD)
    head_shape = (row_count, seq_len, heads, HD)
    start = inputs.astype(jnp.float32) + step_table[timesteps].astype(jnp.float32)[:, None, :]
    start = start.reshape(token_count, model_width)
    normed, first_pull = jax.vjp(normalize, start, ln1_gain, ln1_shift)
    normed_low = normed.astype(low_type)
    queries = (over_cols(normed_low, w_query_t) + b_query).astype(low_type)
    key_rows = over_cols(normed_low, w_key_t).astype(low_type)
    value_rows = (over_cols(normed_low, w_value_t) + b_value).astype(low_type)
    queries_split = queries.reshape(head_shape)
    keys_split = key_rows.reshape(head_shape)
    values_split = value_rows.reshape(head_shape)
    places = jnp.arange(seq_len, dtype=jnp.int32)
    diagonal = places[:, None] == places[None, :]
    allowed = (segments[:, :, None] == segments[:, None, :]) & (
        (valid_mask[:, None, :] > 0) | diagonal[None]
    )
    scores = attention_scores(queries_split, keys_split, allowed)
    row_max = jnp.max(scores, axis=-1, keepdims=True)
    powers = jnp.exp(scores - row_max)
    total = jnp.sum(powers, axis=-1, keepdims=True)
    log_total = row_max + jnp.log(total)
    probabilities = powers / total
    probabilities_low = probabilities.astype(low_type)
    mixed = jnp.einsum(
        "rhqk,rkhe->rqhe",
        probabilities_low,
        values_split,
        preferred_element_type=jnp.float32,
    )
    mixed = mixed.reshape(token_count, heads * HD).astype(low_type)
    attended = product(mixed, w_out) + b_out
    middle = start + attended
    normed2, second_pull = jax.vjp(normalize, middle, ln2_gain, ln2_shift)
    normed2_low = normed2.astype(low_type)
    upper_own = product(normed2_low, w_up_shard) + b_up_shard
    activated_own, gelu_pull_own = jax.vjp(exact_gelu, upper_own)
    hidden_own = activated_own.astype(low_type)
    lowered_own = product(hidden_own, w_down_shard)
    grad_out = cotangent.reshape(token_count, model_width).astype(jnp.float32)
    grad_out = grad_out * valid_mask.reshape(token_count, 1).astype(jnp.float32)
    grad_out_low = grad_out.astype(low_type)
    grad_out, grad_out_low = lax.optimization_barrier((grad_out, grad_out_low))
    grad_w_down = over_rows(hidden_own, grad_out_low)
    grad_b_down = jnp.sum(grad_out, axis=0)
    (grad_upper_own,) = gelu_pull_own(over_cols(grad_out_low, w_down_shard))
    grad_upper_own = grad_upper_own.astype(low_type)
    grad_w_up = over_rows(normed2_low, grad_upper_own)
    grad_b_up = column_sum(grad_upper_own)
    ffn_grads = lax.psum(jnp.concatenate([grad_w_down, grad_w_up], axis=0), "dp")
    grad_w_down, grad_w_up = ffn_grads[:ff_width], ffn_grads[ff_width:]
    grad_normed2_own = over_cols(grad_upper_own, w_up_shard)
    upper = over_cols(normed2_low, w_up_others) + b_up_others
    activated, gelu_pull = jax.vjp(exact_gelu, upper)
    hidden = lax.optimization_barrier(activated.astype(low_type))
    lowered = lowered_own + product(hidden, w_down_others)
    output = (middle + lowered + b_down).astype(low_type)
    output = output.reshape(row_count, seq_len, model_width)
    (grad_upper,) = gelu_pull(over_cols(grad_out_low, w_down_others))
    grad_upper_low = lax.optimization_barrier(grad_upper.astype(low_type))
    grad_normed2 = grad_normed2_own + product(grad_upper_low, w_up_others)
    grad_mid_norm, grad_ln2_gain, grad_ln2_shift = second_pull(grad_normed2)
    grad_middle = grad_out + grad_mid_norm
    grad_mid_low = grad_middle.astype(low_type)
    grad_w_out = over_rows(own_columns(mixed, qkv_width), grad_mid_low)
    grad_b_out = column_sum(grad_mid_low)
    grad_mixed = over_cols(grad_mid_low, w_out).astype(low_type).reshape(head_shape)
    soft_again = probabilities
    grad_soft = jnp.einsum(
        "rqhe,rkhe->rhqk", grad_mixed, values_split, preferred_element_type=jnp.float32
    )
    delta = jnp.sum(soft_again * grad_soft, axis=-1, keepdims=True)
    grad_scores = (soft_again * (grad_soft - delta)).astype(low_type)
    grad_queries = jnp.einsum(
        "rhqk,rkhe->rqhe", grad_scores, keys_split, preferred_element_type=jnp.float32
    )
    grad_queries = (grad_queries * scaling).reshape(token_count, heads * HD).astype(low_type)
    grad_keys = jnp.einsum(
        "rhqk,rqhe->rkhe", grad_scores, queries_split, preferred_element_type=jnp.float32
    )
    grad_keys = (grad_keys * scaling).reshape(token_count, heads * HD).astype(low_type)
    grad_values = jnp.einsum(
        "rhqk,rqhe->rkhe",
        probabilities_low,
        grad_mixed,
        preferred_element_type=jnp.float32,
    )
    grad_values = grad_values.reshape(token_count, heads * HD).astype(low_type)
    own_grad_queries = own_columns(grad_queries, qkv_width)
    own_grad_values = own_columns(grad_values, qkv_width)
    grad_w_query = over_rows(normed_low, own_grad_queries)
    grad_b_query = column_sum(own_grad_queries)
    grad_w_key = over_rows(normed_low, own_columns(grad_keys, qkv_width))
    grad_w_value = over_rows(normed_low, own_grad_values)
    grad_b_value = column_sum(own_grad_values)
    tie = 0.0 * ffn_grads[0, 0]
    grad_w_query, grad_w_key, grad_w_value, grad_w_out = lax.psum(
        (grad_w_query + tie, grad_w_key, grad_w_value, grad_w_out), "dp"
    )
    grad_normed = (
        product(grad_queries, w_query_t)
        + product(grad_keys, w_key_t)
        + product(grad_values, w_value_t)
    )
    grad_start_norm, grad_ln1_gain, grad_ln1_shift = first_pull(grad_normed)
    grad_start = grad_middle + grad_start_norm
    input_grad = grad_start.astype(low_type).reshape(row_count, seq_len, model_width)
    row_sums = jnp.sum(grad_start.reshape(row_count, seq_len, model_width), axis=1)
    column_count = model_width // lax.axis_size("mp")
    table_columns = own_columns(row_sums, column_count)
    small = (
        grad_ln1_gain,
        grad_ln1_shift,
        grad_b_query,
        grad_b_value,
        grad_b_out,
        grad_b_down,
        grad_b_up,
        grad_ln2_gain,
        grad_ln2_shift,
    )
    small_rows = jnp.concatenate(small).reshape(-1, column_count)
    step_row = jnp.pad(
        timesteps.astype(jnp.float32), (0, column_count - row_count)
    ).reshape(1, column_count)
    block = jnp.concatenate([table_columns, small_rows, step_row], axis=0)
    blocks = gather_over_dp(block)
    n_blocks = blocks.shape[0] // block.shape[0]
    blocks = blocks.reshape(n_blocks, block.shape[0], column_count)
    all_rows = blocks[:, :row_count].reshape(n_blocks * row_count, column_count)
    all_steps = blocks[:, -1, :row_count].reshape(-1).astype(jnp.int32)
    step_count = step_table.shape[0]
    one_hot = (all_steps[:, None] == jnp.arange(step_count, dtype=jnp.int32)[None, :]).astype(
        jnp.float32
    )
    table_grad = lax.dot_general(
        one_hot,
        all_rows,
        CONTRACT_ROWS,
        precision=lax.Precision.HIGHEST,
        preferred_element_type=jnp.float32,
    )
    small_sum = blocks[0, row_count:-1]
    for i in range(1, n_blocks):
        small_sum = small_sum + blocks[i, row_count:-1]
    flat_small = small_sum.reshape(-1)
    unpacked, at = [], 0
    for item in small:
        unpacked.append(flat_small[at : at + item.shape[0]])
        at += item.shape[0]
    (
        grad_ln1_gain,
        grad_ln1_shift,
        grad_b_query,
        grad_b_value,
        grad_b_out,
        grad_b_down,
        grad_b_up,
        grad_ln2_gain,
        grad_ln2_shift,
    ) = unpacked
    return (
        output,
        input_grad,
        grad_ln1_gain,
        grad_ln1_shift,
        grad_w_query,
        grad_b_query,
        grad_w_key,
        grad_w_value,
        grad_b_value,
        grad_w_out,
        grad_b_out,
        grad_ln2_gain,
        grad_ln2_shift,
        grad_w_up,
        grad_b_up,
        grad_w_down,
        grad_b_down,
        table_grad,
    )


def solution(mesh):
    in_specs = (
        P("dp", None, None),
        P("dp"),
        P("dp", None),
        P("dp", None),
        P(),
        P(),
        P(),
        P(None, "mp"),
        P("mp"),
        P(None, "mp"),
        P(None, "mp"),
        P("mp"),
        P("mp", None),
        P(),
        P(),
        P(),
        P(None, "mp"),
        P("mp"),
        P("mp", None),
        P(),
        P("dp", None, None),
    )
    out_specs = (
        P("dp", None, None),
        P("dp", None, None),
        P(),
        P(),
        P(None, "mp"),
        P("mp"),
        P(None, "mp"),
        P(None, "mp"),
        P("mp"),
        P("mp", None),
        P(),
        P(),
        P(),
        P(None, "mp"),
        P("mp"),
        P("mp", None),
        P(),
        P(None, "mp"),
    )

    return jax.shard_map(
        on_device, mesh=mesh, in_specs=in_specs, out_specs=out_specs, check_vma=False
    )
```
